256 devices in a mesh: ctx: 32 (over x, y, core), head: 8 (over z).
Axes of the slice: x: 4, y: 4, z: 8, core: 2. Of those that a mesh axis runs over, the one named last changes fastest.
Arguments:
- query_rows: bfloat16 [32, 32768, 128], P('head', 'ctx'), parts along dimension 0, may hold values from -1.75 to 1.75
- key_rows: bfloat16 [32, 32768, 128], P('head', 'ctx'), parts along dimension 0, may hold values from -1.75 to 1.75
- value_rows: bfloat16 [32, 32768, 128], P('head', 'ctx'), parts along dimension 0, may hold values from -6 to 6
- out_grad: bfloat16 [32, 32768, 128], P('head', 'ctx'), parts along dimension 0, may hold values from -6 to 6
- level_gate: float32 [16, 32, 32768], P(None, 'head', 'ctx'), parts along dimension 1, may hold values from -12 to 1
- block_levels: int32 [32, 32], replicated, may hold values from -1 to 15, as said below
Outputs:
- attn_out: bfloat16 [32, 32768, 128], P('head', 'ctx'), parts along dimension 0
- grad_query: bfloat16 [32, 32768, 128], P('head', 'ctx'), parts along dimension 0
- grad_key: bfloat16 [32, 32768, 128], P('head', 'ctx'), parts along dimension 0
- grad_value: bfloat16 [32, 32768, 128], P('head', 'ctx'), parts along dimension 0
- grad_gate: float32 [16, 32, 32768], P(None, 'head', 'ctx'), parts along dimension 1
The draws below stay inside these ranges and needn't reach their ends.
There are 8 independent parts, one for each index of `head`. The reference program is written for one: setup_inputs(seed, part) draws one part's arguments, and reference() takes and returns one part's arrays. A program takes and returns all parts, laid end to end along the dimension named above; an argument that names none is the same for every part. Nothing has to cross between parts.
Inputs may be any that keep to these rules, and one draw needn't show every extreme that they name: The sequence packs documents made of whole blocks; block 0 starts one. block_levels[c, c'] = 10 plus the bit length of (c xor c') where c' < c and both blocks lie in one document, else -1.
All inputs are finite; a program needn't handle non-finite values.
Results may differ from the reference program's by a relative error of at most 0.011.
Values may be sent and summed in bfloat16 or wider, within the bound.
No kernel may reach another device: no remote copies, remote signals or barrier semaphores. Data moves between devices by JAX's collectives and lax.ppermute only.
A program may use at most 128 MiB of HBM per device.

```python
import math
import jax
import jax.numpy as jnp
from jax import lax

HD = 128
HEADS = 4
BLOCK = 1024
LOG_BLOCK = 10
BLOCKS = 32
LOG_CTX = 5
NLEV = 16
TOKENS = 32768


def draw_level_gate(key, part):
    levels = jnp.arange(NLEV, dtype=jnp.float32)
    log_size = jnp.where(levels > 0.5, (levels - 1.0) * math.log(2.0), 0.0)
    base = -0.5 * (log_size + math.log(NLEV))
    shape = (NLEV, HEADS, TOKENS)
    noise = jax.random.uniform(key, shape, jnp.float32, -1.2, 1.2)
    return (base[:, None, None] + noise).astype(jnp.float32)


def draw_block_levels(key, part):
    positions = jnp.arange(BLOCKS, dtype=jnp.int32)
    upper_key, lower_key, forced_key = jax.random.split(jax.random.fold_in(key, 7), 3)
    upper_starts = jax.random.randint(upper_key, (BLOCKS,), 0, 2) == 0
    lower_starts = jax.random.randint(lower_key, (BLOCKS,), 0, 4) == 0
    forced = BLOCKS // 2 + 1 + jax.random.randint(forced_key, (), 0, BLOCKS // 2 - 1)
    starts = jnp.where(positions > BLOCKS // 2, upper_starts, False)
    starts = jnp.where((positions >= 1) & (positions < BLOCKS // 4), lower_starts, starts)
    starts = jnp.where(positions == forced, True, starts)
    starts = jnp.where(positions == 0, True, starts)
    document = jnp.cumsum(starts.astype(jnp.int32))
    crossed = jnp.bitwise_xor(positions[:, None], positions[None, :])
    length = jnp.zeros(crossed.shape, jnp.int32)
    for shift_by in range(LOG_CTX):
        length = length + (jnp.right_shift(crossed, shift_by) > 0).astype(jnp.int32)
    visible = (document[:, None] == document[None, :]) & (positions[None, :] < positions[:, None])
    return jnp.where(visible, LOG_BLOCK + length, -1).astype(jnp.int32)


def level_of(stream_key, shape, cuts, low, top_value):
    def one(axis_at, parts):
        draws = jax.random.uniform(jax.random.fold_in(jax.random.fold_in(stream_key, 6), axis_at), (parts,), jnp.float32, low / len(cuts), top_value / len(cuts))
        return jnp.repeat(jnp.exp(draws), shape[axis_at] // parts).reshape((-1,) + (1,) * (len(shape) - axis_at - 1))

    gain = one(*cuts[0])
    for cut in cuts[1:]:
        gain = gain * one(*cut)
    return gain


def centred(key, extent, width, reach, shards=(), kind=jnp.bfloat16):
    drawn = width * jax.random.normal(key, extent, jnp.float32)
    if shards:
        drawn = drawn * level_of(key, extent, shards, -0.22, 0.18)
    return jnp.clip(drawn, -reach, reach).astype(kind)


def setup_inputs(seed: int = 0, part: int = 0) -> dict:
    arg_keys = jax.random.split(jax.random.key(seed), 7)
    part_keys = jax.random.split(jax.random.fold_in(arg_keys[6], part), 7)
    return {
        "query_rows": centred(part_keys[0], (HEADS, TOKENS, HD), 0.3, 1.75, ((1, 32),)),
        "key_rows": centred(part_keys[1], (HEADS, TOKENS, HD), 0.3, 1.75, ((1, 32),)),
        "value_rows": centred(part_keys[2], (HEADS, TOKENS, HD), 1.0, 6.0, ((1, 32),)),
        "out_grad": centred(part_keys[3], (HEADS, TOKENS, HD), 1.0, 6.0, ((1, 32),)),
        "level_gate": draw_level_gate(jax.random.fold_in(jax.random.fold_in(arg_keys[6], part), 71), part),
        "block_levels": draw_block_levels(jax.random.fold_in(arg_keys[6], 71), part),
    }


def bit_length(numbers, count):
    total = jnp.zeros(numbers.shape, jnp.int32)
    for shift_by in range(count):
        total = total + (jnp.right_shift(numbers, shift_by) > 0).astype(jnp.int32)
    return total


def rounded(array):
    return lax.optimization_barrier(array.astype(jnp.bfloat16)).astype(jnp.float32)


def to_blocks(array):
    return array.reshape(HEADS, BLOCKS, BLOCK, HD).transpose(1, 0, 2, 3)


def from_blocks(array):
    return array.transpose(1, 0, 2, 3).reshape(HEADS, TOKENS, HD)


def reference(query_rows, key_rows, value_rows, out_grad, level_gate, block_levels):
    gate_all = jnp.exp(level_gate)
    gate_blocks = gate_all.reshape(NLEV, HEADS, BLOCKS, BLOCK).transpose(2, 0, 1, 3)
    query_b = to_blocks(query_rows)
    key_b = to_blocks(key_rows)
    value_b = to_blocks(value_rows)
    grad_b = to_blocks(out_grad)
    positions = jnp.arange(BLOCK, dtype=jnp.int32)
    inner = bit_length(jnp.bitwise_xor(positions[:, None], positions[None, :]), LOG_BLOCK)
    inner = jnp.where(positions[None, :] <= positions[:, None], inner, -1)
    cross_ids = LOG_BLOCK + 1 + jnp.arange(LOG_CTX, dtype=jnp.int32)

    def make_state(pair):
        return jnp.einsum("hcd,hce->hde", pair[0].astype(jnp.float32), pair[1].astype(jnp.float32)).astype(jnp.bfloat16)

    block_states = lax.map(make_state, (key_b, value_b))
    states_wide = lax.optimization_barrier(block_states).astype(jnp.float32)

    def per_block(inputs):
        query_h, key_h, value_h, grad_h, gate_h, row_levels = inputs
        match = row_levels[None, :] == cross_ids[:, None]
        level_sum = jnp.sum(jnp.where(match[:, :, None, None, None], states_wide[None], jnp.float32(0.0)), axis=1)
        level_state = rounded(level_sum)
        query_f = query_h.astype(jnp.float32)
        key_f = key_h.astype(jnp.float32)
        value_f = value_h.astype(jnp.float32)
        grad_f = grad_h.astype(jnp.float32)
        gate_rows = jnp.transpose(gate_h, (1, 2, 0))
        picks = jnp.broadcast_to(jnp.maximum(inner, 0)[None], (HEADS, BLOCK, BLOCK)).astype(jnp.int32)
        weight = jnp.take_along_axis(gate_rows, picks, axis=2)
        weight = jnp.where(inner[None] >= 0, weight, jnp.float32(0.0))
        scores = jnp.einsum("htd,hsd->hts", query_f, key_f)
        probs = rounded(weight * scores)
        back = jnp.einsum("hte,hse->hts", grad_f, value_f)
        dprobs = rounded(weight * back)
        cross_gate = gate_h[LOG_BLOCK + 1:]
        level_out = jnp.einsum("htd,bhde->bhte", query_f, level_state)
        level_back = jnp.einsum("hte,bhde->bhtd", grad_f, level_state)
        attn = jnp.einsum("hts,hse->hte", probs, value_f) + jnp.sum(cross_gate[..., None] * level_out, axis=0)
        grad_q = jnp.einsum("hts,hsd->htd", dprobs, key_f) + jnp.sum(cross_gate[..., None] * level_back, axis=0)
        grad_k_in = jnp.einsum("hts,htd->hsd", dprobs, query_f)
        grad_v_in = jnp.einsum("hts,hte->hse", probs, grad_f)
        product = scores * back
        inner_terms = [jnp.sum(jnp.where(inner[None] == level_num, product, jnp.float32(0.0)), axis=2) for level_num in range(LOG_BLOCK + 1)]
        cross_terms = jnp.sum(level_out * grad_f[None], axis=3)
        grad_gate = gate_h * jnp.concatenate([jnp.stack(inner_terms), cross_terms], axis=0)
        scaled = rounded(cross_gate[..., None] * grad_f[None])
        grad_state = jnp.einsum("htd,bhte->bhde", query_f, scaled).astype(jnp.bfloat16)
        return attn.astype(jnp.bfloat16), grad_q.astype(jnp.bfloat16), grad_k_in, grad_v_in, grad_gate, grad_state

    results = lax.map(per_block, (query_b, key_b, value_b, grad_b, gate_blocks, block_levels))
    attn_b, grad_q_b, grad_k_in, grad_v_in, grad_gate_b, grad_states = results
    grads_wide = lax.optimization_barrier(grad_states).astype(jnp.float32)

    def key_sum(column):
        match = column[:, None] == cross_ids[None, :]
        total = jnp.sum(jnp.where(match[:, :, None, None, None], grads_wide, jnp.float32(0.0)), axis=(0, 1))
        return total.astype(jnp.bfloat16)

    key_states = lax.optimization_barrier(lax.map(key_sum, block_levels.T)).astype(jnp.float32)
    grad_key = (grad_k_in + jnp.einsum("nhde,nhse->nhsd", key_states, value_b.astype(jnp.float32))).astype(jnp.bfloat16)
    grad_value = (grad_v_in + jnp.einsum("nhde,nhsd->nhse", key_states, key_b.astype(jnp.float32))).astype(jnp.bfloat16)
    grad_gate = grad_gate_b.transpose(1, 2, 0, 3).reshape(NLEV, HEADS, TOKENS)
    return from_blocks(attn_b), from_blocks(grad_q_b), from_blocks(grad_key), from_blocks(grad_value), grad_gate
```

```python
import jax
import jax.numpy as jnp
from jax import lax
from jax.experimental import pallas as pl
from jax.experimental.pallas import tpu as pltpu
from jax.sharding import PartitionSpec as P


TILE = 256


def bit_length_small(numbers, count):
    total = jnp.zeros(numbers.shape, jnp.int32)
    for shift_by in range(count):
        total = total + (numbers >= (1 << shift_by)).astype(jnp.int32)
    return total


def dot_nt(a, b):
    return lax.dot_general(a, b, (((1,), (1,)), ((), ())), preferred_element_type=jnp.float32)


def dot_tn(a, b):
    return lax.dot_general(a, b, (((0,), (0,)), ((), ())), preferred_element_type=jnp.float32)


def dot_nn(a, b):
    return lax.dot_general(a, b, (((1,), (0,)), ((), ())), preferred_element_type=jnp.float32)


def local_kernel(q_ref, k_ref, v_ref, do_ref, g_ref, o_ref, dq_ref, dk_ref, dv_ref, gg_ref):
    block_len = q_ref.shape[0]
    tiles = block_len // TILE
    log_tile = TILE.bit_length() - 1
    nlev = g_ref.shape[1]
    rows = lax.broadcasted_iota(jnp.int32, (TILE, TILE), 0)
    cols = lax.broadcasted_iota(jnp.int32, (TILE, TILE), 1)
    diag_level = jnp.where(
        cols <= rows, bit_length_small(jnp.bitwise_xor(rows, cols), log_tile), -1
    )
    lane = lax.broadcasted_iota(jnp.int32, (TILE, nlev), 1)
    dk_ref[...] = jnp.zeros(dk_ref.shape, jnp.float32)
    dv_ref[...] = jnp.zeros(dv_ref.shape, jnp.float32)
    for i in range(tiles):
        rs = pl.ds(i * TILE, TILE)
        qi = q_ref[rs, :]
        doi = do_ref[rs, :]
        gi = g_ref[rs, :]
        o_acc = jnp.zeros((TILE, q_ref.shape[1]), jnp.float32)
        dq_acc = jnp.zeros((TILE, q_ref.shape[1]), jnp.float32)
        sums = {}
        for j in range(i + 1):
            cs = pl.ds(j * TILE, TILE)
            kj = k_ref[cs, :]
            vj = v_ref[cs, :]
            scores = dot_nt(qi, kj)
            back = dot_nt(doi, vj)
            prod = scores * back
            if j < i:
                level = log_tile + (i ^ j).bit_length()
                weight = gi[:, level : level + 1]
                probs = (scores * weight).astype(jnp.bfloat16)
                dprobs = (back * weight).astype(jnp.bfloat16)
                part = jnp.sum(prod, axis=1, keepdims=True)
                sums[level] = sums[level] + part if level in sums else part
            else:
                weight = jnp.zeros((TILE, TILE), jnp.float32)
                for level in range(log_tile + 1):
                    hit = diag_level == level
                    weight = jnp.where(hit, gi[:, level : level + 1], weight)
                    part = jnp.sum(jnp.where(hit, prod, 0.0), axis=1, keepdims=True)
                    sums[level] = sums[level] + part if level in sums else part
                probs = (scores * weight).astype(jnp.bfloat16)
                dprobs = (back * weight).astype(jnp.bfloat16)
            o_acc = o_acc + dot_nn(probs, vj)
            dq_acc = dq_acc + dot_nn(dprobs, kj)
            dk_ref[cs, :] += dot_tn(dprobs, qi)
            dv_ref[cs, :] += dot_tn(probs, doi)
        o_ref[rs, :] = o_acc
        dq_ref[rs, :] = dq_acc
        gg = jnp.zeros((TILE, nlev), jnp.float32)
        for level, part in sums.items():
            gg = jnp.where(lane == level, part, gg)
        gg_ref[rs, :] = gg * gi


def local_part(query_rows, key_rows, value_rows, out_grad, gate_t):
    heads, block_len, width = query_rows.shape
    nlev = gate_t.shape[2]
    row_spec = pl.BlockSpec((None, block_len, width), lambda h: (h, 0, 0))
    gate_spec = pl.BlockSpec((None, block_len, nlev), lambda h: (h, 0, 0))
    f32 = jnp.float32
    pairs = (block_len // TILE) * (block_len // TILE + 1) // 2
    flops = heads * pairs * 6 * 2 * TILE * TILE * width
    return pl.pallas_call(
        local_kernel,
        grid=(heads,),
        in_specs=[row_spec] * 4 + [gate_spec],
        out_specs=[row_spec] * 4 + [gate_spec],
        out_shape=[jax.ShapeDtypeStruct((heads, block_len, width), f32)] * 4
        + [jax.ShapeDtypeStruct((heads, block_len, nlev), f32)],
        compiler_params=pltpu.CompilerParams(dimension_semantics=("arbitrary",)),
        cost_estimate=pl.CostEstimate(
            flops=flops,
            transcendentals=0,
            bytes_accessed=heads * block_len * (4 * width * 2 + 4 * width * 4 + 2 * nlev * 4),
        ),
    )(query_rows, key_rows, value_rows, out_grad, gate_t)


def same_doc(block_levels, earlier, later):
    return block_levels[later, earlier] >= 0


def level_network(state, block_levels, me, nbits, ctx_len):
    x = state
    levels = []
    for k in range(nbits):
        bit = ((me >> k) & 1) == 1
        lo = (me >> (k + 1)) << (k + 1)
        end_low = lo + (1 << k) - 1
        end_high = lo + (2 << k) - 1
        joined = same_doc(block_levels, end_low, end_high)
        mine = same_doc(block_levels, end_low, me)
        if k < nbits - 1:
            perm = [(j, j ^ (1 << k)) for j in range(ctx_len)]
        else:
            perm = [(j, j ^ (1 << k)) for j in range(ctx_len) if not (j >> k) & 1]
        got = lax.ppermute(x, "ctx", perm)
        levels.append(jnp.where(bit & mine, got, 0.0).astype(jnp.bfloat16))
        if k < nbits - 1:
            x = jnp.where(
                bit, x + jnp.where(joined, got, 0.0), got + jnp.where(joined, x, 0.0)
            )
    return jnp.stack(levels)


def key_network(grad_state, block_levels, me, nbits, ctx_len):
    acc = None
    for k in reversed(range(nbits)):
        bit = ((me >> k) & 1) == 1
        lo = (me >> (k + 1)) << (k + 1)
        end_low = lo + (1 << k) - 1
        end_high = lo + (2 << k) - 1
        joined = same_doc(block_levels, end_low, end_high)
        mine = same_doc(block_levels, end_low, me)
        term = jnp.where(bit & mine, grad_state[k], 0.0)
        if acc is None:
            send = term
            own = None
            perm = [(j, j ^ (1 << k)) for j in range(ctx_len) if (j >> k) & 1]
        else:
            kept = jnp.where(joined, acc, 0.0)
            send = jnp.where(bit, term + kept, acc)
            own = jnp.where(bit, acc, kept)
            perm = [(j, j ^ (1 << k)) for j in range(ctx_len)]
        got = lax.ppermute(send, "ctx", perm)
        acc = got if own is None else own + got
    return acc


def per_device(query_rows, key_rows, value_rows, out_grad, level_gate, block_levels, ctx_len):
    level_total = level_gate.shape[0]
    block_len = query_rows.shape[1]
    log_block = block_len.bit_length() - 1
    nbits = level_total - log_block - 1
    me = lax.axis_index("ctx")
    weights = jnp.exp(level_gate)
    cross_weight = weights[log_block + 1 :]

    own_state = jnp.einsum(
        "hcd,hce->hde", key_rows, value_rows, preferred_element_type=jnp.float32
    ).astype(jnp.bfloat16)
    scaled = (cross_weight[..., None] * out_grad[None].astype(jnp.float32)).astype(jnp.bfloat16)
    grad_state = jnp.einsum(
        "hcd,bhce->bhde", query_rows, scaled, preferred_element_type=jnp.float32
    ).astype(jnp.bfloat16)

    level_state = level_network(
        own_state.astype(jnp.float32), block_levels, me, nbits, ctx_len
    )
    key_state = key_network(
        grad_state.astype(jnp.float32), block_levels, me, nbits, ctx_len
    ).astype(jnp.bfloat16)

    gate_t = weights.transpose(1, 2, 0)
    out_inner, dq_inner, dk_inner, dv_inner, grad_inner = local_part(
        query_rows, key_rows, value_rows, out_grad, gate_t
    )

    level_out = jnp.einsum(
        "hcd,bhde->bhce", query_rows, level_state, preferred_element_type=jnp.float32
    )
    level_back = jnp.einsum(
        "hce,bhde->bhcd", out_grad, level_state, preferred_element_type=jnp.float32
    )
    attn = out_inner + jnp.sum(cross_weight[..., None] * level_out, axis=0)
    grad_q = dq_inner + jnp.sum(cross_weight[..., None] * level_back, axis=0)
    grad_cross = cross_weight * jnp.sum(level_out * out_grad[None].astype(jnp.float32), axis=3)
    grad_gate = jnp.concatenate(
        [grad_inner.transpose(2, 0, 1)[: log_block + 1], grad_cross], axis=0
    )
    grad_k = (
        dk_inner
        + jnp.einsum("hde,hce->hcd", key_state, value_rows, preferred_element_type=jnp.float32)
    ).astype(jnp.bfloat16)
    grad_v = (
        dv_inner
        + jnp.einsum("hde,hcd->hce", key_state, key_rows, preferred_element_type=jnp.float32)
    ).astype(jnp.bfloat16)
    return (attn.astype(jnp.bfloat16), grad_q.astype(jnp.bfloat16), grad_k, grad_v, grad_gate)


def solution(mesh):
    ctx_len = mesh.shape["ctx"]
    in_specs = (
        P("head", "ctx", None),
        P("head", "ctx", None),
        P("head", "ctx", None),
        P("head", "ctx", None),
        P(None, "head", "ctx"),
        P(),
    )
    out_specs = (
        P("head", "ctx", None),
        P("head", "ctx", None),
        P("head", "ctx", None),
        P("head", "ctx", None),
        P(None, "head", "ctx"),
    )

    def body(*args):
        return per_device(*args, ctx_len=ctx_len)

    return jax.shard_map(
        body, mesh=mesh, in_specs=in_specs, out_specs=out_specs, check_vma=False
    )
```

```python
import jax
import jax.numpy as jnp
from jax import lax
from jax.experimental import pallas as pl
from jax.experimental.pallas import tpu as pltpu
from jax.sharding import PartitionSpec as P


TILE = 256
SUB = 128


def bit_length_small(numbers, count):
    total = jnp.zeros(numbers.shape, jnp.int32)
    for shift_by in range(count):
        total = total + (numbers >= (1 << shift_by)).astype(jnp.int32)
    return total


def dot_nt(a, b):
    return lax.dot_general(a, b, (((1,), (1,)), ((), ())), preferred_element_type=jnp.float32)


def dot_tn(a, b):
    return lax.dot_general(a, b, (((0,), (0,)), ((), ())), preferred_element_type=jnp.float32)


def dot_nn(a, b):
    return lax.dot_general(a, b, (((1,), (0,)), ((), ())), preferred_element_type=jnp.float32)


def local_kernel(q_ref, k_ref, v_ref, do_ref, g_ref, *refs):
    o_ref, dq_ref, dk_ref, dv_ref, gg_ref = refs[-5:]
    block_len = q_ref.shape[0]
    tiles = block_len // TILE
    log_tile = TILE.bit_length() - 1
    log_sub = SUB.bit_length() - 1
    keys = lax.broadcasted_iota(jnp.int32, (SUB, SUB), 0)
    queries = lax.broadcasted_iota(jnp.int32, (SUB, SUB), 1)
    diag_level = jnp.where(
        keys <= queries, bit_length_small(jnp.bitwise_xor(keys, queries), log_sub), -1
    )
    for ref in (o_ref, dq_ref, dk_ref, dv_ref, gg_ref):
        ref[...] = jnp.zeros(ref.shape, jnp.float32)

    def pair(t0, s0, size, level):
        ts = pl.ds(t0, size)
        ss = pl.ds(s0, size)
        qi = q_ref[ts, :]
        doi = do_ref[ts, :]
        kj = k_ref[ss, :]
        vj = v_ref[ss, :]
        gi = g_ref[:, ts]
        scores = dot_nt(kj, qi)
        back = dot_nt(vj, doi)
        prod = scores * back
        if level is not None:
            weight = gi[level : level + 1, :]
            gg_ref[level : level + 1, ts] += jnp.sum(prod, axis=0, keepdims=True)
        else:
            weight = jnp.zeros((size, size), jnp.float32)
            for lev in range(log_sub + 1):
                hit = diag_level == lev
                weight = jnp.where(hit, gi[lev : lev + 1, :], weight)
                gg_ref[lev : lev + 1, ts] += jnp.sum(
                    jnp.where(hit, prod, 0.0), axis=0, keepdims=True
                )
        probs = (scores * weight).astype(jnp.bfloat16)
        dprobs = (back * weight).astype(jnp.bfloat16)
        o_ref[ts, :] += dot_tn(probs, vj)
        dq_ref[ts, :] += dot_tn(dprobs, kj)
        dk_ref[ss, :] += dot_nn(dprobs, qi)
        dv_ref[ss, :] += dot_nn(probs, doi)

    for i in range(tiles):
        for j in range(i):
            pair(i * TILE, j * TILE, TILE, log_tile + (i ^ j).bit_length())
        for a in range(TILE // SUB):
            for b in range(a):
                pair(i * TILE + a * SUB, i * TILE + b * SUB, SUB, log_sub + (a ^ b).bit_length())
            pair(i * TILE + a * SUB, i * TILE + a * SUB, SUB, None)
    gg_ref[...] = gg_ref[...] * g_ref[...]


def local_part(query_rows, key_rows, value_rows, out_grad, gate_t):
    heads, block_len, width = query_rows.shape
    nlev = gate_t.shape[1]
    f32 = jnp.float32
    pairs = (block_len // TILE) * (block_len // TILE + 1) // 2
    flops = pairs * 6 * 2 * TILE * TILE * width
    shapes = [jax.ShapeDtypeStruct((heads, block_len, width), f32)] * 4 + [
        jax.ShapeDtypeStruct((heads, nlev, block_len), f32)
    ]
    outs = None
    for h in range(heads):
        row_spec = pl.BlockSpec((None, block_len, width), lambda i, h=h: (h, 0, 0))
        gate_spec = pl.BlockSpec((None, nlev, block_len), lambda i, h=h: (h, 0, 0))
        args = (query_rows, key_rows, value_rows, out_grad, gate_t)
        in_specs = [row_spec] * 4 + [gate_spec]
        aliases = {}
        if outs is not None:
            args = args + tuple(outs)
            in_specs = in_specs + [pl.BlockSpec(memory_space=pl.ANY)] * 5
            aliases = {5 + n: n for n in range(5)}
        outs = pl.pallas_call(
            local_kernel,
            grid=(1,),
            in_specs=in_specs,
            out_specs=[row_spec] * 4 + [gate_spec],
            out_shape=shapes,
            input_output_aliases=aliases,
            compiler_params=pltpu.CompilerParams(dimension_semantics=("arbitrary",)),
            cost_estimate=pl.CostEstimate(
                flops=flops,
                transcendentals=0,
                bytes_accessed=block_len * (4 * width * 2 + 4 * width * 4 + 2 * nlev * 4),
            ),
        )(*args)
    return outs


def final_kernel(q_ref, k_ref, v_ref, do_ref, o_ref, dq_ref, dk_ref, dv_ref, ggl_ref, g_ref,
                 ls_ref, ks_ref, attn_ref, gq_ref, gk_ref, gv_ref, gg_ref):
    block_len = q_ref.shape[0]
    nlev = g_ref.shape[0]
    nbits = ls_ref.shape[0]
    first = nlev - nbits
    gate_cols = jnp.transpose(g_ref[...])
    key_state = ks_ref[...]
    lane = lax.broadcasted_iota(jnp.int32, (TILE, nlev), 1)
    cross_parts = []
    for i in range(block_len // TILE):
        ts = pl.ds(i * TILE, TILE)
        qi = q_ref[ts, :]
        doi = do_ref[ts, :]
        do_f = doi.astype(jnp.float32)
        attn = o_ref[ts, :]
        grad_q = dq_ref[ts, :]
        cross = jnp.zeros((TILE, nlev), jnp.float32)
        for b in range(nbits):
            state = ls_ref[b]
            weight = gate_cols[i * TILE : (i + 1) * TILE, first + b : first + b + 1]
            level_out = dot_nn(qi, state)
            level_back = dot_nt(doi, state)
            attn = attn + weight * level_out
            grad_q = grad_q + weight * level_back
            dotted = jnp.sum(level_out * do_f, axis=1, keepdims=True)
            cross = jnp.where(lane == first + b, weight * dotted, cross)
        attn_ref[ts, :] = attn.astype(attn_ref.dtype)
        gq_ref[ts, :] = grad_q.astype(gq_ref.dtype)
        gk_ref[ts, :] = (dk_ref[ts, :] + dot_nt(v_ref[ts, :], key_state)).astype(gk_ref.dtype)
        gv_ref[ts, :] = (dv_ref[ts, :] + dot_nn(k_ref[ts, :], key_state)).astype(gv_ref.dtype)
        cross_parts.append(cross)
    cross_all = jnp.concatenate(cross_parts, axis=0)
    gg_ref[...] = ggl_ref[...] + jnp.transpose(cross_all)


def final_part(query_rows, key_rows, value_rows, out_grad, partials, gate_t, level_state, key_state):
    heads, block_len, width = query_rows.shape
    nlev = gate_t.shape[1]
    nbits = level_state.shape[0]
    row_spec = pl.BlockSpec((None, block_len, width), lambda h: (h, 0, 0))
    gate_spec = pl.BlockSpec((None, nlev, block_len), lambda h: (h, 0, 0))
    ls_spec = pl.BlockSpec((nbits, None, width, width), lambda h: (0, h, 0, 0))
    ks_spec = pl.BlockSpec((None, width, width), lambda h: (h, 0, 0))
    bf = jnp.bfloat16
    return pl.pallas_call(
        final_kernel,
        grid=(heads,),
        in_specs=[row_spec] * 8 + [gate_spec, gate_spec, ls_spec, ks_spec],
        out_specs=[row_spec] * 4 + [gate_spec],
        out_shape=[jax.ShapeDtypeStruct((heads, block_len, width), bf)] * 4
        + [jax.ShapeDtypeStruct((heads, nlev, block_len), jnp.float32)],
        compiler_params=pltpu.CompilerParams(dimension_semantics=("arbitrary",)),
        cost_estimate=pl.CostEstimate(
            flops=heads * block_len * width * width * 2 * (2 * nbits + 2),
            transcendentals=0,
            bytes_accessed=heads * block_len * (8 * width * 2 + 4 * width * 4 + 4 * nlev * 4),
        ),
    )(query_rows, key_rows, value_rows, out_grad, *partials[:4], partials[4], gate_t,
      level_state, key_state)


def same_doc(block_levels, earlier, later):
    return block_levels[later, earlier] >= 0


def level_network(state, block_levels, me, nbits, ctx_len):
    x = state
    levels = []
    for k in range(nbits):
        bit = ((me >> k) & 1) == 1
        lo = (me >> (k + 1)) << (k + 1)
        end_low = lo + (1 << k) - 1
        end_high = lo + (2 << k) - 1
        joined = same_doc(block_levels, end_low, end_high)
        mine = same_doc(block_levels, end_low, me)
        if k < nbits - 1:
            perm = [(j, j ^ (1 << k)) for j in range(ctx_len)]
        else:
            perm = [(j, j ^ (1 << k)) for j in range(ctx_len) if not (j >> k) & 1]
        got = lax.ppermute(x, "ctx", perm)
        levels.append(jnp.where(bit & mine, got, 0.0).astype(jnp.bfloat16))
        if k < nbits - 1:
            x = jnp.where(
                bit, x + jnp.where(joined, got, 0.0), got + jnp.where(joined, x, 0.0)
            )
    return jnp.stack(levels)


def key_network(grad_state, block_levels, me, nbits, ctx_len):
    acc = None
    for k in reversed(range(nbits)):
        bit = ((me >> k) & 1) == 1
        lo = (me >> (k + 1)) << (k + 1)
        end_low = lo + (1 << k) - 1
        end_high = lo + (2 << k) - 1
        joined = same_doc(block_levels, end_low, end_high)
        mine = same_doc(block_levels, end_low, me)
        term = jnp.where(bit & mine, grad_state[k], 0.0)
        if acc is None:
            send = term
            own = None
            perm = [(j, j ^ (1 << k)) for j in range(ctx_len) if (j >> k) & 1]
        else:
            kept = jnp.where(joined, acc, 0.0)
            send = jnp.where(bit, term + kept, acc)
            own = jnp.where(bit, acc, kept)
            perm = [(j, j ^ (1 << k)) for j in range(ctx_len)]
        got = lax.ppermute(send, "ctx", perm)
        acc = got if own is None else own + got
    return acc


def per_device(query_rows, key_rows, value_rows, out_grad, level_gate, block_levels, ctx_len):
    level_total = level_gate.shape[0]
    block_len = query_rows.shape[1]
    log_block = block_len.bit_length() - 1
    nbits = level_total - log_block - 1
    me = lax.axis_index("ctx")
    weights = jnp.exp(level_gate)
    cross_weight = weights[log_block + 1 :]

    own_state = jnp.einsum(
        "hcd,hce->hde", key_rows, value_rows, preferred_element_type=jnp.float32
    ).astype(jnp.bfloat16)
    scaled = (cross_weight[..., None] * out_grad[None].astype(jnp.float32)).astype(jnp.bfloat16)
    grad_state = jnp.einsum(
        "hcd,bhce->bhde", query_rows, scaled, preferred_element_type=jnp.float32
    ).astype(jnp.bfloat16)

    level_state = level_network(
        own_state.astype(jnp.float32), block_levels, me, nbits, ctx_len
    )
    key_state = key_network(
        grad_state.astype(jnp.float32), block_levels, me, nbits, ctx_len
    ).astype(jnp.bfloat16)

    gate_t = weights.transpose(1, 0, 2)
    partials = local_part(query_rows, key_rows, value_rows, out_grad, gate_t)
    attn, grad_q, grad_k, grad_v, grad_gate = final_part(
        query_rows, key_rows, value_rows, out_grad, partials, gate_t, level_state, key_state
    )
    return (attn, grad_q, grad_k, grad_v, grad_gate.transpose(1, 0, 2))


def solution(mesh):
    ctx_len = mesh.shape["ctx"]
    in_specs = (
        P("head", "ctx", None),
        P("head", "ctx", None),
        P("head", "ctx", None),
        P("head", "ctx", None),
        P(None, "head", "ctx"),
        P(),
    )
    out_specs = (
        P("head", "ctx", None),
        P("head", "ctx", None),
        P("head", "ctx", None),
        P("head", "ctx", None),
        P(None, "head", "ctx"),
    )

    def body(*args):
        return per_device(*args, ctx_len=ctx_len)

    return jax.shard_map(
        body, mesh=mesh, in_specs=in_specs, out_specs=out_specs, check_vma=False
    )
```

```python
import jax
import jax.numpy as jnp
from jax import lax
from jax.experimental import pallas as pl
from jax.experimental.pallas import tpu as pltpu
from jax.sharding import PartitionSpec as P


TILE = 256
SUB = 128


def bit_length_small(numbers, count):
    total = jnp.zeros(numbers.shape, jnp.int32)
    for shift_by in range(count):
        total = total + (numbers >= (1 << shift_by)).astype(jnp.int32)
    return total


def dot_nt(a, b):
    return lax.dot_general(a, b, (((1,), (1,)), ((), ())), preferred_element_type=jnp.float32)


def dot_tn(a, b):
    return lax.dot_general(a, b, (((0,), (0,)), ((), ())), preferred_element_type=jnp.float32)


def dot_nn(a, b):
    return lax.dot_general(a, b, (((1,), (0,)), ((), ())), preferred_element_type=jnp.float32)


def local_kernel(q_ref, k_ref, v_ref, do_ref, g_ref, *refs):
    o_ref, dq_ref, dk_ref, dv_ref, gg_ref = refs[-5:]
    block_len = q_ref.shape[0]
    tiles = block_len // TILE
    log_tile = TILE.bit_length() - 1
    log_sub = SUB.bit_length() - 1
    keys = lax.broadcasted_iota(jnp.int32, (SUB, SUB), 0)
    queries = lax.broadcasted_iota(jnp.int32, (SUB, SUB), 1)
    diag_level = jnp.where(
        keys <= queries, bit_length_small(jnp.bitwise_xor(keys, queries), log_sub), -1
    )
    for ref in (o_ref, dq_ref, dk_ref, dv_ref, gg_ref):
        ref[...] = jnp.zeros(ref.shape, jnp.float32)

    def pair(t0, s0, size, level):
        ts = pl.ds(t0, size)
        ss = pl.ds(s0, size)
        qi = q_ref[ts, :]
        doi = do_ref[ts, :]
        kj = k_ref[ss, :]
        vj = v_ref[ss, :]
        gi = g_ref[:, ts]
        scores = dot_nt(kj, qi)
        back = dot_nt(vj, doi)
        prod = scores * back
        if level is not None:
            weight = gi[level : level + 1, :]
            gg_ref[level : level + 1, ts] += jnp.sum(prod, axis=0, keepdims=True)
        else:
            weight = jnp.zeros((size, size), jnp.float32)
            for lev in range(log_sub + 1):
                hit = diag_level == lev
                weight = jnp.where(hit, gi[lev : lev + 1, :], weight)
                gg_ref[lev : lev + 1, ts] += jnp.sum(
                    jnp.where(hit, prod, 0.0), axis=0, keepdims=True
                )
        probs = (scores * weight).astype(jnp.bfloat16)
        dprobs = (back * weight).astype(jnp.bfloat16)
        o_ref[ts, :] += dot_tn(probs, vj)
        dq_ref[ts, :] += dot_tn(dprobs, kj)
        dk_ref[ss, :] += dot_nn(dprobs, qi)
        dv_ref[ss, :] += dot_nn(probs, doi)

    for i in range(tiles):
        for j in range(i):
            pair(i * TILE, j * TILE, TILE, log_tile + (i ^ j).bit_length())
        for a in range(TILE // SUB):
            for b in range(a):
                pair(i * TILE + a * SUB, i * TILE + b * SUB, SUB, log_sub + (a ^ b).bit_length())
            pair(i * TILE + a * SUB, i * TILE + a * SUB, SUB, None)
    gg_ref[...] = gg_ref[...] * g_ref[...]


def local_part(query_rows, key_rows, value_rows, out_grad, gate_t, h, outs):
    heads, block_len, width = query_rows.shape
    nlev = gate_t.shape[1]
    f32 = jnp.float32
    pairs = (block_len // TILE) * (block_len // TILE + 1) // 2
    flops = pairs * 6 * 2 * TILE * TILE * width
    shapes = [jax.ShapeDtypeStruct((heads, block_len, width), f32)] * 4 + [
        jax.ShapeDtypeStruct((heads, nlev, block_len), f32)
    ]
    row_spec = pl.BlockSpec((None, block_len, width), lambda i: (h, 0, 0))
    gate_spec = pl.BlockSpec((None, nlev, block_len), lambda i: (h, 0, 0))
    args = (query_rows, key_rows, value_rows, out_grad, gate_t)
    in_specs = [row_spec] * 4 + [gate_spec]
    aliases = {}
    if outs is not None:
        args = args + tuple(outs)
        in_specs = in_specs + [pl.BlockSpec(memory_space=pl.ANY)] * 5
        aliases = {5 + n: n for n in range(5)}
    return pl.pallas_call(
        local_kernel,
        grid=(1,),
        in_specs=in_specs,
        out_specs=[row_spec] * 4 + [gate_spec],
        out_shape=shapes,
        input_output_aliases=aliases,
        compiler_params=pltpu.CompilerParams(dimension_semantics=("arbitrary",)),
        cost_estimate=pl.CostEstimate(
            flops=flops,
            transcendentals=0,
            bytes_accessed=block_len * (4 * width * 2 + 4 * width * 4 + 2 * nlev * 4),
        ),
    )(*args)


def final_kernel(q_ref, k_ref, v_ref, do_ref, o_ref, dq_ref, dk_ref, dv_ref, ggl_ref, g_ref,
                 ls_ref, ks_ref, attn_ref, gq_ref, gk_ref, gv_ref, gg_ref):
    block_len = q_ref.shape[0]
    nlev = g_ref.shape[0]
    nbits = ls_ref.shape[0]
    first = nlev - nbits
    gate_cols = jnp.transpose(g_ref[...])
    key_state = ks_ref[...]
    lane = lax.broadcasted_iota(jnp.int32, (TILE, nlev), 1)
    cross_parts = []
    for i in range(block_len // TILE):
        ts = pl.ds(i * TILE, TILE)
        qi = q_ref[ts, :]
        doi = do_ref[ts, :]
        do_f = doi.astype(jnp.float32)
        attn = o_ref[ts, :]
        grad_q = dq_ref[ts, :]
        cross = jnp.zeros((TILE, nlev), jnp.float32)
        for b in range(nbits):
            state = ls_ref[b]
            weight = gate_cols[i * TILE : (i + 1) * TILE, first + b : first + b + 1]
            level_out = dot_nn(qi, state)
            level_back = dot_nt(doi, state)
            attn = attn + weight * level_out
            grad_q = grad_q + weight * level_back
            dotted = jnp.sum(level_out * do_f, axis=1, keepdims=True)
            cross = jnp.where(lane == first + b, weight * dotted, cross)
        attn_ref[ts, :] = attn.astype(attn_ref.dtype)
        gq_ref[ts, :] = grad_q.astype(gq_ref.dtype)
        gk_ref[ts, :] = (dk_ref[ts, :] + dot_nt(v_ref[ts, :], key_state)).astype(gk_ref.dtype)
        gv_ref[ts, :] = (dv_ref[ts, :] + dot_nn(k_ref[ts, :], key_state)).astype(gv_ref.dtype)
        cross_parts.append(cross)
    cross_all = jnp.concatenate(cross_parts, axis=0)
    gg_ref[...] = ggl_ref[...] + jnp.transpose(cross_all)


def final_part(query_rows, key_rows, value_rows, out_grad, partials, gate_t, level_state, key_state):
    heads, block_len, width = query_rows.shape
    nlev = gate_t.shape[1]
    nbits = level_state.shape[0]
    row_spec = pl.BlockSpec((None, block_len, width), lambda h: (h, 0, 0))
    gate_spec = pl.BlockSpec((None, nlev, block_len), lambda h: (h, 0, 0))
    ls_spec = pl.BlockSpec((nbits, None, width, width), lambda h: (0, h, 0, 0))
    ks_spec = pl.BlockSpec((None, width, width), lambda h: (h, 0, 0))
    bf = jnp.bfloat16
    return pl.pallas_call(
        final_kernel,
        grid=(heads,),
        in_specs=[row_spec] * 8 + [gate_spec, gate_spec, ls_spec, ks_spec],
        out_specs=[row_spec] * 4 + [gate_spec],
        out_shape=[jax.ShapeDtypeStruct((heads, block_len, width), bf)] * 4
        + [jax.ShapeDtypeStruct((heads, nlev, block_len), jnp.float32)],
        compiler_params=pltpu.CompilerParams(dimension_semantics=("arbitrary",)),
        cost_estimate=pl.CostEstimate(
            flops=heads * block_len * width * width * 2 * (2 * nbits + 2),
            transcendentals=0,
            bytes_accessed=heads * block_len * (8 * width * 2 + 4 * width * 4 + 4 * nlev * 4),
        ),
    )(query_rows, key_rows, value_rows, out_grad, *partials[:4], partials[4], gate_t,
      level_state, key_state)


def same_doc(block_levels, earlier, later):
    return block_levels[later, earlier] >= 0


def step_masks(block_levels, me, k):
    bit = ((me >> k) & 1) == 1
    lo = (me >> (k + 1)) << (k + 1)
    end_low = lo + (1 << k) - 1
    end_high = lo + (2 << k) - 1
    joined = same_doc(block_levels, end_low, end_high)
    mine = same_doc(block_levels, end_low, me)
    return bit, joined, mine


def pairs_of(k, ctx_len, sender_bit=None):
    return [
        (j, j ^ (1 << k))
        for j in range(ctx_len)
        if sender_bit is None or ((j >> k) & 1) == sender_bit
    ]


def per_device(query_rows, key_rows, value_rows, out_grad, level_gate, block_levels, ctx_len):
    level_total = level_gate.shape[0]
    block_len = query_rows.shape[1]
    log_block = block_len.bit_length() - 1
    nbits = level_total - log_block - 1
    me = lax.axis_index("ctx")
    weights = jnp.exp(level_gate)
    cross_weight = weights[log_block + 1 :]

    own_state = jnp.einsum(
        "hcd,hce->hde", key_rows, value_rows, preferred_element_type=jnp.float32
    ).astype(jnp.bfloat16)
    scaled = (cross_weight[..., None] * out_grad[None].astype(jnp.float32)).astype(jnp.bfloat16)
    grad_state = jnp.einsum(
        "hcd,bhce->bhde", query_rows, scaled, preferred_element_type=jnp.float32
    ).astype(jnp.bfloat16)

    gate_t = weights.transpose(1, 0, 2)
    grad_wide = grad_state.astype(jnp.float32)
    heads = query_rows.shape[0]
    fwd_x = own_state.astype(jnp.float32)
    bwd_acc = None
    levels = []
    partials = None
    for r in range(nbits):
        kf = r
        kb = nbits - 1 - r
        fwd_got = lax.ppermute(
            fwd_x, "ctx", pairs_of(kf, ctx_len, None if kf < nbits - 1 else 0)
        )
        bit, joined, mine = step_masks(block_levels, me, kb)
        term = jnp.where(bit & mine, grad_wide[kb], 0.0)
        if bwd_acc is None:
            send, own = term, None
            bwd_pairs = pairs_of(kb, ctx_len, 1)
        else:
            kept = jnp.where(joined, bwd_acc, 0.0)
            send = jnp.where(bit, term + kept, bwd_acc)
            own = jnp.where(bit, bwd_acc, kept)
            bwd_pairs = pairs_of(kb, ctx_len)
        bwd_got = lax.ppermute(send, "ctx", bwd_pairs)
        if r < heads:
            partials = local_part(query_rows, key_rows, value_rows, out_grad, gate_t, r, partials)
            fwd_got, bwd_got, partials = lax.optimization_barrier((fwd_got, bwd_got, partials))
        bwd_acc = bwd_got if own is None else own + bwd_got
        bit, joined, mine = step_masks(block_levels, me, kf)
        levels.append(jnp.where(bit & mine, fwd_got, 0.0).astype(jnp.bfloat16))
        if kf < nbits - 1:
            fwd_x = jnp.where(
                bit, fwd_x + jnp.where(joined, fwd_got, 0.0), fwd_got + jnp.where(joined, fwd_x, 0.0)
            )
    for h in range(nbits, heads):
        partials = local_part(query_rows, key_rows, value_rows, out_grad, gate_t, h, partials)
    level_state = jnp.stack(levels)
    key_state = bwd_acc.astype(jnp.bfloat16)
    attn, grad_q, grad_k, grad_v, grad_gate = final_part(
        query_rows, key_rows, value_rows, out_grad, partials, gate_t, level_state, key_state
    )
    return (attn, grad_q, grad_k, grad_v, grad_gate.transpose(1, 0, 2))


def solution(mesh):
    ctx_len = mesh.shape["ctx"]
    in_specs = (
        P("head", "ctx", None),
        P("head", "ctx", None),
        P("head", "ctx", None),
        P("head", "ctx", None),
        P(None, "head", "ctx"),
        P(),
    )
    out_specs = (
        P("head", "ctx", None),
        P("head", "ctx", None),
        P("head", "ctx", None),
        P("head", "ctx", None),
        P(None, "head", "ctx"),
    )

    def body(*args):
        return per_device(*args, ctx_len=ctx_len)

    return jax.shard_map(
        body, mesh=mesh, in_specs=in_specs, out_specs=out_specs, check_vma=False
    )
```

```python
import jax
import jax.numpy as jnp
from jax import lax
from jax.experimental import pallas as pl
from jax.experimental.pallas import tpu as pltpu
from jax.sharding import PartitionSpec as P


TILE = 256
SUB = 128


def bit_length_small(numbers, count):
    total = jnp.zeros(numbers.shape, jnp.int32)
    for shift_by in range(count):
        total = total + (numbers >= (1 << shift_by)).astype(jnp.int32)
    return total


def dot_nt(a, b):
    return lax.dot_general(a, b, (((1,), (1,)), ((), ())), preferred_element_type=jnp.float32)


def dot_tn(a, b):
    return lax.dot_general(a, b, (((0,), (0,)), ((), ())), preferred_element_type=jnp.float32)


def dot_nn(a, b):
    return lax.dot_general(a, b, (((1,), (0,)), ((), ())), preferred_element_type=jnp.float32)


def local_kernel(q_ref, k_ref, v_ref, do_ref, g_ref, *refs):
    o_ref, dq_ref, dk_ref, dv_ref, gg_ref = refs[-5:]
    block_len = q_ref.shape[0]
    tiles = block_len // TILE
    log_tile = TILE.bit_length() - 1
    log_sub = SUB.bit_length() - 1
    keys = lax.broadcasted_iota(jnp.int32, (SUB, SUB), 0)
    queries = lax.broadcasted_iota(jnp.int32, (SUB, SUB), 1)
    diag_level = jnp.where(
        keys <= queries, bit_length_small(jnp.bitwise_xor(keys, queries), log_sub), -1
    )
    for ref in (o_ref, dq_ref, dk_ref, dv_ref, gg_ref):
        ref[...] = jnp.zeros(ref.shape, jnp.float32)

    def pair(t0, s0, size, level):
        ts = pl.ds(t0, size)
        ss = pl.ds(s0, size)
        qi = q_ref[ts, :]
        doi = do_ref[ts, :]
        kj = k_ref[ss, :]
        vj = v_ref[ss, :]
        gi = g_ref[:, ts]
        scores = dot_nt(kj, qi)
        back = dot_nt(vj, doi)
        prod = scores * back
        if level is not None:
            weight = gi[level : level + 1, :]
            gg_ref[level : level + 1, ts] += jnp.sum(prod, axis=0, keepdims=True)
        else:
            weight = jnp.zeros((size, size), jnp.float32)
            for lev in range(log_sub + 1):
                hit = diag_level == lev
                weight = jnp.where(hit, gi[lev : lev + 1, :], weight)
                gg_ref[lev : lev + 1, ts] += jnp.sum(
                    jnp.where(hit, prod, 0.0), axis=0, keepdims=True
                )
        probs = (scores * weight).astype(jnp.bfloat16)
        dprobs = (back * weight).astype(jnp.bfloat16)
        o_ref[:, ts] += dot_tn(vj, probs)
        dq_ref[:, ts] += dot_tn(kj, dprobs)
        dk_ref[ss, :] += dot_nn(dprobs, qi)
        dv_ref[ss, :] += dot_nn(probs, doi)

    for i in range(tiles):
        for j in range(i):
            pair(i * TILE, j * TILE, TILE, log_tile + (i ^ j).bit_length())
        for a in range(TILE // SUB):
            for b in range(a):
                pair(i * TILE + a * SUB, i * TILE + b * SUB, SUB, log_sub + (a ^ b).bit_length())
            pair(i * TILE + a * SUB, i * TILE + a * SUB, SUB, None)
    gg_ref[...] = gg_ref[...] * g_ref[...]


def local_part(query_rows, key_rows, value_rows, out_grad, gate_t, h, outs):
    heads, block_len, width = query_rows.shape
    nlev = gate_t.shape[1]
    f32 = jnp.float32
    pairs = (block_len // TILE) * (block_len // TILE + 1) // 2
    flops = pairs * 6 * 2 * TILE * TILE * width
    shapes = [jax.ShapeDtypeStruct((heads, width, block_len), f32)] * 2 + [
        jax.ShapeDtypeStruct((heads, block_len, width), f32)
    ] * 2 + [jax.ShapeDtypeStruct((heads, nlev, block_len), f32)]
    row_spec = pl.BlockSpec((None, block_len, width), lambda i: (h, 0, 0))
    col_spec = pl.BlockSpec((None, width, block_len), lambda i: (h, 0, 0))
    gate_spec = pl.BlockSpec((None, nlev, block_len), lambda i: (h, 0, 0))
    args = (query_rows, key_rows, value_rows, out_grad, gate_t)
    in_specs = [row_spec] * 4 + [gate_spec]
    aliases = {}
    if outs is not None:
        args = args + tuple(outs)
        in_specs = in_specs + [pl.BlockSpec(memory_space=pl.ANY)] * 5
        aliases = {5 + n: n for n in range(5)}
    return pl.pallas_call(
        local_kernel,
        grid=(1,),
        in_specs=in_specs,
        out_specs=[col_spec] * 2 + [row_spec] * 2 + [gate_spec],
        out_shape=shapes,
        input_output_aliases=aliases,
        compiler_params=pltpu.CompilerParams(dimension_semantics=("arbitrary",)),
        cost_estimate=pl.CostEstimate(
            flops=flops,
            transcendentals=0,
            bytes_accessed=block_len * (4 * width * 2 + 4 * width * 4 + 2 * nlev * 4),
        ),
    )(*args)


def state_kernel(q_ref, k_ref, v_ref, do_ref, g_ref, st_ref, gs_ref):
    nlev = g_ref.shape[0]
    nbits = gs_ref.shape[0]
    first = nlev - nbits
    st_ref[...] = dot_tn(k_ref[...], v_ref[...]).astype(st_ref.dtype)
    do_t = jnp.transpose(do_ref[...].astype(jnp.float32))
    q = q_ref[...]
    for b in range(nbits):
        scaled_t = (g_ref[first + b : first + b + 1, :] * do_t).astype(jnp.bfloat16)
        gs_ref[b] = dot_nn(scaled_t, q).astype(gs_ref.dtype)


def state_part(query_rows, key_rows, value_rows, out_grad, gate_t, nbits):
    heads, block_len, width = query_rows.shape
    nlev = gate_t.shape[1]
    row_spec = pl.BlockSpec((None, block_len, width), lambda h: (h, 0, 0))
    gate_spec = pl.BlockSpec((None, nlev, block_len), lambda h: (h, 0, 0))
    bf = jnp.bfloat16
    return pl.pallas_call(
        state_kernel,
        grid=(heads,),
        in_specs=[row_spec] * 4 + [gate_spec],
        out_specs=[
            pl.BlockSpec((None, width, width), lambda h: (h, 0, 0)),
            pl.BlockSpec((nbits, None, width, width), lambda h: (0, h, 0, 0)),
        ],
        out_shape=[
            jax.ShapeDtypeStruct((heads, width, width), bf),
            jax.ShapeDtypeStruct((nbits, heads, width, width), bf),
        ],
        compiler_params=pltpu.CompilerParams(dimension_semantics=("arbitrary",)),
        cost_estimate=pl.CostEstimate(
            flops=heads * block_len * width * width * 2 * (nbits + 1),
            transcendentals=0,
            bytes_accessed=heads * block_len * (4 * width * 2 + nlev * 4),
        ),
    )(query_rows, key_rows, value_rows, out_grad, gate_t)


def final_kernel(q_ref, k_ref, v_ref, do_ref, o_ref, dq_ref, dk_ref, dv_ref, ggl_ref, g_ref,
                 ls_ref, lst_ref, kst_ref, attn_ref, gq_ref, gk_ref, gv_ref, gg_ref):
    block_len = q_ref.shape[0]
    nlev = g_ref.shape[0]
    nbits = ls_ref.shape[0]
    first = nlev - nbits
    key_state_t = kst_ref[...]
    gg_ref[...] = ggl_ref[...]
    for i in range(block_len // TILE):
        ts = pl.ds(i * TILE, TILE)
        qi = q_ref[ts, :]
        doi = do_ref[ts, :]
        do_t = jnp.transpose(doi.astype(jnp.float32))
        attn_t = o_ref[:, ts]
        grad_q_t = dq_ref[:, ts]
        for b in range(nbits):
            weight = g_ref[first + b : first + b + 1, ts]
            level_out_t = dot_nt(lst_ref[b], qi)
            level_back_t = dot_nt(ls_ref[b], doi)
            attn_t = attn_t + weight * level_out_t
            grad_q_t = grad_q_t + weight * level_back_t
            dotted = jnp.sum(level_out_t * do_t, axis=0, keepdims=True)
            gg_ref[first + b : first + b + 1, ts] = weight * dotted
        attn_ref[ts, :] = jnp.transpose(attn_t).astype(attn_ref.dtype)
        gq_ref[ts, :] = jnp.transpose(grad_q_t).astype(gq_ref.dtype)
        gk_ref[ts, :] = (dk_ref[ts, :] + dot_nn(v_ref[ts, :], key_state_t)).astype(gk_ref.dtype)
        gv_ref[ts, :] = (dv_ref[ts, :] + dot_nt(k_ref[ts, :], key_state_t)).astype(gv_ref.dtype)


def final_part(query_rows, key_rows, value_rows, out_grad, partials, gate_t, level_state, key_state_t):
    heads, block_len, width = query_rows.shape
    nlev = gate_t.shape[1]
    nbits = level_state.shape[0]
    row_spec = pl.BlockSpec((None, block_len, width), lambda h: (h, 0, 0))
    col_spec = pl.BlockSpec((None, width, block_len), lambda h: (h, 0, 0))
    gate_spec = pl.BlockSpec((None, nlev, block_len), lambda h: (h, 0, 0))
    ls_spec = pl.BlockSpec((nbits, None, width, width), lambda h: (0, h, 0, 0))
    ks_spec = pl.BlockSpec((None, width, width), lambda h: (h, 0, 0))
    bf = jnp.bfloat16
    level_state_t = jnp.swapaxes(level_state, 2, 3)
    return pl.pallas_call(
        final_kernel,
        grid=(heads,),
        in_specs=[row_spec] * 4 + [col_spec] * 2 + [row_spec] * 2
        + [gate_spec, gate_spec, ls_spec, ls_spec, ks_spec],
        out_specs=[row_spec] * 4 + [gate_spec],
        out_shape=[jax.ShapeDtypeStruct((heads, block_len, width), bf)] * 4
        + [jax.ShapeDtypeStruct((heads, nlev, block_len), jnp.float32)],
        compiler_params=pltpu.CompilerParams(dimension_semantics=("arbitrary",)),
        cost_estimate=pl.CostEstimate(
            flops=heads * block_len * width * width * 2 * (2 * nbits + 2),
            transcendentals=0,
            bytes_accessed=heads * block_len * (8 * width * 2 + 4 * width * 4 + 4 * nlev * 4),
        ),
    )(query_rows, key_rows, value_rows, out_grad, *partials[:4], partials[4], gate_t,
      level_state, level_state_t, key_state_t)


def same_doc(block_levels, earlier, later):
    return block_levels[later, earlier] >= 0


def step_masks(block_levels, me, k):
    bit = ((me >> k) & 1) == 1
    lo = (me >> (k + 1)) << (k + 1)
    end_low = lo + (1 << k) - 1
    end_high = lo + (2 << k) - 1
    joined = same_doc(block_levels, end_low, end_high)
    mine = same_doc(block_levels, end_low, me)
    return bit, joined, mine


def pairs_of(k, ctx_len, sender_bit=None):
    return [
        (j, j ^ (1 << k))
        for j in range(ctx_len)
        if sender_bit is None or ((j >> k) & 1) == sender_bit
    ]


def per_device(query_rows, key_rows, value_rows, out_grad, level_gate, block_levels, ctx_len):
    level_total = level_gate.shape[0]
    block_len = query_rows.shape[1]
    log_block = block_len.bit_length() - 1
    nbits = level_total - log_block - 1
    me = lax.axis_index("ctx")
    weights = jnp.exp(level_gate)
    cross_weight = weights[log_block + 1 :]

    gate_t = weights.transpose(1, 0, 2)
    own_state, grad_state = state_part(query_rows, key_rows, value_rows, out_grad, gate_t, nbits)
    grad_wide = grad_state.astype(jnp.float32)
    heads = query_rows.shape[0]
    fwd_x = own_state.astype(jnp.float32)
    bwd_acc = None
    levels = []
    partials = None
    for r in range(nbits):
        kf = r
        kb = nbits - 1 - r
        fwd_got = lax.ppermute(
            fwd_x, "ctx", pairs_of(kf, ctx_len, None if kf < nbits - 1 else 0)
        )
        bit, joined, mine = step_masks(block_levels, me, kb)
        term = jnp.where(bit & mine, grad_wide[kb], 0.0)
        if bwd_acc is None:
            send, own = term, None
            bwd_pairs = pairs_of(kb, ctx_len, 1)
        else:
            kept = jnp.where(joined, bwd_acc, 0.0)
            send = jnp.where(bit, term + kept, bwd_acc)
            own = jnp.where(bit, bwd_acc, kept)
            bwd_pairs = pairs_of(kb, ctx_len)
        bwd_got = lax.ppermute(send, "ctx", bwd_pairs)
        if r < heads:
            partials = local_part(query_rows, key_rows, value_rows, out_grad, gate_t, r, partials)
            fwd_got, bwd_got, partials = lax.optimization_barrier((fwd_got, bwd_got, partials))
        bwd_acc = bwd_got if own is None else own + bwd_got
        bit, joined, mine = step_masks(block_levels, me, kf)
        levels.append(jnp.where(bit & mine, fwd_got, 0.0).astype(jnp.bfloat16))
        if kf < nbits - 1:
            fwd_x = jnp.where(
                bit, fwd_x + jnp.where(joined, fwd_got, 0.0), fwd_got + jnp.where(joined, fwd_x, 0.0)
            )
    for h in range(nbits, heads):
        partials = local_part(query_rows, key_rows, value_rows, out_grad, gate_t, h, partials)
    level_state = jnp.stack(levels)
    key_state_t = bwd_acc.astype(jnp.bfloat16)
    attn, grad_q, grad_k, grad_v, grad_gate = final_part(
        query_rows, key_rows, value_rows, out_grad, partials, gate_t, level_state, key_state_t
    )
    return (attn, grad_q, grad_k, grad_v, grad_gate.transpose(1, 0, 2))


def solution(mesh):
    ctx_len = mesh.shape["ctx"]
    in_specs = (
        P("head", "ctx", None),
        P("head", "ctx", None),
        P("head", "ctx", None),
        P("head", "ctx", None),
        P(None, "head", "ctx"),
        P(),
    )
    out_specs = (
        P("head", "ctx", None),
        P("head", "ctx", None),
        P("head", "ctx", None),
        P("head", "ctx", None),
        P(None, "head", "ctx"),
    )

    def body(*args):
        return per_device(*args, ctx_len=ctx_len)

    return jax.shard_map(
        body, mesh=mesh, in_specs=in_specs, out_specs=out_specs, check_vma=False
    )
```

```python
import jax
import jax.numpy as jnp
from jax import lax
from jax.experimental import pallas as pl
from jax.experimental.pallas import tpu as pltpu
from jax.sharding import PartitionSpec as P


TILE = 256
SUB = 128


def bit_length_small(numbers, count):
    total = jnp.zeros(numbers.shape, jnp.int32)
    for shift_by in range(count):
        total = total + (numbers >= (1 << shift_by)).astype(jnp.int32)
    return total


def dot_nt(a, b):
    return lax.dot_general(a, b, (((1,), (1,)), ((), ())), preferred_element_type=jnp.float32)


def dot_tn(a, b):
    return lax.dot_general(a, b, (((0,), (0,)), ((), ())), preferred_element_type=jnp.float32)


def dot_nn(a, b):
    return lax.dot_general(a, b, (((1,), (0,)), ((), ())), preferred_element_type=jnp.float32)


def local_kernel(q_ref, k_ref, v_ref, do_ref, g_ref, *refs):
    o_ref, dq_ref, dk_ref, dv_ref, gg_ref = refs[-5:]
    block_len = q_ref.shape[0]
    tiles = block_len // TILE
    log_tile = TILE.bit_length() - 1
    log_sub = SUB.bit_length() - 1
    keys = lax.broadcasted_iota(jnp.int32, (SUB, SUB), 0)
    queries = lax.broadcasted_iota(jnp.int32, (SUB, SUB), 1)
    diag_level = jnp.where(
        keys <= queries, bit_length_small(jnp.bitwise_xor(keys, queries), log_sub), -1
    )
    for ref in (o_ref, dq_ref, dk_ref, dv_ref, gg_ref):
        ref[...] = jnp.zeros(ref.shape, jnp.float32)

    def pair(t0, s0, size, level):
        ts = pl.ds(t0, size)
        ss = pl.ds(s0, size)
        qi = q_ref[ts, :]
        doi = do_ref[ts, :]
        kj = k_ref[ss, :]
        vj = v_ref[ss, :]
        gi = g_ref[:, ts]
        scores = dot_nt(kj, qi)
        back = dot_nt(vj, doi)
        prod = scores * back
        if level is not None:
            weight = gi[level : level + 1, :]
            gg_ref[level : level + 1, ts] += jnp.sum(prod, axis=0, keepdims=True)
        else:
            weight = jnp.zeros((size, size), jnp.float32)
            for lev in range(log_sub + 1):
                hit = diag_level == lev
                weight = jnp.where(hit, gi[lev : lev + 1, :], weight)
                gg_ref[lev : lev + 1, ts] += jnp.sum(
                    jnp.where(hit, prod, 0.0), axis=0, keepdims=True
                )
        probs = (scores * weight).astype(jnp.bfloat16)
        dprobs = (back * weight).astype(jnp.bfloat16)
        o_ref[:, ts] += dot_tn(vj, probs)
        dq_ref[:, ts] += dot_tn(kj, dprobs)
        dk_ref[ss, :] += dot_nn(dprobs, qi)
        dv_ref[ss, :] += dot_nn(probs, doi)

    for i in range(tiles):
        for j in range(i):
            pair(i * TILE, j * TILE, TILE, log_tile + (i ^ j).bit_length())
        for a in range(TILE // SUB):
            for b in range(a):
                pair(i * TILE + a * SUB, i * TILE + b * SUB, SUB, log_sub + (a ^ b).bit_length())
            pair(i * TILE + a * SUB, i * TILE + a * SUB, SUB, None)
    gg_ref[...] = gg_ref[...] * g_ref[...]


def local_part(query_rows, key_rows, value_rows, out_grad, gate_t, h, outs):
    heads, block_len, width = query_rows.shape
    nlev = gate_t.shape[1]
    f32 = jnp.float32
    pairs = (block_len // TILE) * (block_len // TILE + 1) // 2
    flops = pairs * 6 * 2 * TILE * TILE * width
    shapes = [jax.ShapeDtypeStruct((heads, width, block_len), f32)] * 2 + [
        jax.ShapeDtypeStruct((heads, block_len, width), f32)
    ] * 2 + [jax.ShapeDtypeStruct((heads, nlev, block_len), f32)]
    row_spec = pl.BlockSpec((None, block_len, width), lambda i: (h, 0, 0))
    col_spec = pl.BlockSpec((None, width, block_len), lambda i: (h, 0, 0))
    gate_spec = pl.BlockSpec((None, nlev, block_len), lambda i: (h, 0, 0))
    args = (query_rows, key_rows, value_rows, out_grad, gate_t)
    in_specs = [row_spec] * 4 + [gate_spec]
    aliases = {}
    if outs is not None:
        args = args + tuple(outs)
        in_specs = in_specs + [pl.BlockSpec(memory_space=pl.ANY)] * 5
        aliases = {5 + n: n for n in range(5)}
    return pl.pallas_call(
        local_kernel,
        grid=(1,),
        in_specs=in_specs,
        out_specs=[col_spec] * 2 + [row_spec] * 2 + [gate_spec],
        out_shape=shapes,
        input_output_aliases=aliases,
        compiler_params=pltpu.CompilerParams(dimension_semantics=("arbitrary",)),
        cost_estimate=pl.CostEstimate(
            flops=flops,
            transcendentals=0,
            bytes_accessed=block_len * (4 * width * 2 + 4 * width * 4 + 2 * nlev * 4),
        ),
    )(*args)


def state_kernel(q_ref, k_ref, v_ref, do_ref, g_ref, st_ref, gs_ref):
    nlev = g_ref.shape[0]
    nbits = gs_ref.shape[0]
    first = nlev - nbits
    st_ref[...] = dot_tn(k_ref[...], v_ref[...]).astype(st_ref.dtype)
    do_t = jnp.transpose(do_ref[...].astype(jnp.float32))
    q = q_ref[...]
    for b in range(nbits):
        scaled_t = (g_ref[first + b : first + b + 1, :] * do_t).astype(jnp.bfloat16)
        gs_ref[b] = dot_nn(scaled_t, q).astype(gs_ref.dtype)


def state_part(query_rows, key_rows, value_rows, out_grad, gate_t, nbits):
    heads, block_len, width = query_rows.shape
    nlev = gate_t.shape[1]
    row_spec = pl.BlockSpec((None, block_len, width), lambda h: (h, 0, 0))
    gate_spec = pl.BlockSpec((None, nlev, block_len), lambda h: (h, 0, 0))
    bf = jnp.bfloat16
    return pl.pallas_call(
        state_kernel,
        grid=(heads,),
        in_specs=[row_spec] * 4 + [gate_spec],
        out_specs=[
            pl.BlockSpec((None, width, width), lambda h: (h, 0, 0)),
            pl.BlockSpec((nbits, None, width, width), lambda h: (0, h, 0, 0)),
        ],
        out_shape=[
            jax.ShapeDtypeStruct((heads, width, width), bf),
            jax.ShapeDtypeStruct((nbits, heads, width, width), bf),
        ],
        compiler_params=pltpu.CompilerParams(dimension_semantics=("arbitrary",)),
        cost_estimate=pl.CostEstimate(
            flops=heads * block_len * width * width * 2 * (nbits + 1),
            transcendentals=0,
            bytes_accessed=heads * block_len * (4 * width * 2 + nlev * 4),
        ),
    )(query_rows, key_rows, value_rows, out_grad, gate_t)


def final_kernel(q_ref, k_ref, v_ref, do_ref, o_ref, dq_ref, dk_ref, dv_ref, ggl_ref, g_ref,
                 ls_ref, lst_ref, kst_ref, attn_ref, gq_ref, gk_ref, gv_ref, gg_ref):
    block_len = q_ref.shape[0]
    nlev = g_ref.shape[0]
    nbits = ls_ref.shape[0]
    first = nlev - nbits
    key_state_t = kst_ref[...]
    gg_ref[...] = ggl_ref[...]
    for i in range(block_len // TILE):
        ts = pl.ds(i * TILE, TILE)
        qi = q_ref[ts, :]
        doi = do_ref[ts, :]
        do_t = jnp.transpose(doi.astype(jnp.float32))
        attn_t = o_ref[:, ts]
        grad_q_t = dq_ref[:, ts]
        for b in range(nbits):
            weight = g_ref[first + b : first + b + 1, ts]
            level_out_t = dot_nt(lst_ref[b], qi)
            level_back_t = dot_nt(ls_ref[b], doi)
            attn_t = attn_t + weight * level_out_t
            grad_q_t = grad_q_t + weight * level_back_t
            dotted = jnp.sum(level_out_t * do_t, axis=0, keepdims=True)
            gg_ref[first + b : first + b + 1, ts] = weight * dotted
        attn_ref[ts, :] = jnp.transpose(attn_t).astype(attn_ref.dtype)
        gq_ref[ts, :] = jnp.transpose(grad_q_t).astype(gq_ref.dtype)
        gk_ref[ts, :] = (dk_ref[ts, :] + dot_nn(v_ref[ts, :], key_state_t)).astype(gk_ref.dtype)
        gv_ref[ts, :] = (dv_ref[ts, :] + dot_nt(k_ref[ts, :], key_state_t)).astype(gv_ref.dtype)


def final_part(query_rows, key_rows, value_rows, out_grad, partials, gate_t, level_state, key_state_t):
    heads, block_len, width = query_rows.shape
    nlev = gate_t.shape[1]
    nbits = level_state.shape[0]
    row_spec = pl.BlockSpec((None, block_len, width), lambda h: (h, 0, 0))
    col_spec = pl.BlockSpec((None, width, block_len), lambda h: (h, 0, 0))
    gate_spec = pl.BlockSpec((None, nlev, block_len), lambda h: (h, 0, 0))
    ls_spec = pl.BlockSpec((nbits, None, width, width), lambda h: (0, h, 0, 0))
    ks_spec = pl.BlockSpec((None, width, width), lambda h: (h, 0, 0))
    bf = jnp.bfloat16
    level_state_t = jnp.swapaxes(level_state, 2, 3)
    return pl.pallas_call(
        final_kernel,
        grid=(heads,),
        in_specs=[row_spec] * 4 + [col_spec] * 2 + [row_spec] * 2
        + [gate_spec, gate_spec, ls_spec, ls_spec, ks_spec],
        out_specs=[row_spec] * 4 + [gate_spec],
        out_shape=[jax.ShapeDtypeStruct((heads, block_len, width), bf)] * 4
        + [jax.ShapeDtypeStruct((heads, nlev, block_len), jnp.float32)],
        compiler_params=pltpu.CompilerParams(dimension_semantics=("arbitrary",)),
        cost_estimate=pl.CostEstimate(
            flops=heads * block_len * width * width * 2 * (2 * nbits + 2),
            transcendentals=0,
            bytes_accessed=heads * block_len * (8 * width * 2 + 4 * width * 4 + 4 * nlev * 4),
        ),
    )(query_rows, key_rows, value_rows, out_grad, *partials[:4], partials[4], gate_t,
      level_state, level_state_t, key_state_t)


def same_doc(block_levels, earlier, later):
    return block_levels[later, earlier] >= 0


def step_masks(block_levels, me, k):
    bit = ((me >> k) & 1) == 1
    lo = (me >> (k + 1)) << (k + 1)
    end_low = lo + (1 << k) - 1
    end_high = lo + (2 << k) - 1
    joined = same_doc(block_levels, end_low, end_high)
    mine = same_doc(block_levels, end_low, me)
    return bit, joined, mine


def pairs_of(k, ctx_len, sender_bit=None):
    return [
        (j, j ^ (1 << k))
        for j in range(ctx_len)
        if sender_bit is None or ((j >> k) & 1) == sender_bit
    ]


def per_device(query_rows, key_rows, value_rows, out_grad, level_gate, block_levels, ctx_len):
    level_total = level_gate.shape[0]
    block_len = query_rows.shape[1]
    log_block = block_len.bit_length() - 1
    nbits = level_total - log_block - 1
    me = lax.axis_index("ctx")
    weights = jnp.exp(level_gate)

    gate_t = weights.transpose(1, 0, 2)
    own_state, grad_state = state_part(query_rows, key_rows, value_rows, out_grad, gate_t, nbits)
    grad_wide = grad_state.astype(jnp.float32)
    heads = query_rows.shape[0]
    fwd_x = own_state.astype(jnp.float32)
    bwd_acc = None
    levels = []
    partials = None
    for r in range(nbits):
        kf = r
        kb = nbits - 1 - r
        if kf == 0 or kf == nbits - 1:
            fwd_got = lax.ppermute(
                fwd_x.astype(jnp.bfloat16), "ctx",
                pairs_of(kf, ctx_len, None if kf < nbits - 1 else 0),
            ).astype(jnp.float32)
        else:
            fwd_got = lax.ppermute(fwd_x, "ctx", pairs_of(kf, ctx_len))
        bit, joined, mine = step_masks(block_levels, me, kb)
        term = jnp.where(bit & mine, grad_wide[kb], 0.0)
        if bwd_acc is None:
            send, own = term, None
            bwd_pairs = pairs_of(kb, ctx_len, 1)
        else:
            kept = jnp.where(joined, bwd_acc, 0.0)
            send = jnp.where(bit, term + kept, bwd_acc)
            own = jnp.where(bit, bwd_acc, kept)
            bwd_pairs = pairs_of(kb, ctx_len)
        if own is None:
            bwd_got = lax.ppermute(send.astype(jnp.bfloat16), "ctx", bwd_pairs).astype(jnp.float32)
        else:
            bwd_got = lax.ppermute(send, "ctx", bwd_pairs)
        if r < heads:
            partials = local_part(query_rows, key_rows, value_rows, out_grad, gate_t, r, partials)
            fwd_got, bwd_got, partials = lax.optimization_barrier((fwd_got, bwd_got, partials))
        bwd_acc = bwd_got if own is None else own + bwd_got
        bit, joined, mine = step_masks(block_levels, me, kf)
        levels.append(jnp.where(bit & mine, fwd_got, 0.0).astype(jnp.bfloat16))
        if kf < nbits - 1:
            fwd_x = jnp.where(
                bit, fwd_x + jnp.where(joined, fwd_got, 0.0), fwd_got + jnp.where(joined, fwd_x, 0.0)
            )
    for h in range(nbits, heads):
        partials = local_part(query_rows, key_rows, value_rows, out_grad, gate_t, h, partials)
    level_state = jnp.stack(levels)
    key_state_t = bwd_acc.astype(jnp.bfloat16)
    attn, grad_q, grad_k, grad_v, grad_gate = final_part(
        query_rows, key_rows, value_rows, out_grad, partials, gate_t, level_state, key_state_t
    )
    return (attn, grad_q, grad_k, grad_v, grad_gate.transpose(1, 0, 2))


def solution(mesh):
    ctx_len = mesh.shape["ctx"]
    in_specs = (
        P("head", "ctx", None),
        P("head", "ctx", None),
        P("head", "ctx", None),
        P("head", "ctx", None),
        P(None, "head", "ctx"),
        P(),
    )
    out_specs = (
        P("head", "ctx", None),
        P("head", "ctx", None),
        P("head", "ctx", None),
        P("head", "ctx", None),
        P(None, "head", "ctx"),
    )

    def body(*args):
        return per_device(*args, ctx_len=ctx_len)

    return jax.shard_map(
        body, mesh=mesh, in_specs=in_specs, out_specs=out_specs, check_vma=False
    )
```

```python
import jax
import jax.numpy as jnp
from jax import lax
from jax.experimental import pallas as pl
from jax.experimental.pallas import tpu as pltpu
from jax.sharding import PartitionSpec as P


TILE = 256
SUB = 128


def bit_length_small(numbers, count):
    total = jnp.zeros(numbers.shape, jnp.int32)
    for shift_by in range(count):
        total = total + (numbers >= (1 << shift_by)).astype(jnp.int32)
    return total


def dot_nt(a, b):
    return lax.dot_general(a, b, (((1,), (1,)), ((), ())), preferred_element_type=jnp.float32)


def dot_tn(a, b):
    return lax.dot_general(a, b, (((0,), (0,)), ((), ())), preferred_element_type=jnp.float32)


def dot_nn(a, b):
    return lax.dot_general(a, b, (((1,), (0,)), ((), ())), preferred_element_type=jnp.float32)


def local_kernel(q_ref, k_ref, v_ref, do_ref, g_ref, *refs):
    o_ref, dq_ref, dk_ref, dv_ref, gg_ref = refs[-5:]
    block_len = q_ref.shape[0]
    tiles = block_len // TILE
    log_tile = TILE.bit_length() - 1
    log_sub = SUB.bit_length() - 1
    keys = lax.broadcasted_iota(jnp.int32, (SUB, SUB), 0)
    queries = lax.broadcasted_iota(jnp.int32, (SUB, SUB), 1)
    diag_level = jnp.where(
        keys <= queries, bit_length_small(jnp.bitwise_xor(keys, queries), log_sub), -1
    )
    for ref in (o_ref, dq_ref, dk_ref, dv_ref, gg_ref):
        ref[...] = jnp.zeros(ref.shape, jnp.float32)

    def pair(t0, s0, size, level):
        ts = pl.ds(t0, size)
        ss = pl.ds(s0, size)
        qi = q_ref[ts, :]
        doi = do_ref[ts, :]
        kj = k_ref[ss, :]
        vj = v_ref[ss, :]
        gi = g_ref[:, ts]
        scores = dot_nt(kj, qi)
        back = dot_nt(vj, doi)
        prod = scores * back
        if level is not None:
            weight = gi[level : level + 1, :]
            gg_ref[level : level + 1, ts] += jnp.sum(prod, axis=0, keepdims=True)
        else:
            weight = jnp.zeros((size, size), jnp.float32)
            for lev in range(log_sub + 1):
                hit = diag_level == lev
                weight = jnp.where(hit, gi[lev : lev + 1, :], weight)
                gg_ref[lev : lev + 1, ts] += jnp.sum(
                    jnp.where(hit, prod, 0.0), axis=0, keepdims=True
                )
        probs = (scores * weight).astype(jnp.bfloat16)
        dprobs = (back * weight).astype(jnp.bfloat16)
        o_ref[:, ts] += dot_tn(vj, probs)
        dq_ref[:, ts] += dot_tn(kj, dprobs)
        dk_ref[ss, :] += dot_nn(dprobs, qi)
        dv_ref[ss, :] += dot_nn(probs, doi)

    for i in range(tiles):
        for j in range(i):
            pair(i * TILE, j * TILE, TILE, log_tile + (i ^ j).bit_length())
        for a in range(TILE // SUB):
            for b in range(a):
                pair(i * TILE + a * SUB, i * TILE + b * SUB, SUB, log_sub + (a ^ b).bit_length())
            pair(i * TILE + a * SUB, i * TILE + a * SUB, SUB, None)
    gg_ref[...] = gg_ref[...] * g_ref[...]


def local_part(query_rows, key_rows, value_rows, out_grad, gate_t, h, outs):
    heads, block_len, width = query_rows.shape
    nlev = gate_t.shape[1]
    f32 = jnp.float32
    pairs = (block_len // TILE) * (block_len // TILE + 1) // 2
    flops = pairs * 6 * 2 * TILE * TILE * width
    shapes = [jax.ShapeDtypeStruct((heads, width, block_len), f32)] * 2 + [
        jax.ShapeDtypeStruct((heads, block_len, width), f32)
    ] * 2 + [jax.ShapeDtypeStruct((heads, nlev, block_len), f32)]
    row_spec = pl.BlockSpec((None, block_len, width), lambda i: (h, 0, 0))
    col_spec = pl.BlockSpec((None, width, block_len), lambda i: (h, 0, 0))
    gate_spec = pl.BlockSpec((None, nlev, block_len), lambda i: (h, 0, 0))
    args = (query_rows, key_rows, value_rows, out_grad, gate_t)
    in_specs = [row_spec] * 4 + [gate_spec]
    aliases = {}
    if outs is not None:
        args = args + tuple(outs)
        in_specs = in_specs + [pl.BlockSpec(memory_space=pl.ANY)] * 5
        aliases = {5 + n: n for n in range(5)}
    return pl.pallas_call(
        local_kernel,
        grid=(1,),
        in_specs=in_specs,
        out_specs=[col_spec] * 2 + [row_spec] * 2 + [gate_spec],
        out_shape=shapes,
        input_output_aliases=aliases,
        compiler_params=pltpu.CompilerParams(dimension_semantics=("arbitrary",)),
        cost_estimate=pl.CostEstimate(
            flops=flops,
            transcendentals=0,
            bytes_accessed=block_len * (4 * width * 2 + 4 * width * 4 + 2 * nlev * 4),
        ),
    )(*args)


def state_kernel(q_ref, k_ref, v_ref, do_ref, g_ref, st_ref, gs_ref):
    nlev = g_ref.shape[0]
    nbits = gs_ref.shape[0]
    first = nlev - nbits
    st_ref[...] = dot_tn(k_ref[...], v_ref[...]).astype(st_ref.dtype)
    do_t = jnp.transpose(do_ref[...].astype(jnp.float32))
    q = q_ref[...]
    for b in range(nbits):
        scaled_t = (g_ref[first + b : first + b + 1, :] * do_t).astype(jnp.bfloat16)
        gs_ref[b] = dot_nn(scaled_t, q).astype(gs_ref.dtype)


def state_part(query_rows, key_rows, value_rows, out_grad, gate_t, nbits):
    heads, block_len, width = query_rows.shape
    nlev = gate_t.shape[1]
    row_spec = pl.BlockSpec((None, block_len, width), lambda h: (h, 0, 0))
    gate_spec = pl.BlockSpec((None, nlev, block_len), lambda h: (h, 0, 0))
    bf = jnp.bfloat16
    return pl.pallas_call(
        state_kernel,
        grid=(heads,),
        in_specs=[row_spec] * 4 + [gate_spec],
        out_specs=[
            pl.BlockSpec((None, width, width), lambda h: (h, 0, 0)),
            pl.BlockSpec((nbits, None, width, width), lambda h: (0, h, 0, 0)),
        ],
        out_shape=[
            jax.ShapeDtypeStruct((heads, width, width), bf),
            jax.ShapeDtypeStruct((nbits, heads, width, width), bf),
        ],
        compiler_params=pltpu.CompilerParams(dimension_semantics=("arbitrary",)),
        cost_estimate=pl.CostEstimate(
            flops=heads * block_len * width * width * 2 * (nbits + 1),
            transcendentals=0,
            bytes_accessed=heads * block_len * (4 * width * 2 + nlev * 4),
        ),
    )(query_rows, key_rows, value_rows, out_grad, gate_t)


def final_kernel(q_ref, k_ref, v_ref, do_ref, o_ref, dq_ref, dk_ref, dv_ref, ggl_ref, g_ref,
                 ls_ref, lst_ref, kst_ref, attn_ref, gq_ref, gk_ref, gv_ref, gg_ref):
    block_len = q_ref.shape[0]
    nlev = g_ref.shape[0]
    nbits = ls_ref.shape[0]
    first = nlev - nbits
    key_state_t = kst_ref[...]
    gg_ref[...] = ggl_ref[...]
    for i in range(block_len // TILE):
        ts = pl.ds(i * TILE, TILE)
        qi = q_ref[ts, :]
        doi = do_ref[ts, :]
        do_t = jnp.transpose(doi.astype(jnp.float32))
        attn_t = o_ref[:, ts]
        grad_q_t = dq_ref[:, ts]
        for b in range(nbits):
            weight = g_ref[first + b : first + b + 1, ts]
            level_out_t = dot_nt(lst_ref[b], qi)
            level_back_t = dot_nt(ls_ref[b], doi)
            attn_t = attn_t + weight * level_out_t
            grad_q_t = grad_q_t + weight * level_back_t
            dotted = jnp.sum(level_out_t * do_t, axis=0, keepdims=True)
            gg_ref[first + b : first + b + 1, ts] = weight * dotted
        attn_ref[ts, :] = jnp.transpose(attn_t).astype(attn_ref.dtype)
        gq_ref[ts, :] = jnp.transpose(grad_q_t).astype(gq_ref.dtype)
        gk_ref[ts, :] = (dk_ref[ts, :] + dot_nn(v_ref[ts, :], key_state_t)).astype(gk_ref.dtype)
        gv_ref[ts, :] = (dv_ref[ts, :] + dot_nt(k_ref[ts, :], key_state_t)).astype(gv_ref.dtype)


def final_part(query_rows, key_rows, value_rows, out_grad, partials, gate_t, level_state, key_state_t):
    heads, block_len, width = query_rows.shape
    nlev = gate_t.shape[1]
    nbits = level_state.shape[0]
    row_spec = pl.BlockSpec((None, block_len, width), lambda h: (h, 0, 0))
    col_spec = pl.BlockSpec((None, width, block_len), lambda h: (h, 0, 0))
    gate_spec = pl.BlockSpec((None, nlev, block_len), lambda h: (h, 0, 0))
    ls_spec = pl.BlockSpec((nbits, None, width, width), lambda h: (0, h, 0, 0))
    ks_spec = pl.BlockSpec((None, width, width), lambda h: (h, 0, 0))
    bf = jnp.bfloat16
    level_state_t = jnp.swapaxes(level_state, 2, 3)
    return pl.pallas_call(
        final_kernel,
        grid=(heads,),
        in_specs=[row_spec] * 4 + [col_spec] * 2 + [row_spec] * 2
        + [gate_spec, gate_spec, ls_spec, ls_spec, ks_spec],
        out_specs=[row_spec] * 4 + [gate_spec],
        out_shape=[jax.ShapeDtypeStruct((heads, block_len, width), bf)] * 4
        + [jax.ShapeDtypeStruct((heads, nlev, block_len), jnp.float32)],
        compiler_params=pltpu.CompilerParams(dimension_semantics=("arbitrary",)),
        cost_estimate=pl.CostEstimate(
            flops=heads * block_len * width * width * 2 * (2 * nbits + 2),
            transcendentals=0,
            bytes_accessed=heads * block_len * (8 * width * 2 + 4 * width * 4 + 4 * nlev * 4),
        ),
    )(query_rows, key_rows, value_rows, out_grad, *partials[:4], partials[4], gate_t,
      level_state, level_state_t, key_state_t)


def same_doc(block_levels, earlier, later):
    return block_levels[later, earlier] >= 0


def step_masks(block_levels, me, k):
    bit = ((me >> k) & 1) == 1
    lo = (me >> (k + 1)) << (k + 1)
    end_low = lo + (1 << k) - 1
    end_high = lo + (2 << k) - 1
    joined = same_doc(block_levels, end_low, end_high)
    mine = same_doc(block_levels, end_low, me)
    return bit, joined, mine


def pairs_of(k, ctx_len, sender_bit=None):
    return [
        (j, j ^ (1 << k))
        for j in range(ctx_len)
        if sender_bit is None or ((j >> k) & 1) == sender_bit
    ]


def per_device(query_rows, key_rows, value_rows, out_grad, level_gate, block_levels, ctx_len):
    level_total = level_gate.shape[0]
    block_len = query_rows.shape[1]
    log_block = block_len.bit_length() - 1
    nbits = level_total - log_block - 1
    me = lax.axis_index("ctx")
    weights = jnp.exp(level_gate)

    gate_t = weights.transpose(1, 0, 2)
    own_state, grad_state = state_part(query_rows, key_rows, value_rows, out_grad, gate_t, nbits)
    grad_wide = grad_state.astype(jnp.float32)
    heads = query_rows.shape[0]
    fwd_x = own_state.astype(jnp.float32)
    bwd_acc = None
    levels = []
    partials = None
    for r in range(nbits):
        kf = r
        kb = nbits - 1 - r
        if kf == 0 or kf == nbits - 1:
            fwd_got = lax.ppermute(
                fwd_x.astype(jnp.bfloat16), "ctx",
                pairs_of(kf, ctx_len),
            ).astype(jnp.float32)
        else:
            fwd_got = lax.ppermute(fwd_x, "ctx", pairs_of(kf, ctx_len))
        bit, joined, mine = step_masks(block_levels, me, kb)
        term = jnp.where(bit & mine, grad_wide[kb], 0.0)
        if bwd_acc is None:
            send, own = term, None
            bwd_pairs = pairs_of(kb, ctx_len)
        else:
            kept = jnp.where(joined, bwd_acc, 0.0)
            send = jnp.where(bit, term + kept, bwd_acc)
            own = jnp.where(bit, bwd_acc, kept)
            bwd_pairs = pairs_of(kb, ctx_len)
        if own is None:
            bwd_got = lax.ppermute(send.astype(jnp.bfloat16), "ctx", bwd_pairs).astype(jnp.float32)
        else:
            bwd_got = lax.ppermute(send, "ctx", bwd_pairs)
        if r < heads:
            partials = local_part(query_rows, key_rows, value_rows, out_grad, gate_t, r, partials)
            fwd_got, bwd_got, partials = lax.optimization_barrier((fwd_got, bwd_got, partials))
        bwd_acc = bwd_got if own is None else own + bwd_got
        bit, joined, mine = step_masks(block_levels, me, kf)
        levels.append(jnp.where(bit & mine, fwd_got, 0.0).astype(jnp.bfloat16))
        if kf < nbits - 1:
            fwd_x = jnp.where(
                bit, fwd_x + jnp.where(joined, fwd_got, 0.0), fwd_got + jnp.where(joined, fwd_x, 0.0)
            )
    for h in range(nbits, heads):
        partials = local_part(query_rows, key_rows, value_rows, out_grad, gate_t, h, partials)
    level_state = jnp.stack(levels)
    key_state_t = bwd_acc.astype(jnp.bfloat16)
    attn, grad_q, grad_k, grad_v, grad_gate = final_part(
        query_rows, key_rows, value_rows, out_grad, partials, gate_t, level_state, key_state_t
    )
    return (attn, grad_q, grad_k, grad_v, grad_gate.transpose(1, 0, 2))


def solution(mesh):
    ctx_len = mesh.shape["ctx"]
    in_specs = (
        P("head", "ctx", None),
        P("head", "ctx", None),
        P("head", "ctx", None),
        P("head", "ctx", None),
        P(None, "head", "ctx"),
        P(),
    )
    out_specs = (
        P("head", "ctx", None),
        P("head", "ctx", None),
        P("head", "ctx", None),
        P("head", "ctx", None),
        P(None, "head", "ctx"),
    )

    def body(*args):
        return per_device(*args, ctx_len=ctx_len)

    return jax.shard_map(
        body, mesh=mesh, in_specs=in_specs, out_specs=out_specs, check_vma=False
    )
```

```python
import jax
import jax.numpy as jnp
from jax import lax
from jax.experimental import pallas as pl
from jax.experimental.pallas import tpu as pltpu
from jax.sharding import PartitionSpec as P


TILE = 256
SUB = 128


def bit_length_small(numbers, count):
    total = jnp.zeros(numbers.shape, jnp.int32)
    for shift_by in range(count):
        total = total + (numbers >= (1 << shift_by)).astype(jnp.int32)
    return total


def dot_nt(a, b):
    return lax.dot_general(a, b, (((1,), (1,)), ((), ())), preferred_element_type=jnp.float32)


def dot_tn(a, b):
    return lax.dot_general(a, b, (((0,), (0,)), ((), ())), preferred_element_type=jnp.float32)


def dot_nn(a, b):
    return lax.dot_general(a, b, (((1,), (0,)), ((), ())), preferred_element_type=jnp.float32)


def local_kernel(q_ref, k_ref, v_ref, do_ref, g_ref, *refs):
    o_ref, dq_ref, dk_ref, dv_ref, gg_ref = refs[-5:]
    block_len = q_ref.shape[0]
    tiles = block_len // TILE
    log_tile = TILE.bit_length() - 1
    log_sub = SUB.bit_length() - 1
    keys = lax.broadcasted_iota(jnp.int32, (SUB, SUB), 0)
    queries = lax.broadcasted_iota(jnp.int32, (SUB, SUB), 1)
    diag_level = jnp.where(
        keys <= queries, bit_length_small(jnp.bitwise_xor(keys, queries), log_sub), -1
    )
    for ref in (o_ref, dq_ref, dk_ref, dv_ref, gg_ref):
        ref[...] = jnp.zeros(ref.shape, jnp.float32)

    def pair(t0, s0, size, level):
        ts = pl.ds(t0, size)
        ss = pl.ds(s0, size)
        qi = q_ref[ts, :]
        doi = do_ref[ts, :]
        kj = k_ref[ss, :]
        vj = v_ref[ss, :]
        gi = g_ref[:, ts]
        scores = dot_nt(kj, qi)
        back = dot_nt(vj, doi)
        prod = scores * back
        if level is not None:
            weight = gi[level : level + 1, :]
            gg_ref[level : level + 1, ts] += jnp.sum(prod, axis=0, keepdims=True)
        else:
            weight = jnp.zeros((size, size), jnp.float32)
            for lev in range(log_sub + 1):
                hit = diag_level == lev
                weight = jnp.where(hit, gi[lev : lev + 1, :], weight)
                gg_ref[lev : lev + 1, ts] += jnp.sum(
                    jnp.where(hit, prod, 0.0), axis=0, keepdims=True
                )
        probs = (scores * weight).astype(jnp.bfloat16)
        dprobs = (back * weight).astype(jnp.bfloat16)
        o_ref[:, ts] += dot_tn(vj, probs)
        dq_ref[:, ts] += dot_tn(kj, dprobs)
        dk_ref[ss, :] += dot_nn(dprobs, qi)
        dv_ref[ss, :] += dot_nn(probs, doi)

    for i in range(tiles):
        for j in range(i):
            pair(i * TILE, j * TILE, TILE, log_tile + (i ^ j).bit_length())
        for a in range(TILE // SUB):
            for b in range(a):
                pair(i * TILE + a * SUB, i * TILE + b * SUB, SUB, log_sub + (a ^ b).bit_length())
            pair(i * TILE + a * SUB, i * TILE + a * SUB, SUB, None)
    gg_ref[...] = gg_ref[...] * g_ref[...]


def local_part(query_rows, key_rows, value_rows, out_grad, gate_t, h, outs):
    heads, block_len, width = query_rows.shape
    nlev = gate_t.shape[1]
    f32 = jnp.float32
    pairs = (block_len // TILE) * (block_len // TILE + 1) // 2
    flops = pairs * 6 * 2 * TILE * TILE * width
    shapes = [jax.ShapeDtypeStruct((heads, width, block_len), f32)] * 2 + [
        jax.ShapeDtypeStruct((heads, block_len, width), f32)
    ] * 2 + [jax.ShapeDtypeStruct((heads, nlev, block_len), f32)]
    row_spec = pl.BlockSpec((None, block_len, width), lambda i: (h, 0, 0))
    col_spec = pl.BlockSpec((None, width, block_len), lambda i: (h, 0, 0))
    gate_spec = pl.BlockSpec((None, nlev, block_len), lambda i: (h, 0, 0))
    args = (query_rows, key_rows, value_rows, out_grad, gate_t)
    in_specs = [row_spec] * 4 + [gate_spec]
    aliases = {}
    if outs is not None:
        args = args + tuple(outs)
        in_specs = in_specs + [pl.BlockSpec(memory_space=pl.ANY)] * 5
        aliases = {5 + n: n for n in range(5)}
    return pl.pallas_call(
        local_kernel,
        grid=(1,),
        in_specs=in_specs,
        out_specs=[col_spec] * 2 + [row_spec] * 2 + [gate_spec],
        out_shape=shapes,
        input_output_aliases=aliases,
        compiler_params=pltpu.CompilerParams(dimension_semantics=("arbitrary",)),
        cost_estimate=pl.CostEstimate(
            flops=flops,
            transcendentals=0,
            bytes_accessed=block_len * (4 * width * 2 + 4 * width * 4 + 2 * nlev * 4),
        ),
    )(*args)


def state_kernel(q_ref, k_ref, v_ref, do_ref, g_ref, st_ref, gs_ref):
    nlev = g_ref.shape[0]
    nbits = gs_ref.shape[0]
    first = nlev - nbits
    st_ref[...] = dot_tn(k_ref[...], v_ref[...]).astype(st_ref.dtype)
    do_t = jnp.transpose(do_ref[...].astype(jnp.float32))
    q = q_ref[...]
    for b in range(nbits):
        scaled_t = (g_ref[first + b : first + b + 1, :] * do_t).astype(jnp.bfloat16)
        gs_ref[b] = dot_nn(scaled_t, q).astype(gs_ref.dtype)


def state_part(query_rows, key_rows, value_rows, out_grad, gate_t, nbits):
    heads, block_len, width = query_rows.shape
    nlev = gate_t.shape[1]
    row_spec = pl.BlockSpec((None, block_len, width), lambda h: (h, 0, 0))
    gate_spec = pl.BlockSpec((None, nlev, block_len), lambda h: (h, 0, 0))
    bf = jnp.bfloat16
    return pl.pallas_call(
        state_kernel,
        grid=(heads,),
        in_specs=[row_spec] * 4 + [gate_spec],
        out_specs=[
            pl.BlockSpec((None, width, width), lambda h: (h, 0, 0)),
            pl.BlockSpec((nbits, None, width, width), lambda h: (0, h, 0, 0)),
        ],
        out_shape=[
            jax.ShapeDtypeStruct((heads, width, width), bf),
            jax.ShapeDtypeStruct((nbits, heads, width, width), bf),
        ],
        compiler_params=pltpu.CompilerParams(dimension_semantics=("arbitrary",)),
        cost_estimate=pl.CostEstimate(
            flops=heads * block_len * width * width * 2 * (nbits + 1),
            transcendentals=0,
            bytes_accessed=heads * block_len * (4 * width * 2 + nlev * 4),
        ),
    )(query_rows, key_rows, value_rows, out_grad, gate_t)


def final_kernel(q_ref, k_ref, v_ref, do_ref, o_ref, dq_ref, dk_ref, dv_ref, ggl_ref, g_ref,
                 ls_ref, lst_ref, kst_ref, attn_ref, gq_ref, gk_ref, gv_ref, gg_ref):
    block_len = q_ref.shape[0]
    nlev = g_ref.shape[0]
    nbits = ls_ref.shape[0]
    first = nlev - nbits
    key_state_t = kst_ref[...]
    gg_ref[...] = ggl_ref[...]
    for i in range(block_len // TILE):
        ts = pl.ds(i * TILE, TILE)
        qi = q_ref[ts, :]
        doi = do_ref[ts, :]
        do_t = jnp.transpose(doi.astype(jnp.float32))
        attn_t = o_ref[:, ts]
        grad_q_t = dq_ref[:, ts]
        for b in range(nbits):
            weight = g_ref[first + b : first + b + 1, ts]
            level_out_t = dot_nt(lst_ref[b], qi)
            level_back_t = dot_nt(ls_ref[b], doi)
            attn_t = attn_t + weight * level_out_t
            grad_q_t = grad_q_t + weight * level_back_t
            dotted = jnp.sum(level_out_t * do_t, axis=0, keepdims=True)
            gg_ref[first + b : first + b + 1, ts] = weight * dotted
        attn_ref[ts, :] = jnp.transpose(attn_t).astype(attn_ref.dtype)
        gq_ref[ts, :] = jnp.transpose(grad_q_t).astype(gq_ref.dtype)
        gk_ref[ts, :] = (dk_ref[ts, :] + dot_nn(v_ref[ts, :], key_state_t)).astype(gk_ref.dtype)
        gv_ref[ts, :] = (dv_ref[ts, :] + dot_nt(k_ref[ts, :], key_state_t)).astype(gv_ref.dtype)


def final_part(query_rows, key_rows, value_rows, out_grad, partials, gate_t, level_state, key_state_t):
    heads, block_len, width = query_rows.shape
    nlev = gate_t.shape[1]
    nbits = level_state.shape[0]
    row_spec = pl.BlockSpec((None, block_len, width), lambda h: (h, 0, 0))
    col_spec = pl.BlockSpec((None, width, block_len), lambda h: (h, 0, 0))
    gate_spec = pl.BlockSpec((None, nlev, block_len), lambda h: (h, 0, 0))
    ls_spec = pl.BlockSpec((nbits, None, width, width), lambda h: (0, h, 0, 0))
    ks_spec = pl.BlockSpec((None, width, width), lambda h: (h, 0, 0))
    bf = jnp.bfloat16
    level_state_t = jnp.swapaxes(level_state, 2, 3)
    return pl.pallas_call(
        final_kernel,
        grid=(heads,),
        in_specs=[row_spec] * 4 + [col_spec] * 2 + [row_spec] * 2
        + [gate_spec, gate_spec, ls_spec, ls_spec, ks_spec],
        out_specs=[row_spec] * 4 + [gate_spec],
        out_shape=[jax.ShapeDtypeStruct((heads, block_len, width), bf)] * 4
        + [jax.ShapeDtypeStruct((heads, nlev, block_len), jnp.float32)],
        compiler_params=pltpu.CompilerParams(dimension_semantics=("arbitrary",)),
        cost_estimate=pl.CostEstimate(
            flops=heads * block_len * width * width * 2 * (2 * nbits + 2),
            transcendentals=0,
            bytes_accessed=heads * block_len * (8 * width * 2 + 4 * width * 4 + 4 * nlev * 4),
        ),
    )(query_rows, key_rows, value_rows, out_grad, *partials[:4], partials[4], gate_t,
      level_state, level_state_t, key_state_t)


def same_doc(block_levels, earlier, later):
    return block_levels[later, earlier] >= 0


def step_masks(block_levels, me, k):
    bit = ((me >> k) & 1) == 1
    lo = (me >> (k + 1)) << (k + 1)
    end_low = lo + (1 << k) - 1
    end_high = lo + (2 << k) - 1
    joined = same_doc(block_levels, end_low, end_high)
    mine = same_doc(block_levels, end_low, me)
    return bit, joined, mine


def pairs_of(k, ctx_len, sender_bit=None):
    return [
        (j, j ^ (1 << k))
        for j in range(ctx_len)
        if sender_bit is None or ((j >> k) & 1) == sender_bit
    ]


def per_device(query_rows, key_rows, value_rows, out_grad, level_gate, block_levels, ctx_len):
    level_total = level_gate.shape[0]
    block_len = query_rows.shape[1]
    log_block = block_len.bit_length() - 1
    nbits = level_total - log_block - 1
    me = lax.axis_index("ctx")
    weights = jnp.exp(level_gate)

    gate_t = weights.transpose(1, 0, 2)
    own_state, grad_state = state_part(query_rows, key_rows, value_rows, out_grad, gate_t, nbits)
    grad_wide = grad_state.astype(jnp.float32)
    heads = query_rows.shape[0]
    steps = jnp.arange(nbits, dtype=jnp.int32)
    bit = ((me >> steps) & 1) == 1
    lo = (me >> (steps + 1)) << (steps + 1)
    end_low = lo + (1 << steps) - 1
    end_high = lo + (2 << steps) - 1
    joined = block_levels[end_high, end_low] >= 0
    mine = block_levels[me, end_low] >= 0
    one = jnp.float32(1.0)
    zero = jnp.float32(0.0)
    take = jnp.where(bit & mine, one, zero)
    keep_own = jnp.where(bit, one, jnp.where(joined, one, zero))
    keep_got = jnp.where(bit, jnp.where(joined, one, zero), one)
    fwd_x = own_state.astype(jnp.float32)
    bwd_acc = None
    levels = []
    partials = None
    for r in range(nbits):
        kf = r
        kb = nbits - 1 - r
        if kf == 0 or kf == nbits - 1:
            fwd_got = lax.ppermute(
                fwd_x.astype(jnp.bfloat16), "ctx", pairs_of(kf, ctx_len)
            ).astype(jnp.float32)
        else:
            fwd_got = lax.ppermute(fwd_x, "ctx", pairs_of(kf, ctx_len))
        term = take[kb] * grad_wide[kb]
        if bwd_acc is None:
            send, own = term, None
            bwd_got = lax.ppermute(send.astype(jnp.bfloat16), "ctx", pairs_of(kb, ctx_len)).astype(jnp.float32)
        else:
            send = term + keep_got[kb] * bwd_acc
            own = keep_own[kb] * bwd_acc
            bwd_got = lax.ppermute(send, "ctx", pairs_of(kb, ctx_len))
        if r < heads:
            partials = local_part(query_rows, key_rows, value_rows, out_grad, gate_t, r, partials)
            fwd_got, bwd_got, partials = lax.optimization_barrier((fwd_got, bwd_got, partials))
        bwd_acc = bwd_got if own is None else own + bwd_got
        levels.append((take[kf] * fwd_got).astype(jnp.bfloat16))
        if kf < nbits - 1:
            fwd_x = keep_own[kf] * fwd_x + keep_got[kf] * fwd_got
    for h in range(nbits, heads):
        partials = local_part(query_rows, key_rows, value_rows, out_grad, gate_t, h, partials)
    level_state = jnp.stack(levels)
    key_state_t = bwd_acc.astype(jnp.bfloat16)
    attn, grad_q, grad_k, grad_v, grad_gate = final_part(
        query_rows, key_rows, value_rows, out_grad, partials, gate_t, level_state, key_state_t
    )
    return (attn, grad_q, grad_k, grad_v, grad_gate.transpose(1, 0, 2))


def solution(mesh):
    ctx_len = mesh.shape["ctx"]
    in_specs = (
        P("head", "ctx", None),
        P("head", "ctx", None),
        P("head", "ctx", None),
        P("head", "ctx", None),
        P(None, "head", "ctx"),
        P(),
    )
    out_specs = (
        P("head", "ctx", None),
        P("head", "ctx", None),
        P("head", "ctx", None),
        P("head", "ctx", None),
        P(None, "head", "ctx"),
    )

    def body(*args):
        return per_device(*args, ctx_len=ctx_len)

    return jax.shard_map(
        body, mesh=mesh, in_specs=in_specs, out_specs=out_specs, check_vma=False
    )
```

```python
import jax
import jax.numpy as jnp
from jax import lax
from jax.experimental import pallas as pl
from jax.experimental.pallas import tpu as pltpu
from jax.sharding import PartitionSpec as P


TILE = 256
SUB = 128


def bit_length_small(numbers, count):
    total = jnp.zeros(numbers.shape, jnp.int32)
    for shift_by in range(count):
        total = total + (numbers >= (1 << shift_by)).astype(jnp.int32)
    return total


def dot_nt(a, b):
    return lax.dot_general(a, b, (((1,), (1,)), ((), ())), preferred_element_type=jnp.float32)


def dot_tn(a, b):
    return lax.dot_general(a, b, (((0,), (0,)), ((), ())), preferred_element_type=jnp.float32)


def dot_nn(a, b):
    return lax.dot_general(a, b, (((1,), (0,)), ((), ())), preferred_element_type=jnp.float32)


def local_kernel(q_ref, k_ref, v_ref, do_ref, g_ref, *refs):
    o_ref, dq_ref, dk_ref, dv_ref, gg_ref = refs[-5:]
    block_len = q_ref.shape[0]
    tiles = block_len // TILE
    log_tile = TILE.bit_length() - 1
    log_sub = SUB.bit_length() - 1
    keys = lax.broadcasted_iota(jnp.int32, (SUB, SUB), 0)
    queries = lax.broadcasted_iota(jnp.int32, (SUB, SUB), 1)
    diag_level = jnp.where(
        keys <= queries, bit_length_small(jnp.bitwise_xor(keys, queries), log_sub), -1
    )
    for ref in (o_ref, dq_ref, dk_ref, dv_ref, gg_ref):
        ref[...] = jnp.zeros(ref.shape, jnp.float32)

    def pair(t0, s0, size, level):
        ts = pl.ds(t0, size)
        ss = pl.ds(s0, size)
        qi = q_ref[ts, :]
        doi = do_ref[ts, :]
        kj = k_ref[ss, :]
        vj = v_ref[ss, :]
        gi = g_ref[:, ts]
        scores = dot_nt(kj, qi)
        back = dot_nt(vj, doi)
        prod = scores * back
        if level is not None:
            weight = gi[level : level + 1, :]
            gg_ref[level : level + 1, ts] += jnp.sum(prod, axis=0, keepdims=True)
        else:
            weight = jnp.zeros((size, size), jnp.float32)
            for lev in range(log_sub + 1):
                hit = diag_level == lev
                weight = jnp.where(hit, gi[lev : lev + 1, :], weight)
                gg_ref[lev : lev + 1, ts] += jnp.sum(
                    jnp.where(hit, prod, 0.0), axis=0, keepdims=True
                )
        probs = (scores * weight).astype(jnp.bfloat16)
        dprobs = (back * weight).astype(jnp.bfloat16)
        o_ref[:, ts] += dot_tn(vj, probs)
        dq_ref[:, ts] += dot_tn(kj, dprobs)
        dk_ref[ss, :] += dot_nn(dprobs, qi)
        dv_ref[ss, :] += dot_nn(probs, doi)

    for i in range(tiles):
        for j in range(i):
            pair(i * TILE, j * TILE, TILE, log_tile + (i ^ j).bit_length())
        for a in range(TILE // SUB):
            for b in range(a):
                pair(i * TILE + a * SUB, i * TILE + b * SUB, SUB, log_sub + (a ^ b).bit_length())
            pair(i * TILE + a * SUB, i * TILE + a * SUB, SUB, None)
    gg_ref[...] = gg_ref[...] * g_ref[...]


def local_part(query_rows, key_rows, value_rows, out_grad, gate_t, h, outs):
    heads, block_len, width = query_rows.shape
    nlev = gate_t.shape[1]
    f32 = jnp.float32
    pairs = (block_len // TILE) * (block_len // TILE + 1) // 2
    flops = pairs * 6 * 2 * TILE * TILE * width
    shapes = [jax.ShapeDtypeStruct((heads, width, block_len), f32)] * 2 + [
        jax.ShapeDtypeStruct((heads, block_len, width), f32)
    ] * 2 + [jax.ShapeDtypeStruct((heads, nlev, block_len), f32)]
    row_spec = pl.BlockSpec((None, block_len, width), lambda i: (h, 0, 0))
    col_spec = pl.BlockSpec((None, width, block_len), lambda i: (h, 0, 0))
    gate_spec = pl.BlockSpec((None, nlev, block_len), lambda i: (h, 0, 0))
    args = (query_rows, key_rows, value_rows, out_grad, gate_t)
    in_specs = [row_spec] * 4 + [gate_spec]
    aliases = {}
    if outs is not None:
        args = args + tuple(outs)
        in_specs = in_specs + [pl.BlockSpec(memory_space=pl.ANY)] * 5
        aliases = {5 + n: n for n in range(5)}
    return pl.pallas_call(
        local_kernel,
        grid=(1,),
        in_specs=in_specs,
        out_specs=[col_spec] * 2 + [row_spec] * 2 + [gate_spec],
        out_shape=shapes,
        input_output_aliases=aliases,
        compiler_params=pltpu.CompilerParams(dimension_semantics=("arbitrary",)),
        cost_estimate=pl.CostEstimate(
            flops=flops,
            transcendentals=0,
            bytes_accessed=block_len * (4 * width * 2 + 4 * width * 4 + 2 * nlev * 4),
        ),
    )(*args)


def state_kernel(q_ref, k_ref, v_ref, do_ref, g_ref, st_ref, gs_ref):
    nlev = g_ref.shape[0]
    nbits = gs_ref.shape[0]
    first = nlev - nbits
    st_ref[...] = dot_tn(k_ref[...], v_ref[...]).astype(st_ref.dtype)
    do_t = jnp.transpose(do_ref[...].astype(jnp.float32))
    q = q_ref[...]
    for b in range(nbits):
        scaled_t = (g_ref[first + b : first + b + 1, :] * do_t).astype(jnp.bfloat16)
        gs_ref[b] = dot_nn(scaled_t, q).astype(gs_ref.dtype)


def state_part(query_rows, key_rows, value_rows, out_grad, gate_t, nbits):
    heads, block_len, width = query_rows.shape
    nlev = gate_t.shape[1]
    row_spec = pl.BlockSpec((None, block_len, width), lambda h: (h, 0, 0))
    gate_spec = pl.BlockSpec((None, nlev, block_len), lambda h: (h, 0, 0))
    bf = jnp.bfloat16
    return pl.pallas_call(
        state_kernel,
        grid=(heads,),
        in_specs=[row_spec] * 4 + [gate_spec],
        out_specs=[
            pl.BlockSpec((None, width, width), lambda h: (h, 0, 0)),
            pl.BlockSpec((nbits, None, width, width), lambda h: (0, h, 0, 0)),
        ],
        out_shape=[
            jax.ShapeDtypeStruct((heads, width, width), bf),
            jax.ShapeDtypeStruct((nbits, heads, width, width), bf),
        ],
        compiler_params=pltpu.CompilerParams(dimension_semantics=("arbitrary",)),
        cost_estimate=pl.CostEstimate(
            flops=heads * block_len * width * width * 2 * (nbits + 1),
            transcendentals=0,
            bytes_accessed=heads * block_len * (4 * width * 2 + nlev * 4),
        ),
    )(query_rows, key_rows, value_rows, out_grad, gate_t)


def final_kernel(q_ref, k_ref, v_ref, do_ref, o_ref, dq_ref, dk_ref, dv_ref, ggl_ref, g_ref,
                 ls_ref, lst_ref, kst_ref, attn_ref, gq_ref, gk_ref, gv_ref, gg_ref):
    block_len = q_ref.shape[0]
    nlev = g_ref.shape[0]
    nbits = ls_ref.shape[0]
    first = nlev - nbits
    key_state_t = kst_ref[...]
    gg_ref[...] = ggl_ref[...]
    for i in range(block_len // TILE):
        ts = pl.ds(i * TILE, TILE)
        qi = q_ref[ts, :]
        doi = do_ref[ts, :]
        do_t = jnp.transpose(doi.astype(jnp.float32))
        attn_t = o_ref[:, ts]
        grad_q_t = dq_ref[:, ts]
        for b in range(nbits):
            weight = g_ref[first + b : first + b + 1, ts]
            level_out_t = dot_nt(lst_ref[b], qi)
            level_back_t = dot_nt(ls_ref[b], doi)
            attn_t = attn_t + weight * level_out_t
            grad_q_t = grad_q_t + weight * level_back_t
            dotted = jnp.sum(level_out_t * do_t, axis=0, keepdims=True)
            gg_ref[first + b : first + b + 1, ts] = weight * dotted
        attn_ref[ts, :] = jnp.transpose(attn_t).astype(attn_ref.dtype)
        gq_ref[ts, :] = jnp.transpose(grad_q_t).astype(gq_ref.dtype)
        gk_ref[ts, :] = (dk_ref[ts, :] + dot_nn(v_ref[ts, :], key_state_t)).astype(gk_ref.dtype)
        gv_ref[ts, :] = (dv_ref[ts, :] + dot_nt(k_ref[ts, :], key_state_t)).astype(gv_ref.dtype)


def final_part(query_rows, key_rows, value_rows, out_grad, partials, gate_t, level_state, key_state_t):
    heads, block_len, width = query_rows.shape
    nlev = gate_t.shape[1]
    nbits = level_state.shape[0]
    row_spec = pl.BlockSpec((None, block_len, width), lambda h: (h, 0, 0))
    col_spec = pl.BlockSpec((None, width, block_len), lambda h: (h, 0, 0))
    gate_spec = pl.BlockSpec((None, nlev, block_len), lambda h: (h, 0, 0))
    ls_spec = pl.BlockSpec((nbits, None, width, width), lambda h: (0, h, 0, 0))
    ks_spec = pl.BlockSpec((None, width, width), lambda h: (h, 0, 0))
    bf = jnp.bfloat16
    level_state_t = jnp.swapaxes(level_state, 2, 3)
    return pl.pallas_call(
        final_kernel,
        grid=(heads,),
        in_specs=[row_spec] * 4 + [col_spec] * 2 + [row_spec] * 2
        + [gate_spec, gate_spec, ls_spec, ls_spec, ks_spec],
        out_specs=[row_spec] * 4 + [gate_spec],
        out_shape=[jax.ShapeDtypeStruct((heads, block_len, width), bf)] * 4
        + [jax.ShapeDtypeStruct((heads, nlev, block_len), jnp.float32)],
        compiler_params=pltpu.CompilerParams(dimension_semantics=("arbitrary",)),
        cost_estimate=pl.CostEstimate(
            flops=heads * block_len * width * width * 2 * (2 * nbits + 2),
            transcendentals=0,
            bytes_accessed=heads * block_len * (8 * width * 2 + 4 * width * 4 + 4 * nlev * 4),
        ),
    )(query_rows, key_rows, value_rows, out_grad, *partials[:4], partials[4], gate_t,
      level_state, level_state_t, key_state_t)


def same_doc(block_levels, earlier, later):
    return block_levels[later, earlier] >= 0


def step_masks(block_levels, me, k):
    bit = ((me >> k) & 1) == 1
    lo = (me >> (k + 1)) << (k + 1)
    end_low = lo + (1 << k) - 1
    end_high = lo + (2 << k) - 1
    joined = same_doc(block_levels, end_low, end_high)
    mine = same_doc(block_levels, end_low, me)
    return bit, joined, mine


def pairs_of(k, ctx_len, sender_bit=None):
    return [
        (j, j ^ (1 << k))
        for j in range(ctx_len)
        if sender_bit is None or ((j >> k) & 1) == sender_bit
    ]


def per_device(query_rows, key_rows, value_rows, out_grad, level_gate, block_levels, ctx_len):
    level_total = level_gate.shape[0]
    block_len = query_rows.shape[1]
    log_block = block_len.bit_length() - 1
    nbits = level_total - log_block - 1
    me = lax.axis_index("ctx")
    weights = jnp.exp(level_gate)

    gate_t = weights.transpose(1, 0, 2)
    own_state, grad_state = state_part(query_rows, key_rows, value_rows, out_grad, gate_t, nbits)
    grad_wide = grad_state.astype(jnp.float32)
    heads = query_rows.shape[0]
    steps = jnp.arange(nbits, dtype=jnp.int32)
    bit = ((me >> steps) & 1) == 1
    lo = (me >> (steps + 1)) << (steps + 1)
    end_low = lo + (1 << steps) - 1
    end_high = lo + (2 << steps) - 1
    joined = block_levels[end_high, end_low] >= 0
    mine = block_levels[me, end_low] >= 0
    one = jnp.float32(1.0)
    zero = jnp.float32(0.0)
    take = jnp.where(bit & mine, one, zero)
    keep_own = jnp.where(bit, one, jnp.where(joined, one, zero))
    keep_got = jnp.where(bit, jnp.where(joined, one, zero), one)
    take, keep_own, keep_got = lax.optimization_barrier((take, keep_own, keep_got))
    fwd_x = own_state.astype(jnp.float32)
    bwd_acc = None
    levels = []
    partials = None
    for r in range(nbits):
        kf = r
        kb = nbits - 1 - r
        if kf == 0 or kf == nbits - 1:
            fwd_got = lax.ppermute(
                fwd_x.astype(jnp.bfloat16), "ctx", pairs_of(kf, ctx_len)
            ).astype(jnp.float32)
        else:
            fwd_got = lax.ppermute(fwd_x, "ctx", pairs_of(kf, ctx_len))
        term = take[kb] * grad_wide[kb]
        if bwd_acc is None:
            send, own = term, None
            bwd_got = lax.ppermute(send.astype(jnp.bfloat16), "ctx", pairs_of(kb, ctx_len)).astype(jnp.float32)
        else:
            send = term + keep_got[kb] * bwd_acc
            own = keep_own[kb] * bwd_acc
            bwd_got = lax.ppermute(send, "ctx", pairs_of(kb, ctx_len))
        if r < heads:
            partials = local_part(query_rows, key_rows, value_rows, out_grad, gate_t, r, partials)
            fwd_got, bwd_got, partials = lax.optimization_barrier((fwd_got, bwd_got, partials))
        bwd_acc = bwd_got if own is None else own + bwd_got
        levels.append((take[kf] * fwd_got).astype(jnp.bfloat16))
        if kf < nbits - 1:
            fwd_x = keep_own[kf] * fwd_x + keep_got[kf] * fwd_got
    for h in range(nbits, heads):
        partials = local_part(query_rows, key_rows, value_rows, out_grad, gate_t, h, partials)
    level_state = jnp.stack(levels)
    key_state_t = bwd_acc.astype(jnp.bfloat16)
    attn, grad_q, grad_k, grad_v, grad_gate = final_part(
        query_rows, key_rows, value_rows, out_grad, partials, gate_t, level_state, key_state_t
    )
    return (attn, grad_q, grad_k, grad_v, grad_gate.transpose(1, 0, 2))


def solution(mesh):
    ctx_len = mesh.shape["ctx"]
    in_specs = (
        P("head", "ctx", None),
        P("head", "ctx", None),
        P("head", "ctx", None),
        P("head", "ctx", None),
        P(None, "head", "ctx"),
        P(),
    )
    out_specs = (
        P("head", "ctx", None),
        P("head", "ctx", None),
        P("head", "ctx", None),
        P("head", "ctx", None),
        P(None, "head", "ctx"),
    )

    def body(*args):
        return per_device(*args, ctx_len=ctx_len)

    return jax.shard_map(
        body, mesh=mesh, in_specs=in_specs, out_specs=out_specs, check_vma=False
    )
```

```python
import jax
import jax.numpy as jnp
from jax import lax
from jax.experimental import pallas as pl
from jax.experimental.pallas import tpu as pltpu
from jax.sharding import PartitionSpec as P


TILE = 256
SUB = 128


def bit_length_small(numbers, count):
    total = jnp.zeros(numbers.shape, jnp.int32)
    for shift_by in range(count):
        total = total + (numbers >= (1 << shift_by)).astype(jnp.int32)
    return total


def dot_nt(a, b):
    return lax.dot_general(a, b, (((1,), (1,)), ((), ())), preferred_element_type=jnp.float32)


def dot_tn(a, b):
    return lax.dot_general(a, b, (((0,), (0,)), ((), ())), preferred_element_type=jnp.float32)


def dot_nn(a, b):
    return lax.dot_general(a, b, (((1,), (0,)), ((), ())), preferred_element_type=jnp.float32)


def local_kernel(q_ref, k_ref, v_ref, do_ref, g_ref, *refs):
    o_ref, dq_ref, dk_ref, dv_ref, gg_ref = refs[-5:]
    block_len = q_ref.shape[0]
    tiles = block_len // TILE
    log_tile = TILE.bit_length() - 1
    log_sub = SUB.bit_length() - 1
    keys = lax.broadcasted_iota(jnp.int32, (SUB, SUB), 0)
    queries = lax.broadcasted_iota(jnp.int32, (SUB, SUB), 1)
    diag_level = jnp.where(
        keys <= queries, bit_length_small(jnp.bitwise_xor(keys, queries), log_sub), -1
    )
    for ref in (o_ref, dq_ref, dk_ref, dv_ref, gg_ref):
        ref[...] = jnp.zeros(ref.shape, jnp.float32)

    def pair(t0, s0, size, level):
        ts = pl.ds(t0, size)
        ss = pl.ds(s0, size)
        qi = q_ref[ts, :]
        doi = do_ref[ts, :]
        kj = k_ref[ss, :]
        vj = v_ref[ss, :]
        gi = g_ref[:, ts]
        scores = dot_nt(kj, qi)
        back = dot_nt(vj, doi)
        prod = scores * back
        if level is not None:
            weight = gi[level : level + 1, :]
            gg_ref[level : level + 1, ts] += jnp.sum(prod, axis=0, keepdims=True)
        else:
            weight = jnp.zeros((size, size), jnp.float32)
            for lev in range(log_sub + 1):
                hit = diag_level == lev
                weight = jnp.where(hit, gi[lev : lev + 1, :], weight)
                gg_ref[lev : lev + 1, ts] += jnp.sum(
                    jnp.where(hit, prod, 0.0), axis=0, keepdims=True
                )
        probs = (scores * weight).astype(jnp.bfloat16)
        dprobs = (back * weight).astype(jnp.bfloat16)
        o_ref[:, ts] += dot_tn(vj, probs)
        dq_ref[:, ts] += dot_tn(kj, dprobs)
        dk_ref[ss, :] += dot_nn(dprobs, qi)
        dv_ref[ss, :] += dot_nn(probs, doi)

    for i in range(tiles):
        for j in range(i):
            pair(i * TILE, j * TILE, TILE, log_tile + (i ^ j).bit_length())
        for a in range(TILE // SUB):
            for b in range(a):
                pair(i * TILE + a * SUB, i * TILE + b * SUB, SUB, log_sub + (a ^ b).bit_length())
            pair(i * TILE + a * SUB, i * TILE + a * SUB, SUB, None)
    gg_ref[...] = gg_ref[...] * g_ref[...]


def local_part(query_rows, key_rows, value_rows, out_grad, gate_t, h, outs):
    heads, block_len, width = query_rows.shape
    nlev = gate_t.shape[1]
    f32 = jnp.float32
    pairs = (block_len // TILE) * (block_len // TILE + 1) // 2
    flops = pairs * 6 * 2 * TILE * TILE * width
    shapes = [jax.ShapeDtypeStruct((heads, width, block_len), f32)] * 2 + [
        jax.ShapeDtypeStruct((heads, block_len, width), f32)
    ] * 2 + [jax.ShapeDtypeStruct((heads, nlev, block_len), f32)]
    row_spec = pl.BlockSpec((None, block_len, width), lambda i: (h, 0, 0))
    col_spec = pl.BlockSpec((None, width, block_len), lambda i: (h, 0, 0))
    gate_spec = pl.BlockSpec((None, nlev, block_len), lambda i: (h, 0, 0))
    args = (query_rows, key_rows, value_rows, out_grad, gate_t)
    in_specs = [row_spec] * 4 + [gate_spec]
    aliases = {}
    if outs is not None:
        args = args + tuple(outs)
        in_specs = in_specs + [pl.BlockSpec(memory_space=pl.ANY)] * 5
        aliases = {5 + n: n for n in range(5)}
    return pl.pallas_call(
        local_kernel,
        grid=(1,),
        in_specs=in_specs,
        out_specs=[col_spec] * 2 + [row_spec] * 2 + [gate_spec],
        out_shape=shapes,
        input_output_aliases=aliases,
        compiler_params=pltpu.CompilerParams(dimension_semantics=("arbitrary",)),
        cost_estimate=pl.CostEstimate(
            flops=flops,
            transcendentals=0,
            bytes_accessed=block_len * (4 * width * 2 + 4 * width * 4 + 2 * nlev * 4),
        ),
    )(*args)


def state_kernel(q_ref, k_ref, v_ref, do_ref, g_ref, st_ref, gs_ref):
    nlev = g_ref.shape[0]
    nbits = gs_ref.shape[0]
    first = nlev - nbits
    st_ref[...] = dot_tn(k_ref[...], v_ref[...]).astype(jnp.bfloat16).astype(st_ref.dtype)
    do_t = jnp.transpose(do_ref[...].astype(jnp.float32))
    q = q_ref[...]
    for b in range(nbits):
        scaled_t = (g_ref[first + b : first + b + 1, :] * do_t).astype(jnp.bfloat16)
        gs_ref[b] = dot_nn(scaled_t, q).astype(jnp.bfloat16).astype(gs_ref.dtype)


def state_part(query_rows, key_rows, value_rows, out_grad, gate_t, nbits):
    heads, block_len, width = query_rows.shape
    nlev = gate_t.shape[1]
    row_spec = pl.BlockSpec((None, block_len, width), lambda h: (h, 0, 0))
    gate_spec = pl.BlockSpec((None, nlev, block_len), lambda h: (h, 0, 0))
    bf = jnp.bfloat16
    return pl.pallas_call(
        state_kernel,
        grid=(heads,),
        in_specs=[row_spec] * 4 + [gate_spec],
        out_specs=[
            pl.BlockSpec((None, width, width), lambda h: (h, 0, 0)),
            pl.BlockSpec((nbits, None, width, width), lambda h: (0, h, 0, 0)),
        ],
        out_shape=[
            jax.ShapeDtypeStruct((heads, width, width), jnp.float32),
            jax.ShapeDtypeStruct((nbits, heads, width, width), jnp.float32),
        ],
        compiler_params=pltpu.CompilerParams(dimension_semantics=("arbitrary",)),
        cost_estimate=pl.CostEstimate(
            flops=heads * block_len * width * width * 2 * (nbits + 1),
            transcendentals=0,
            bytes_accessed=heads * block_len * (4 * width * 2 + nlev * 4),
        ),
    )(query_rows, key_rows, value_rows, out_grad, gate_t)


def final_kernel(q_ref, k_ref, v_ref, do_ref, o_ref, dq_ref, dk_ref, dv_ref, ggl_ref, g_ref,
                 ls_ref, kst_ref, attn_ref, gq_ref, gk_ref, gv_ref, gg_ref):
    block_len = q_ref.shape[0]
    nlev = g_ref.shape[0]
    nbits = ls_ref.shape[0]
    first = nlev - nbits
    key_state_t = kst_ref[...]
    h = pl.program_id(0)
    state_t = [jnp.transpose(ls_ref[b].astype(jnp.float32)).astype(jnp.bfloat16) for b in range(nbits)]
    gg = [ggl_ref[lev : lev + 1, :] for lev in range(nlev)]
    cross_rows = [[] for _ in range(nbits)]
    for i in range(block_len // TILE):
        ts = pl.ds(i * TILE, TILE)
        qi = q_ref[ts, :]
        doi = do_ref[ts, :]
        do_t = jnp.transpose(doi.astype(jnp.float32))
        attn_t = o_ref[:, ts]
        grad_q_t = dq_ref[:, ts]
        for b in range(nbits):
            weight = g_ref[first + b : first + b + 1, ts]
            level_out_t = dot_nt(state_t[b], qi)
            level_back_t = dot_nt(ls_ref[b], doi)
            attn_t = attn_t + weight * level_out_t
            grad_q_t = grad_q_t + weight * level_back_t
            dotted = jnp.sum(level_out_t * do_t, axis=0, keepdims=True)
            cross_rows[b].append(weight * dotted)
        attn_ref[ts, :] = jnp.transpose(attn_t).astype(attn_ref.dtype)
        gq_ref[ts, :] = jnp.transpose(grad_q_t).astype(gq_ref.dtype)
        gk_ref[ts, :] = (dk_ref[ts, :] + dot_nn(v_ref[ts, :], key_state_t)).astype(gk_ref.dtype)
        gv_ref[ts, :] = (dv_ref[ts, :] + dot_nt(k_ref[ts, :], key_state_t)).astype(gv_ref.dtype)
    for b in range(nbits):
        gg[first + b] = jnp.concatenate(cross_rows[b], axis=1)
    for lev in range(nlev):
        gg_ref[lev, pl.ds(h, 1), :] = gg[lev]


def final_part(query_rows, key_rows, value_rows, out_grad, partials, gate_t, level_state, key_state_t):
    heads, block_len, width = query_rows.shape
    nlev = gate_t.shape[1]
    nbits = level_state.shape[0]
    row_spec = pl.BlockSpec((None, block_len, width), lambda h: (h, 0, 0))
    col_spec = pl.BlockSpec((None, width, block_len), lambda h: (h, 0, 0))
    gate_spec = pl.BlockSpec((None, nlev, block_len), lambda h: (h, 0, 0))
    ls_spec = pl.BlockSpec((nbits, None, width, width), lambda h: (0, h, 0, 0))
    ks_spec = pl.BlockSpec((None, width, width), lambda h: (h, 0, 0))
    bf = jnp.bfloat16
    return pl.pallas_call(
        final_kernel,
        grid=(heads,),
        in_specs=[row_spec] * 4 + [col_spec] * 2 + [row_spec] * 2
        + [gate_spec, gate_spec, ls_spec, ks_spec],
        out_specs=[row_spec] * 4 + [pl.BlockSpec((nlev, heads, block_len), lambda h: (0, 0, 0))],
        out_shape=[jax.ShapeDtypeStruct((heads, block_len, width), bf)] * 4
        + [jax.ShapeDtypeStruct((nlev, heads, block_len), jnp.float32)],
        compiler_params=pltpu.CompilerParams(dimension_semantics=("arbitrary",)),
        cost_estimate=pl.CostEstimate(
            flops=heads * block_len * width * width * 2 * (2 * nbits + 2),
            transcendentals=0,
            bytes_accessed=heads * block_len * (8 * width * 2 + 4 * width * 4 + 4 * nlev * 4),
        ),
    )(query_rows, key_rows, value_rows, out_grad, *partials[:4], partials[4], gate_t,
      level_state, key_state_t)


def same_doc(block_levels, earlier, later):
    return block_levels[later, earlier] >= 0


def step_masks(block_levels, me, k):
    bit = ((me >> k) & 1) == 1
    lo = (me >> (k + 1)) << (k + 1)
    end_low = lo + (1 << k) - 1
    end_high = lo + (2 << k) - 1
    joined = same_doc(block_levels, end_low, end_high)
    mine = same_doc(block_levels, end_low, me)
    return bit, joined, mine


def pairs_of(k, ctx_len, sender_bit=None):
    return [
        (j, j ^ (1 << k))
        for j in range(ctx_len)
        if sender_bit is None or ((j >> k) & 1) == sender_bit
    ]


def per_device(query_rows, key_rows, value_rows, out_grad, level_gate, block_levels, ctx_len):
    level_total = level_gate.shape[0]
    block_len = query_rows.shape[1]
    log_block = block_len.bit_length() - 1
    nbits = level_total - log_block - 1
    me = lax.axis_index("ctx")
    weights = jnp.exp(level_gate)

    gate_t = weights.transpose(1, 0, 2)
    own_state, grad_state = state_part(query_rows, key_rows, value_rows, out_grad, gate_t, nbits)
    grad_wide = grad_state
    heads = query_rows.shape[0]
    fwd_x = own_state
    bwd_acc = None
    levels = []
    partials = None
    for r in range(nbits):
        kf = r
        kb = nbits - 1 - r
        if kf == 0 or kf == nbits - 1:
            fwd_got = lax.ppermute(
                fwd_x.astype(jnp.bfloat16), "ctx",
                pairs_of(kf, ctx_len),
            ).astype(jnp.float32)
        else:
            fwd_got = lax.ppermute(fwd_x, "ctx", pairs_of(kf, ctx_len))
        bit, joined, mine = step_masks(block_levels, me, kb)
        term = jnp.where(bit & mine, grad_wide[kb], 0.0)
        if bwd_acc is None:
            send, own = term, None
            bwd_pairs = pairs_of(kb, ctx_len)
        else:
            kept = jnp.where(joined, bwd_acc, 0.0)
            send = jnp.where(bit, term + kept, bwd_acc)
            own = jnp.where(bit, bwd_acc, kept)
            bwd_pairs = pairs_of(kb, ctx_len)
        if own is None:
            bwd_got = lax.ppermute(send.astype(jnp.bfloat16), "ctx", bwd_pairs).astype(jnp.float32)
        else:
            bwd_got = lax.ppermute(send, "ctx", bwd_pairs)
        if r < heads:
            partials = local_part(query_rows, key_rows, value_rows, out_grad, gate_t, r, partials)
            fwd_got, bwd_got, partials = lax.optimization_barrier((fwd_got, bwd_got, partials))
        bwd_acc = bwd_got if own is None else own + bwd_got
        bit, joined, mine = step_masks(block_levels, me, kf)
        levels.append(jnp.where(bit & mine, fwd_got, 0.0).astype(jnp.bfloat16))
        if kf < nbits - 1:
            fwd_x = jnp.where(
                bit, fwd_x + jnp.where(joined, fwd_got, 0.0), fwd_got + jnp.where(joined, fwd_x, 0.0)
            )
    for h in range(nbits, heads):
        partials = local_part(query_rows, key_rows, value_rows, out_grad, gate_t, h, partials)
    level_state = jnp.stack(levels)
    key_state_t = bwd_acc.astype(jnp.bfloat16)
    attn, grad_q, grad_k, grad_v, grad_gate = final_part(
        query_rows, key_rows, value_rows, out_grad, partials, gate_t, level_state, key_state_t
    )
    return (attn, grad_q, grad_k, grad_v, grad_gate)


def solution(mesh):
    ctx_len = mesh.shape["ctx"]
    in_specs = (
        P("head", "ctx", None),
        P("head", "ctx", None),
        P("head", "ctx", None),
        P("head", "ctx", None),
        P(None, "head", "ctx"),
        P(),
    )
    out_specs = (
        P("head", "ctx", None),
        P("head", "ctx", None),
        P("head", "ctx", None),
        P("head", "ctx", None),
        P(None, "head", "ctx"),
    )

    def body(*args):
        return per_device(*args, ctx_len=ctx_len)

    return jax.shard_map(
        body, mesh=mesh, in_specs=in_specs, out_specs=out_specs, check_vma=False
    )
```

```python
import jax
import jax.numpy as jnp
from jax import lax
from jax.experimental import pallas as pl
from jax.experimental.pallas import tpu as pltpu
from jax.sharding import PartitionSpec as P


TILE = 256
SUB = 128


def bit_length_small(numbers, count):
    total = jnp.zeros(numbers.shape, jnp.int32)
    for shift_by in range(count):
        total = total + (numbers >= (1 << shift_by)).astype(jnp.int32)
    return total


def dot_nt(a, b):
    return lax.dot_general(a, b, (((1,), (1,)), ((), ())), preferred_element_type=jnp.float32)


def dot_tn(a, b):
    return lax.dot_general(a, b, (((0,), (0,)), ((), ())), preferred_element_type=jnp.float32)


def dot_nn(a, b):
    return lax.dot_general(a, b, (((1,), (0,)), ((), ())), preferred_element_type=jnp.float32)


def local_kernel(q_ref, k_ref, v_ref, do_ref, g_ref, *refs):
    o_ref, dq_ref, dk_ref, dv_ref, gg_ref = refs[-5:]
    block_len = q_ref.shape[0]
    tiles = block_len // TILE
    log_tile = TILE.bit_length() - 1
    log_sub = SUB.bit_length() - 1
    keys = lax.broadcasted_iota(jnp.int32, (SUB, SUB), 0)
    queries = lax.broadcasted_iota(jnp.int32, (SUB, SUB), 1)
    diag_level = jnp.where(
        keys <= queries, bit_length_small(jnp.bitwise_xor(keys, queries), log_sub), -1
    )
    for ref in (o_ref, dq_ref, dk_ref, dv_ref, gg_ref):
        ref[...] = jnp.zeros(ref.shape, jnp.float32)

    def pair(t0, s0, size, level):
        ts = pl.ds(t0, size)
        ss = pl.ds(s0, size)
        qi = q_ref[ts, :]
        doi = do_ref[ts, :]
        kj = k_ref[ss, :]
        vj = v_ref[ss, :]
        gi = g_ref[:, ts]
        scores = dot_nt(kj, qi)
        back = dot_nt(vj, doi)
        prod = scores * back
        if level is not None:
            weight = gi[level : level + 1, :]
            gg_ref[level : level + 1, ts] += jnp.sum(prod, axis=0, keepdims=True)
        else:
            weight = jnp.zeros((size, size), jnp.float32)
            for lev in range(log_sub + 1):
                hit = diag_level == lev
                weight = jnp.where(hit, gi[lev : lev + 1, :], weight)
                gg_ref[lev : lev + 1, ts] += jnp.sum(
                    jnp.where(hit, prod, 0.0), axis=0, keepdims=True
                )
        probs = (scores * weight).astype(jnp.bfloat16)
        dprobs = (back * weight).astype(jnp.bfloat16)
        o_ref[:, ts] += dot_tn(vj, probs)
        dq_ref[:, ts] += dot_tn(kj, dprobs)
        dk_ref[ss, :] += dot_nn(dprobs, qi)
        dv_ref[ss, :] += dot_nn(probs, doi)

    for i in range(tiles):
        for j in range(i):
            pair(i * TILE, j * TILE, TILE, log_tile + (i ^ j).bit_length())
        for a in range(TILE // SUB):
            for b in range(a):
                pair(i * TILE + a * SUB, i * TILE + b * SUB, SUB, log_sub + (a ^ b).bit_length())
            pair(i * TILE + a * SUB, i * TILE + a * SUB, SUB, None)
    gg_ref[...] = gg_ref[...] * g_ref[...]


def local_part(query_rows, key_rows, value_rows, out_grad, gate_t, h, outs):
    heads, block_len, width = query_rows.shape
    nlev = gate_t.shape[1]
    f32 = jnp.float32
    pairs = (block_len // TILE) * (block_len // TILE + 1) // 2
    flops = pairs * 6 * 2 * TILE * TILE * width
    shapes = [jax.ShapeDtypeStruct((heads, width, block_len), f32)] * 2 + [
        jax.ShapeDtypeStruct((heads, block_len, width), f32)
    ] * 2 + [jax.ShapeDtypeStruct((heads, nlev, block_len), f32)]
    row_spec = pl.BlockSpec((None, block_len, width), lambda i: (h, 0, 0))
    col_spec = pl.BlockSpec((None, width, block_len), lambda i: (h, 0, 0))
    gate_spec = pl.BlockSpec((None, nlev, block_len), lambda i: (h, 0, 0))
    args = (query_rows, key_rows, value_rows, out_grad, gate_t)
    in_specs = [row_spec] * 4 + [gate_spec]
    aliases = {}
    if outs is not None:
        args = args + tuple(outs)
        in_specs = in_specs + [pl.BlockSpec(memory_space=pl.ANY)] * 5
        aliases = {5 + n: n for n in range(5)}
    return pl.pallas_call(
        local_kernel,
        grid=(1,),
        in_specs=in_specs,
        out_specs=[col_spec] * 2 + [row_spec] * 2 + [gate_spec],
        out_shape=shapes,
        input_output_aliases=aliases,
        compiler_params=pltpu.CompilerParams(dimension_semantics=("arbitrary",)),
        cost_estimate=pl.CostEstimate(
            flops=flops,
            transcendentals=0,
            bytes_accessed=block_len * (4 * width * 2 + 4 * width * 4 + 2 * nlev * 4),
        ),
    )(*args)


def state_kernel(q_ref, k_ref, v_ref, do_ref, g_ref, st_ref, gs_ref):
    nlev = g_ref.shape[0]
    nbits = gs_ref.shape[0]
    first = nlev - nbits
    st_ref[...] = dot_tn(k_ref[...], v_ref[...]).astype(jnp.bfloat16).astype(st_ref.dtype)
    do_t = jnp.transpose(do_ref[...].astype(jnp.float32))
    q = q_ref[...]
    for b in range(nbits):
        scaled_t = (g_ref[first + b : first + b + 1, :] * do_t).astype(jnp.bfloat16)
        gs_ref[b] = dot_nn(scaled_t, q).astype(jnp.bfloat16).astype(gs_ref.dtype)


def state_part(query_rows, key_rows, value_rows, out_grad, gate_t, nbits):
    heads, block_len, width = query_rows.shape
    nlev = gate_t.shape[1]
    row_spec = pl.BlockSpec((None, block_len, width), lambda h: (h, 0, 0))
    gate_spec = pl.BlockSpec((None, nlev, block_len), lambda h: (h, 0, 0))
    bf = jnp.bfloat16
    return pl.pallas_call(
        state_kernel,
        grid=(heads,),
        in_specs=[row_spec] * 4 + [gate_spec],
        out_specs=[
            pl.BlockSpec((None, width, width), lambda h: (h, 0, 0)),
            pl.BlockSpec((nbits, None, width, width), lambda h: (0, h, 0, 0)),
        ],
        out_shape=[
            jax.ShapeDtypeStruct((heads, width, width), jnp.float32),
            jax.ShapeDtypeStruct((nbits, heads, width, width), jnp.float32),
        ],
        compiler_params=pltpu.CompilerParams(dimension_semantics=("arbitrary",)),
        cost_estimate=pl.CostEstimate(
            flops=heads * block_len * width * width * 2 * (nbits + 1),
            transcendentals=0,
            bytes_accessed=heads * block_len * (4 * width * 2 + nlev * 4),
        ),
    )(query_rows, key_rows, value_rows, out_grad, gate_t)


def final_kernel(q_ref, k_ref, v_ref, do_ref, o_ref, dq_ref, dk_ref, dv_ref, ggl_ref, g_ref,
                 ls_ref, kst_ref, attn_ref, gq_ref, gk_ref, gv_ref, gg_ref):
    block_len = q_ref.shape[0]
    nlev = g_ref.shape[0]
    nbits = ls_ref.shape[0]
    first = nlev - nbits
    key_state_t = kst_ref[...]
    h = pl.program_id(0)
    state_t = [jnp.transpose(ls_ref[b].astype(jnp.float32)).astype(jnp.bfloat16) for b in range(nbits)]
    gg = [ggl_ref[lev : lev + 1, :] for lev in range(nlev)]
    cross_rows = [[] for _ in range(nbits)]
    for i in range(block_len // TILE):
        ts = pl.ds(i * TILE, TILE)
        qi = q_ref[ts, :]
        doi = do_ref[ts, :]
        do_t = jnp.transpose(doi.astype(jnp.float32))
        attn_t = o_ref[:, ts]
        grad_q_t = dq_ref[:, ts]
        for b in range(nbits):
            weight = g_ref[first + b : first + b + 1, ts]
            level_out_t = dot_nt(state_t[b], qi)
            level_back_t = dot_nt(ls_ref[b], doi)
            attn_t = attn_t + weight * level_out_t
            grad_q_t = grad_q_t + weight * level_back_t
            dotted = jnp.sum(level_out_t * do_t, axis=0, keepdims=True)
            cross_rows[b].append(weight * dotted)
        attn_ref[ts, :] = jnp.transpose(attn_t).astype(attn_ref.dtype)
        gq_ref[ts, :] = jnp.transpose(grad_q_t).astype(gq_ref.dtype)
        gk_ref[ts, :] = (dk_ref[ts, :] + dot_nn(v_ref[ts, :], key_state_t)).astype(gk_ref.dtype)
        gv_ref[ts, :] = (dv_ref[ts, :] + dot_nt(k_ref[ts, :], key_state_t)).astype(gv_ref.dtype)
    for b in range(nbits):
        gg[first + b] = jnp.concatenate(cross_rows[b], axis=1)
    for lev in range(nlev):
        gg_ref[lev, pl.ds(h, 1), :] = gg[lev]


def final_part(query_rows, key_rows, value_rows, out_grad, partials, gate_t, level_state, key_state_t):
    heads, block_len, width = query_rows.shape
    nlev = gate_t.shape[1]
    nbits = level_state.shape[0]
    row_spec = pl.BlockSpec((None, block_len, width), lambda h: (h, 0, 0))
    col_spec = pl.BlockSpec((None, width, block_len), lambda h: (h, 0, 0))
    gate_spec = pl.BlockSpec((None, nlev, block_len), lambda h: (h, 0, 0))
    ls_spec = pl.BlockSpec((nbits, None, width, width), lambda h: (0, h, 0, 0))
    ks_spec = pl.BlockSpec((None, width, width), lambda h: (h, 0, 0))
    bf = jnp.bfloat16
    return pl.pallas_call(
        final_kernel,
        grid=(heads,),
        in_specs=[row_spec] * 4 + [col_spec] * 2 + [row_spec] * 2
        + [gate_spec, gate_spec, ls_spec, ks_spec],
        out_specs=[row_spec] * 4 + [pl.BlockSpec((nlev, heads, block_len), lambda h: (0, 0, 0))],
        out_shape=[jax.ShapeDtypeStruct((heads, block_len, width), bf)] * 4
        + [jax.ShapeDtypeStruct((nlev, heads, block_len), jnp.float32)],
        compiler_params=pltpu.CompilerParams(dimension_semantics=("arbitrary",)),
        cost_estimate=pl.CostEstimate(
            flops=heads * block_len * width * width * 2 * (2 * nbits + 2),
            transcendentals=0,
            bytes_accessed=heads * block_len * (8 * width * 2 + 4 * width * 4 + 4 * nlev * 4),
        ),
    )(query_rows, key_rows, value_rows, out_grad, *partials[:4], partials[4], gate_t,
      level_state, key_state_t)


def same_doc(block_levels, earlier, later):
    picked = lax.dynamic_slice(block_levels, (later, earlier), (1, 1))
    return picked.reshape(1, 1, 1) >= 0


def step_masks(block_levels, me, k):
    bit = ((me >> k) & 1) == 1
    lo = (me >> (k + 1)) << (k + 1)
    end_low = lo + (1 << k) - 1
    end_high = lo + (2 << k) - 1
    joined = same_doc(block_levels, end_low, end_high)
    mine = same_doc(block_levels, end_low, me)
    return bit, joined, mine


def pairs_of(k, ctx_len, sender_bit=None):
    return [
        (j, j ^ (1 << k))
        for j in range(ctx_len)
        if sender_bit is None or ((j >> k) & 1) == sender_bit
    ]


def per_device(query_rows, key_rows, value_rows, out_grad, level_gate, block_levels, ctx_len):
    level_total = level_gate.shape[0]
    block_len = query_rows.shape[1]
    log_block = block_len.bit_length() - 1
    nbits = level_total - log_block - 1
    me = lax.axis_index("ctx")
    weights = jnp.exp(level_gate)

    gate_t = weights.transpose(1, 0, 2)
    own_state, grad_state = state_part(query_rows, key_rows, value_rows, out_grad, gate_t, nbits)
    grad_wide = grad_state
    heads = query_rows.shape[0]
    fwd_x = own_state
    bwd_acc = None
    levels = []
    partials = None
    for r in range(nbits):
        kf = r
        kb = nbits - 1 - r
        if kf == 0 or kf == nbits - 1:
            fwd_got = lax.ppermute(
                fwd_x.astype(jnp.bfloat16), "ctx",
                pairs_of(kf, ctx_len),
            ).astype(jnp.float32)
        else:
            fwd_got = lax.ppermute(fwd_x, "ctx", pairs_of(kf, ctx_len))
        bit, joined, mine = step_masks(block_levels, me, kb)
        term = jnp.where(bit & mine, grad_wide[kb], 0.0)
        if bwd_acc is None:
            send, own = term, None
            bwd_pairs = pairs_of(kb, ctx_len)
        else:
            kept = jnp.where(joined, bwd_acc, 0.0)
            send = jnp.where(bit, term + kept, bwd_acc)
            own = jnp.where(bit, bwd_acc, kept)
            bwd_pairs = pairs_of(kb, ctx_len)
        if own is None:
            bwd_got = lax.ppermute(send.astype(jnp.bfloat16), "ctx", bwd_pairs).astype(jnp.float32)
        else:
            bwd_got = lax.ppermute(send, "ctx", bwd_pairs)
        if r < heads:
            partials = local_part(query_rows, key_rows, value_rows, out_grad, gate_t, r, partials)
            fwd_got, bwd_got, partials = lax.optimization_barrier((fwd_got, bwd_got, partials))
        bwd_acc = bwd_got if own is None else own + bwd_got
        bit, joined, mine = step_masks(block_levels, me, kf)
        levels.append(jnp.where(bit & mine, fwd_got, 0.0).astype(jnp.bfloat16))
        if kf < nbits - 1:
            fwd_x = jnp.where(
                bit, fwd_x + jnp.where(joined, fwd_got, 0.0), fwd_got + jnp.where(joined, fwd_x, 0.0)
            )
    for h in range(nbits, heads):
        partials = local_part(query_rows, key_rows, value_rows, out_grad, gate_t, h, partials)
    level_state = jnp.stack(levels)
    key_state_t = bwd_acc.astype(jnp.bfloat16)
    attn, grad_q, grad_k, grad_v, grad_gate = final_part(
        query_rows, key_rows, value_rows, out_grad, partials, gate_t, level_state, key_state_t
    )
    return (attn, grad_q, grad_k, grad_v, grad_gate)


def solution(mesh):
    ctx_len = mesh.shape["ctx"]
    in_specs = (
        P("head", "ctx", None),
        P("head", "ctx", None),
        P("head", "ctx", None),
        P("head", "ctx", None),
        P(None, "head", "ctx"),
        P(),
    )
    out_specs = (
        P("head", "ctx", None),
        P("head", "ctx", None),
        P("head", "ctx", None),
        P("head", "ctx", None),
        P(None, "head", "ctx"),
    )

    def body(*args):
        return per_device(*args, ctx_len=ctx_len)

    return jax.shard_map(
        body, mesh=mesh, in_specs=in_specs, out_specs=out_specs, check_vma=False
    )
```

```python
import jax
import jax.numpy as jnp
from jax import lax
from jax.experimental import pallas as pl
from jax.experimental.pallas import tpu as pltpu
from jax.sharding import PartitionSpec as P


TILE = 256
SUB = 128


def bit_length_small(numbers, count):
    total = jnp.zeros(numbers.shape, jnp.int32)
    for shift_by in range(count):
        total = total + (numbers >= (1 << shift_by)).astype(jnp.int32)
    return total


def dot_nt(a, b):
    return lax.dot_general(a, b, (((1,), (1,)), ((), ())), preferred_element_type=jnp.float32)


def dot_tn(a, b):
    return lax.dot_general(a, b, (((0,), (0,)), ((), ())), preferred_element_type=jnp.float32)


def dot_nn(a, b):
    return lax.dot_general(a, b, (((1,), (0,)), ((), ())), preferred_element_type=jnp.float32)


def local_kernel(q_ref, k_ref, v_ref, do_ref, g_ref, *refs):
    o_ref, dq_ref, dk_ref, dv_ref, gg_ref = refs[-5:]
    block_len = q_ref.shape[0]
    tiles = block_len // TILE
    log_tile = TILE.bit_length() - 1
    log_sub = SUB.bit_length() - 1
    keys = lax.broadcasted_iota(jnp.int32, (SUB, SUB), 0)
    queries = lax.broadcasted_iota(jnp.int32, (SUB, SUB), 1)
    diag_level = jnp.where(
        keys <= queries, bit_length_small(jnp.bitwise_xor(keys, queries), log_sub), -1
    )
    for ref in (o_ref, dq_ref, dk_ref, dv_ref, gg_ref):
        ref[...] = jnp.zeros(ref.shape, jnp.float32)

    def pair(t0, s0, size, level):
        ts = pl.ds(t0, size)
        ss = pl.ds(s0, size)
        qi = q_ref[ts, :]
        doi = do_ref[ts, :]
        kj = k_ref[ss, :]
        vj = v_ref[ss, :]
        gi = g_ref[:, ts]
        scores = dot_nt(kj, qi)
        back = dot_nt(vj, doi)
        prod = scores * back
        if level is not None:
            weight = gi[level : level + 1, :]
            gg_ref[level : level + 1, ts] += jnp.sum(prod, axis=0, keepdims=True)
        else:
            weight = jnp.zeros((size, size), jnp.float32)
            for lev in range(log_sub + 1):
                hit = diag_level == lev
                weight = jnp.where(hit, gi[lev : lev + 1, :], weight)
                gg_ref[lev : lev + 1, ts] += jnp.sum(
                    jnp.where(hit, prod, 0.0), axis=0, keepdims=True
                )
        probs = (scores * weight).astype(jnp.bfloat16)
        dprobs = (back * weight).astype(jnp.bfloat16)
        o_ref[:, ts] += dot_tn(vj, probs)
        dq_ref[:, ts] += dot_tn(kj, dprobs)
        dk_ref[ss, :] += dot_nn(dprobs, qi)
        dv_ref[ss, :] += dot_nn(probs, doi)

    for i in range(tiles):
        for j in range(i):
            pair(i * TILE, j * TILE, TILE, log_tile + (i ^ j).bit_length())
        for a in range(TILE // SUB):
            for b in range(a):
                pair(i * TILE + a * SUB, i * TILE + b * SUB, SUB, log_sub + (a ^ b).bit_length())
            pair(i * TILE + a * SUB, i * TILE + a * SUB, SUB, None)
    gg_ref[...] = gg_ref[...] * g_ref[...]


def local_part(query_rows, key_rows, value_rows, out_grad, gate_t, h, outs):
    heads, block_len, width = query_rows.shape
    nlev = gate_t.shape[1]
    f32 = jnp.float32
    pairs = (block_len // TILE) * (block_len // TILE + 1) // 2
    flops = pairs * 6 * 2 * TILE * TILE * width
    shapes = [jax.ShapeDtypeStruct((heads, width, block_len), f32)] * 2 + [
        jax.ShapeDtypeStruct((heads, block_len, width), f32)
    ] * 2 + [jax.ShapeDtypeStruct((heads, nlev, block_len), f32)]
    row_spec = pl.BlockSpec((None, block_len, width), lambda i: (h, 0, 0))
    col_spec = pl.BlockSpec((None, width, block_len), lambda i: (h, 0, 0))
    gate_spec = pl.BlockSpec((None, nlev, block_len), lambda i: (h, 0, 0))
    args = (query_rows, key_rows, value_rows, out_grad, gate_t)
    in_specs = [row_spec] * 4 + [gate_spec]
    aliases = {}
    if outs is not None:
        args = args + tuple(outs)
        in_specs = in_specs + [pl.BlockSpec(memory_space=pl.ANY)] * 5
        aliases = {5 + n: n for n in range(5)}
    return pl.pallas_call(
        local_kernel,
        grid=(1,),
        in_specs=in_specs,
        out_specs=[col_spec] * 2 + [row_spec] * 2 + [gate_spec],
        out_shape=shapes,
        input_output_aliases=aliases,
        compiler_params=pltpu.CompilerParams(dimension_semantics=("arbitrary",)),
        cost_estimate=pl.CostEstimate(
            flops=flops,
            transcendentals=0,
            bytes_accessed=block_len * (4 * width * 2 + 4 * width * 4 + 2 * nlev * 4),
        ),
    )(*args)


def state_kernel(q_ref, k_ref, v_ref, do_ref, g_ref, st_ref, gs_ref):
    nlev = g_ref.shape[0]
    nbits = gs_ref.shape[0]
    first = nlev - nbits
    st_ref[...] = dot_tn(k_ref[...], v_ref[...]).astype(jnp.bfloat16).astype(st_ref.dtype)
    do_t = jnp.transpose(do_ref[...].astype(jnp.float32))
    q = q_ref[...]
    for b in range(nbits):
        scaled_t = (g_ref[first + b : first + b + 1, :] * do_t).astype(jnp.bfloat16)
        gs_ref[b] = dot_nn(scaled_t, q).astype(jnp.bfloat16).astype(gs_ref.dtype)


def state_part(query_rows, key_rows, value_rows, out_grad, gate_t, nbits):
    heads, block_len, width = query_rows.shape
    nlev = gate_t.shape[1]
    row_spec = pl.BlockSpec((None, block_len, width), lambda h: (h, 0, 0))
    gate_spec = pl.BlockSpec((None, nlev, block_len), lambda h: (h, 0, 0))
    bf = jnp.bfloat16
    return pl.pallas_call(
        state_kernel,
        grid=(heads,),
        in_specs=[row_spec] * 4 + [gate_spec],
        out_specs=[
            pl.BlockSpec((None, width, width), lambda h: (h, 0, 0)),
            pl.BlockSpec((nbits, None, width, width), lambda h: (0, h, 0, 0)),
        ],
        out_shape=[
            jax.ShapeDtypeStruct((heads, width, width), jnp.float32),
            jax.ShapeDtypeStruct((nbits, heads, width, width), jnp.float32),
        ],
        compiler_params=pltpu.CompilerParams(dimension_semantics=("arbitrary",)),
        cost_estimate=pl.CostEstimate(
            flops=heads * block_len * width * width * 2 * (nbits + 1),
            transcendentals=0,
            bytes_accessed=heads * block_len * (4 * width * 2 + nlev * 4),
        ),
    )(query_rows, key_rows, value_rows, out_grad, gate_t)


def final_kernel(q_ref, k_ref, v_ref, do_ref, o_ref, dq_ref, dk_ref, dv_ref, ggl_ref, g_ref,
                 ls_ref, kst_ref, attn_ref, gq_ref, gk_ref, gv_ref, gg_ref):
    block_len = q_ref.shape[0]
    nlev = g_ref.shape[0]
    nbits = ls_ref.shape[0]
    first = nlev - nbits
    key_state_t = kst_ref[...]
    h = pl.program_id(0)
    width = ls_ref.shape[1]
    state_t = jnp.concatenate(
        [jnp.transpose(ls_ref[b].astype(jnp.float32)).astype(jnp.bfloat16) for b in range(nbits)], axis=0
    )
    state = jnp.concatenate([ls_ref[b] for b in range(nbits)], axis=0)
    gg = [ggl_ref[lev : lev + 1, :] for lev in range(nlev)]
    cross_rows = [[] for _ in range(nbits)]
    for i in range(block_len // TILE):
        ts = pl.ds(i * TILE, TILE)
        qi = q_ref[ts, :]
        doi = do_ref[ts, :]
        do_t = jnp.transpose(doi.astype(jnp.float32))
        attn_t = o_ref[:, ts]
        grad_q_t = dq_ref[:, ts]
        out_all = dot_nt(state_t, qi)
        back_all = dot_nt(state, doi)
        for b in range(nbits):
            weight = g_ref[first + b : first + b + 1, ts]
            level_out_t = out_all[b * width : (b + 1) * width]
            level_back_t = back_all[b * width : (b + 1) * width]
            attn_t = attn_t + weight * level_out_t
            grad_q_t = grad_q_t + weight * level_back_t
            dotted = jnp.sum(level_out_t * do_t, axis=0, keepdims=True)
            cross_rows[b].append(weight * dotted)
        attn_ref[ts, :] = jnp.transpose(attn_t).astype(attn_ref.dtype)
        gq_ref[ts, :] = jnp.transpose(grad_q_t).astype(gq_ref.dtype)
        gk_ref[ts, :] = (dk_ref[ts, :] + dot_nn(v_ref[ts, :], key_state_t)).astype(gk_ref.dtype)
        gv_ref[ts, :] = (dv_ref[ts, :] + dot_nt(k_ref[ts, :], key_state_t)).astype(gv_ref.dtype)
    for b in range(nbits):
        gg[first + b] = jnp.concatenate(cross_rows[b], axis=1)
    for lev in range(nlev):
        gg_ref[lev, pl.ds(h, 1), :] = gg[lev]


def final_part(query_rows, key_rows, value_rows, out_grad, partials, gate_t, level_state, key_state_t):
    heads, block_len, width = query_rows.shape
    nlev = gate_t.shape[1]
    nbits = level_state.shape[0]
    row_spec = pl.BlockSpec((None, block_len, width), lambda h: (h, 0, 0))
    col_spec = pl.BlockSpec((None, width, block_len), lambda h: (h, 0, 0))
    gate_spec = pl.BlockSpec((None, nlev, block_len), lambda h: (h, 0, 0))
    ls_spec = pl.BlockSpec((nbits, None, width, width), lambda h: (0, h, 0, 0))
    ks_spec = pl.BlockSpec((None, width, width), lambda h: (h, 0, 0))
    bf = jnp.bfloat16
    return pl.pallas_call(
        final_kernel,
        grid=(heads,),
        in_specs=[row_spec] * 4 + [col_spec] * 2 + [row_spec] * 2
        + [gate_spec, gate_spec, ls_spec, ks_spec],
        out_specs=[row_spec] * 4 + [pl.BlockSpec((nlev, heads, block_len), lambda h: (0, 0, 0))],
        out_shape=[jax.ShapeDtypeStruct((heads, block_len, width), bf)] * 4
        + [jax.ShapeDtypeStruct((nlev, heads, block_len), jnp.float32)],
        compiler_params=pltpu.CompilerParams(dimension_semantics=("arbitrary",)),
        cost_estimate=pl.CostEstimate(
            flops=heads * block_len * width * width * 2 * (2 * nbits + 2),
            transcendentals=0,
            bytes_accessed=heads * block_len * (8 * width * 2 + 4 * width * 4 + 4 * nlev * 4),
        ),
    )(query_rows, key_rows, value_rows, out_grad, *partials[:4], partials[4], gate_t,
      level_state, key_state_t)


def same_doc(block_levels, earlier, later):
    picked = lax.dynamic_slice(block_levels, (later, earlier), (1, 1))
    return picked.reshape(1, 1, 1) >= 0


def step_masks(block_levels, me, k):
    bit = ((me >> k) & 1) == 1
    lo = (me >> (k + 1)) << (k + 1)
    end_low = lo + (1 << k) - 1
    end_high = lo + (2 << k) - 1
    joined = same_doc(block_levels, end_low, end_high)
    mine = same_doc(block_levels, end_low, me)
    return bit, joined, mine


def pairs_of(k, ctx_len, sender_bit=None):
    return [
        (j, j ^ (1 << k))
        for j in range(ctx_len)
        if sender_bit is None or ((j >> k) & 1) == sender_bit
    ]


def per_device(query_rows, key_rows, value_rows, out_grad, level_gate, block_levels, ctx_len):
    level_total = level_gate.shape[0]
    block_len = query_rows.shape[1]
    log_block = block_len.bit_length() - 1
    nbits = level_total - log_block - 1
    me = lax.axis_index("ctx")
    weights = jnp.exp(level_gate)

    gate_t = weights.transpose(1, 0, 2)
    own_state, grad_state = state_part(query_rows, key_rows, value_rows, out_grad, gate_t, nbits)
    grad_wide = grad_state
    heads = query_rows.shape[0]
    fwd_x = own_state
    bwd_acc = None
    levels = []
    partials = None
    for r in range(nbits):
        kf = r
        kb = nbits - 1 - r
        if kf == 0 or kf == nbits - 1:
            fwd_got = lax.ppermute(
                fwd_x.astype(jnp.bfloat16), "ctx",
                pairs_of(kf, ctx_len),
            ).astype(jnp.float32)
        else:
            fwd_got = lax.ppermute(fwd_x, "ctx", pairs_of(kf, ctx_len))
        bit, joined, mine = step_masks(block_levels, me, kb)
        term = jnp.where(bit & mine, grad_wide[kb], 0.0)
        if bwd_acc is None:
            send, own = term, None
            bwd_pairs = pairs_of(kb, ctx_len)
        else:
            kept = jnp.where(joined, bwd_acc, 0.0)
            send = jnp.where(bit, term + kept, bwd_acc)
            own = jnp.where(bit, bwd_acc, kept)
            bwd_pairs = pairs_of(kb, ctx_len)
        if own is None:
            bwd_got = lax.ppermute(send.astype(jnp.bfloat16), "ctx", bwd_pairs).astype(jnp.float32)
        else:
            bwd_got = lax.ppermute(send, "ctx", bwd_pairs)
        if r < heads:
            partials = local_part(query_rows, key_rows, value_rows, out_grad, gate_t, r, partials)
            fwd_got, bwd_got, partials = lax.optimization_barrier((fwd_got, bwd_got, partials))
        bwd_acc = bwd_got if own is None else own + bwd_got
        bit, joined, mine = step_masks(block_levels, me, kf)
        levels.append(jnp.where(bit & mine, fwd_got, 0.0).astype(jnp.bfloat16))
        if kf < nbits - 1:
            fwd_x = jnp.where(
                bit, fwd_x + jnp.where(joined, fwd_got, 0.0), fwd_got + jnp.where(joined, fwd_x, 0.0)
            )
    for h in range(nbits, heads):
        partials = local_part(query_rows, key_rows, value_rows, out_grad, gate_t, h, partials)
    level_state = jnp.stack(levels)
    key_state_t = bwd_acc.astype(jnp.bfloat16)
    attn, grad_q, grad_k, grad_v, grad_gate = final_part(
        query_rows, key_rows, value_rows, out_grad, partials, gate_t, level_state, key_state_t
    )
    return (attn, grad_q, grad_k, grad_v, grad_gate)


def solution(mesh):
    ctx_len = mesh.shape["ctx"]
    in_specs = (
        P("head", "ctx", None),
        P("head", "ctx", None),
        P("head", "ctx", None),
        P("head", "ctx", None),
        P(None, "head", "ctx"),
        P(),
    )
    out_specs = (
        P("head", "ctx", None),
        P("head", "ctx", None),
        P("head", "ctx", None),
        P("head", "ctx", None),
        P(None, "head", "ctx"),
    )

    def body(*args):
        return per_device(*args, ctx_len=ctx_len)

    return jax.shard_map(
        body, mesh=mesh, in_specs=in_specs, out_specs=out_specs, check_vma=False
    )
```

```python
import jax
import jax.numpy as jnp
from jax import lax
from jax.experimental import pallas as pl
from jax.experimental.pallas import tpu as pltpu
from jax.sharding import PartitionSpec as P


TILE = 256
SUB = 128


def bit_length_small(numbers, count):
    total = jnp.zeros(numbers.shape, jnp.int32)
    for shift_by in range(count):
        total = total + (numbers >= (1 << shift_by)).astype(jnp.int32)
    return total


def dot_nt(a, b):
    return lax.dot_general(a, b, (((1,), (1,)), ((), ())), preferred_element_type=jnp.float32)


def dot_tn(a, b):
    return lax.dot_general(a, b, (((0,), (0,)), ((), ())), preferred_element_type=jnp.float32)


def dot_nn(a, b):
    return lax.dot_general(a, b, (((1,), (0,)), ((), ())), preferred_element_type=jnp.float32)


def local_kernel(q_ref, k_ref, v_ref, do_ref, g_ref, *refs):
    o_ref, dq_ref, dk_ref, dv_ref, gg_ref = refs[-5:]
    block_len = q_ref.shape[0]
    tiles = block_len // TILE
    log_tile = TILE.bit_length() - 1
    log_sub = SUB.bit_length() - 1
    keys = lax.broadcasted_iota(jnp.int32, (SUB, SUB), 0)
    queries = lax.broadcasted_iota(jnp.int32, (SUB, SUB), 1)
    diag_level = jnp.where(
        keys <= queries, bit_length_small(jnp.bitwise_xor(keys, queries), log_sub), -1
    )
    for ref in (o_ref, dq_ref, dk_ref, dv_ref, gg_ref):
        ref[...] = jnp.zeros(ref.shape, jnp.float32)

    def pair(t0, s0, size, level):
        ts = pl.ds(t0, size)
        ss = pl.ds(s0, size)
        qi = q_ref[ts, :]
        doi = do_ref[ts, :]
        kj = k_ref[ss, :]
        vj = v_ref[ss, :]
        gi = g_ref[:, ts]
        scores = dot_nt(kj, qi)
        back = dot_nt(vj, doi)
        prod = scores * back
        if level is not None:
            weight = gi[level : level + 1, :]
            gg_ref[level : level + 1, ts] += jnp.sum(prod, axis=0, keepdims=True)
        else:
            weight = jnp.zeros((size, size), jnp.float32)
            for lev in range(log_sub + 1):
                hit = diag_level == lev
                weight = jnp.where(hit, gi[lev : lev + 1, :], weight)
                gg_ref[lev : lev + 1, ts] += jnp.sum(
                    jnp.where(hit, prod, 0.0), axis=0, keepdims=True
                )
        probs = (scores * weight).astype(jnp.bfloat16)
        dprobs = (back * weight).astype(jnp.bfloat16)
        o_ref[:, ts] += dot_tn(vj, probs)
        dq_ref[:, ts] += dot_tn(kj, dprobs)
        dk_ref[ss, :] += dot_nn(dprobs, qi)
        dv_ref[ss, :] += dot_nn(probs, doi)

    for i in range(tiles):
        for j in range(i):
            pair(i * TILE, j * TILE, TILE, log_tile + (i ^ j).bit_length())
        for a in range(TILE // SUB):
            for b in range(a):
                pair(i * TILE + a * SUB, i * TILE + b * SUB, SUB, log_sub + (a ^ b).bit_length())
            pair(i * TILE + a * SUB, i * TILE + a * SUB, SUB, None)
    gg_ref[...] = gg_ref[...] * g_ref[...]


def local_part(query_rows, key_rows, value_rows, out_grad, gate_t, h, outs):
    heads, block_len, width = query_rows.shape
    nlev = gate_t.shape[1]
    f32 = jnp.float32
    pairs = (block_len // TILE) * (block_len // TILE + 1) // 2
    flops = pairs * 6 * 2 * TILE * TILE * width
    shapes = [jax.ShapeDtypeStruct((heads, width, block_len), f32)] * 2 + [
        jax.ShapeDtypeStruct((heads, block_len, width), f32)
    ] * 2 + [jax.ShapeDtypeStruct((heads, nlev, block_len), f32)]
    row_spec = pl.BlockSpec((None, block_len, width), lambda i: (h, 0, 0))
    col_spec = pl.BlockSpec((None, width, block_len), lambda i: (h, 0, 0))
    gate_spec = pl.BlockSpec((None, nlev, block_len), lambda i: (h, 0, 0))
    args = (query_rows, key_rows, value_rows, out_grad, gate_t)
    in_specs = [row_spec] * 4 + [gate_spec]
    aliases = {}
    if outs is not None:
        args = args + tuple(outs)
        in_specs = in_specs + [pl.BlockSpec(memory_space=pl.ANY)] * 5
        aliases = {5 + n: n for n in range(5)}
    return pl.pallas_call(
        local_kernel,
        grid=(1,),
        in_specs=in_specs,
        out_specs=[col_spec] * 2 + [row_spec] * 2 + [gate_spec],
        out_shape=shapes,
        input_output_aliases=aliases,
        compiler_params=pltpu.CompilerParams(dimension_semantics=("arbitrary",)),
        cost_estimate=pl.CostEstimate(
            flops=flops,
            transcendentals=0,
            bytes_accessed=block_len * (4 * width * 2 + 4 * width * 4 + 2 * nlev * 4),
        ),
    )(*args)


def state_kernel(q_ref, k_ref, v_ref, do_ref, g_ref, st_ref, gs_ref):
    nlev = g_ref.shape[0]
    nbits = gs_ref.shape[0]
    first = nlev - nbits
    st_ref[...] = dot_tn(k_ref[...], v_ref[...]).astype(jnp.bfloat16).astype(st_ref.dtype)
    do_t = jnp.transpose(do_ref[...].astype(jnp.float32))
    q = q_ref[...]
    width = q.shape[1]
    scaled_t = jnp.concatenate(
        [(g_ref[first + b : first + b + 1, :] * do_t).astype(jnp.bfloat16) for b in range(nbits)], axis=0
    )
    states = dot_nn(scaled_t, q).astype(jnp.bfloat16).astype(gs_ref.dtype)
    for b in range(nbits):
        gs_ref[b] = states[b * width : (b + 1) * width]


def state_part(query_rows, key_rows, value_rows, out_grad, gate_t, nbits):
    heads, block_len, width = query_rows.shape
    nlev = gate_t.shape[1]
    row_spec = pl.BlockSpec((None, block_len, width), lambda h: (h, 0, 0))
    gate_spec = pl.BlockSpec((None, nlev, block_len), lambda h: (h, 0, 0))
    bf = jnp.bfloat16
    return pl.pallas_call(
        state_kernel,
        grid=(heads,),
        in_specs=[row_spec] * 4 + [gate_spec],
        out_specs=[
            pl.BlockSpec((None, width, width), lambda h: (h, 0, 0)),
            pl.BlockSpec((nbits, None, width, width), lambda h: (0, h, 0, 0)),
        ],
        out_shape=[
            jax.ShapeDtypeStruct((heads, width, width), jnp.float32),
            jax.ShapeDtypeStruct((nbits, heads, width, width), jnp.float32),
        ],
        compiler_params=pltpu.CompilerParams(dimension_semantics=("arbitrary",)),
        cost_estimate=pl.CostEstimate(
            flops=heads * block_len * width * width * 2 * (nbits + 1),
            transcendentals=0,
            bytes_accessed=heads * block_len * (4 * width * 2 + nlev * 4),
        ),
    )(query_rows, key_rows, value_rows, out_grad, gate_t)


def final_kernel(q_ref, k_ref, v_ref, do_ref, o_ref, dq_ref, dk_ref, dv_ref, ggl_ref, g_ref,
                 ls_ref, kst_ref, attn_ref, gq_ref, gk_ref, gv_ref, gg_ref):
    block_len = q_ref.shape[0]
    nlev = g_ref.shape[0]
    nbits = ls_ref.shape[0]
    first = nlev - nbits
    key_state_t = kst_ref[...]
    h = pl.program_id(0)
    width = ls_ref.shape[1]
    state_t = jnp.concatenate(
        [jnp.transpose(ls_ref[b].astype(jnp.float32)).astype(jnp.bfloat16) for b in range(nbits)], axis=0
    )
    state = jnp.concatenate([ls_ref[b] for b in range(nbits)], axis=0)
    gg = [ggl_ref[lev : lev + 1, :] for lev in range(nlev)]
    cross_rows = [[] for _ in range(nbits)]
    for i in range(block_len // TILE):
        ts = pl.ds(i * TILE, TILE)
        qi = q_ref[ts, :]
        doi = do_ref[ts, :]
        do_t = jnp.transpose(doi.astype(jnp.float32))
        attn_t = o_ref[:, ts]
        grad_q_t = dq_ref[:, ts]
        out_all = dot_nt(state_t, qi)
        back_all = dot_nt(state, doi)
        for b in range(nbits):
            weight = g_ref[first + b : first + b + 1, ts]
            level_out_t = out_all[b * width : (b + 1) * width]
            level_back_t = back_all[b * width : (b + 1) * width]
            attn_t = attn_t + weight * level_out_t
            grad_q_t = grad_q_t + weight * level_back_t
            dotted = jnp.sum(level_out_t * do_t, axis=0, keepdims=True)
            cross_rows[b].append(weight * dotted)
        attn_ref[ts, :] = jnp.transpose(attn_t).astype(attn_ref.dtype)
        gq_ref[ts, :] = jnp.transpose(grad_q_t).astype(gq_ref.dtype)
        gk_ref[ts, :] = (dk_ref[ts, :] + dot_nn(v_ref[ts, :], key_state_t)).astype(gk_ref.dtype)
        gv_ref[ts, :] = (dv_ref[ts, :] + dot_nt(k_ref[ts, :], key_state_t)).astype(gv_ref.dtype)
    for b in range(nbits):
        gg[first + b] = jnp.concatenate(cross_rows[b], axis=1)
    for lev in range(nlev):
        gg_ref[lev, pl.ds(h, 1), :] = gg[lev]


def final_part(query_rows, key_rows, value_rows, out_grad, partials, gate_t, level_state, key_state_t):
    heads, block_len, width = query_rows.shape
    nlev = gate_t.shape[1]
    nbits = level_state.shape[0]
    row_spec = pl.BlockSpec((None, block_len, width), lambda h: (h, 0, 0))
    col_spec = pl.BlockSpec((None, width, block_len), lambda h: (h, 0, 0))
    gate_spec = pl.BlockSpec((None, nlev, block_len), lambda h: (h, 0, 0))
    ls_spec = pl.BlockSpec((nbits, None, width, width), lambda h: (0, h, 0, 0))
    ks_spec = pl.BlockSpec((None, width, width), lambda h: (h, 0, 0))
    bf = jnp.bfloat16
    return pl.pallas_call(
        final_kernel,
        grid=(heads,),
        in_specs=[row_spec] * 4 + [col_spec] * 2 + [row_spec] * 2
        + [gate_spec, gate_spec, ls_spec, ks_spec],
        out_specs=[row_spec] * 4 + [pl.BlockSpec((nlev, heads, block_len), lambda h: (0, 0, 0))],
        out_shape=[jax.ShapeDtypeStruct((heads, block_len, width), bf)] * 4
        + [jax.ShapeDtypeStruct((nlev, heads, block_len), jnp.float32)],
        compiler_params=pltpu.CompilerParams(dimension_semantics=("arbitrary",)),
        cost_estimate=pl.CostEstimate(
            flops=heads * block_len * width * width * 2 * (2 * nbits + 2),
            transcendentals=0,
            bytes_accessed=heads * block_len * (8 * width * 2 + 4 * width * 4 + 4 * nlev * 4),
        ),
    )(query_rows, key_rows, value_rows, out_grad, *partials[:4], partials[4], gate_t,
      level_state, key_state_t)


def same_doc(block_levels, earlier, later):
    picked = lax.dynamic_slice(block_levels, (later, earlier), (1, 1))
    return picked.reshape(1, 1, 1) >= 0


def step_masks(block_levels, me, k):
    bit = ((me >> k) & 1) == 1
    lo = (me >> (k + 1)) << (k + 1)
    end_low = lo + (1 << k) - 1
    end_high = lo + (2 << k) - 1
    joined = same_doc(block_levels, end_low, end_high)
    mine = same_doc(block_levels, end_low, me)
    return bit, joined, mine


def pairs_of(k, ctx_len, sender_bit=None):
    return [
        (j, j ^ (1 << k))
        for j in range(ctx_len)
        if sender_bit is None or ((j >> k) & 1) == sender_bit
    ]


def per_device(query_rows, key_rows, value_rows, out_grad, level_gate, block_levels, ctx_len):
    level_total = level_gate.shape[0]
    block_len = query_rows.shape[1]
    log_block = block_len.bit_length() - 1
    nbits = level_total - log_block - 1
    me = lax.axis_index("ctx")
    weights = jnp.exp(level_gate)

    gate_t = weights.transpose(1, 0, 2)
    own_state, grad_state = state_part(query_rows, key_rows, value_rows, out_grad, gate_t, nbits)
    grad_wide = grad_state
    heads = query_rows.shape[0]
    fwd_x = own_state
    bwd_acc = None
    levels = []
    partials = None
    for r in range(nbits):
        kf = r
        kb = nbits - 1 - r
        if kf == 0 or kf == nbits - 1:
            fwd_got = lax.ppermute(
                fwd_x.astype(jnp.bfloat16), "ctx",
                pairs_of(kf, ctx_len),
            ).astype(jnp.float32)
        else:
            fwd_got = lax.ppermute(fwd_x, "ctx", pairs_of(kf, ctx_len))
        bit, joined, mine = step_masks(block_levels, me, kb)
        term = jnp.where(bit & mine, grad_wide[kb], 0.0)
        if bwd_acc is None:
            send, own = term, None
            bwd_pairs = pairs_of(kb, ctx_len)
        else:
            kept = jnp.where(joined, bwd_acc, 0.0)
            send = jnp.where(bit, term + kept, bwd_acc)
            own = jnp.where(bit, bwd_acc, kept)
            bwd_pairs = pairs_of(kb, ctx_len)
        if own is None:
            bwd_got = lax.ppermute(send.astype(jnp.bfloat16), "ctx", bwd_pairs).astype(jnp.float32)
        else:
            bwd_got = lax.ppermute(send, "ctx", bwd_pairs)
        if r < heads:
            partials = local_part(query_rows, key_rows, value_rows, out_grad, gate_t, r, partials)
            fwd_got, bwd_got, partials = lax.optimization_barrier((fwd_got, bwd_got, partials))
        bwd_acc = bwd_got if own is None else own + bwd_got
        bit, joined, mine = step_masks(block_levels, me, kf)
        levels.append(jnp.where(bit & mine, fwd_got, 0.0).astype(jnp.bfloat16))
        if kf < nbits - 1:
            fwd_x = jnp.where(
                bit, fwd_x + jnp.where(joined, fwd_got, 0.0), fwd_got + jnp.where(joined, fwd_x, 0.0)
            )
    for h in range(nbits, heads):
        partials = local_part(query_rows, key_rows, value_rows, out_grad, gate_t, h, partials)
    level_state = jnp.stack(levels)
    key_state_t = bwd_acc.astype(jnp.bfloat16)
    attn, grad_q, grad_k, grad_v, grad_gate = final_part(
        query_rows, key_rows, value_rows, out_grad, partials, gate_t, level_state, key_state_t
    )
    return (attn, grad_q, grad_k, grad_v, grad_gate)


def solution(mesh):
    ctx_len = mesh.shape["ctx"]
    in_specs = (
        P("head", "ctx", None),
        P("head", "ctx", None),
        P("head", "ctx", None),
        P("head", "ctx", None),
        P(None, "head", "ctx"),
        P(),
    )
    out_specs = (
        P("head", "ctx", None),
        P("head", "ctx", None),
        P("head", "ctx", None),
        P("head", "ctx", None),
        P(None, "head", "ctx"),
    )

    def body(*args):
        return per_device(*args, ctx_len=ctx_len)

    return jax.shard_map(
        body, mesh=mesh, in_specs=in_specs, out_specs=out_specs, check_vma=False
    )
```

```python
import jax
import jax.numpy as jnp
from jax import lax
from jax.experimental import pallas as pl
from jax.experimental.pallas import tpu as pltpu
from jax.sharding import PartitionSpec as P
import functools


def gate_rows(g_ref, h):
    return jnp.concatenate([g_ref[lev, pl.ds(h, 1), :] for lev in range(g_ref.shape[0])], axis=0)


TILE = 256
SUB = 128


def bit_length_small(numbers, count):
    total = jnp.zeros(numbers.shape, jnp.int32)
    for shift_by in range(count):
        total = total + (numbers >= (1 << shift_by)).astype(jnp.int32)
    return total


def dot_nt(a, b):
    return lax.dot_general(a, b, (((1,), (1,)), ((), ())), preferred_element_type=jnp.float32)


def dot_tn(a, b):
    return lax.dot_general(a, b, (((0,), (0,)), ((), ())), preferred_element_type=jnp.float32)


def dot_nn(a, b):
    return lax.dot_general(a, b, (((1,), (0,)), ((), ())), preferred_element_type=jnp.float32)


def local_kernel(h, q_ref, k_ref, v_ref, do_ref, g_ref, *refs):
    gate = gate_rows(g_ref, h)
    o_ref, dq_ref, dk_ref, dv_ref, gg_ref = refs[-5:]
    block_len = q_ref.shape[0]
    tiles = block_len // TILE
    log_tile = TILE.bit_length() - 1
    log_sub = SUB.bit_length() - 1
    keys = lax.broadcasted_iota(jnp.int32, (SUB, SUB), 0)
    queries = lax.broadcasted_iota(jnp.int32, (SUB, SUB), 1)
    diag_level = jnp.where(
        keys <= queries, bit_length_small(jnp.bitwise_xor(keys, queries), log_sub), -1
    )
    for ref in (o_ref, dq_ref, dk_ref, dv_ref, gg_ref):
        ref[...] = jnp.zeros(ref.shape, jnp.float32)

    def pair(t0, s0, size, level):
        ts = pl.ds(t0, size)
        ss = pl.ds(s0, size)
        qi = q_ref[ts, :]
        doi = do_ref[ts, :]
        kj = k_ref[ss, :]
        vj = v_ref[ss, :]
        gi = gate[:, t0 : t0 + size]
        scores = dot_nt(kj, qi)
        back = dot_nt(vj, doi)
        prod = scores * back
        if level is not None:
            weight = gi[level : level + 1, :]
            gg_ref[level : level + 1, ts] += jnp.sum(prod, axis=0, keepdims=True)
        else:
            weight = jnp.zeros((size, size), jnp.float32)
            for lev in range(log_sub + 1):
                hit = diag_level == lev
                weight = jnp.where(hit, gi[lev : lev + 1, :], weight)
                gg_ref[lev : lev + 1, ts] += jnp.sum(
                    jnp.where(hit, prod, 0.0), axis=0, keepdims=True
                )
        probs = (scores * weight).astype(jnp.bfloat16)
        dprobs = (back * weight).astype(jnp.bfloat16)
        o_ref[:, ts] += dot_tn(vj, probs)
        dq_ref[:, ts] += dot_tn(kj, dprobs)
        dk_ref[ss, :] += dot_nn(dprobs, qi)
        dv_ref[ss, :] += dot_nn(probs, doi)

    for i in range(tiles):
        for j in range(i):
            pair(i * TILE, j * TILE, TILE, log_tile + (i ^ j).bit_length())
        for a in range(TILE // SUB):
            for b in range(a):
                pair(i * TILE + a * SUB, i * TILE + b * SUB, SUB, log_sub + (a ^ b).bit_length())
            pair(i * TILE + a * SUB, i * TILE + a * SUB, SUB, None)
    gg_ref[...] = gg_ref[...] * gate


def local_part(query_rows, key_rows, value_rows, out_grad, gate_t, h, outs):
    heads, block_len, width = query_rows.shape
    nlev = gate_t.shape[0]
    f32 = jnp.float32
    pairs = (block_len // TILE) * (block_len // TILE + 1) // 2
    flops = pairs * 6 * 2 * TILE * TILE * width
    shapes = [jax.ShapeDtypeStruct((heads, width, block_len), f32)] * 2 + [
        jax.ShapeDtypeStruct((heads, block_len, width), f32)
    ] * 2 + [jax.ShapeDtypeStruct((heads, nlev, block_len), f32)]
    row_spec = pl.BlockSpec((None, block_len, width), lambda i: (h, 0, 0))
    col_spec = pl.BlockSpec((None, width, block_len), lambda i: (h, 0, 0))
    gate_spec = pl.BlockSpec((None, nlev, block_len), lambda i: (h, 0, 0))
    full_gate = pl.BlockSpec((nlev, heads, block_len), lambda i: (0, 0, 0))
    args = (query_rows, key_rows, value_rows, out_grad, gate_t)
    in_specs = [row_spec] * 4 + [full_gate]
    aliases = {}
    if outs is not None:
        args = args + tuple(outs)
        in_specs = in_specs + [pl.BlockSpec(memory_space=pl.ANY)] * 5
        aliases = {5 + n: n for n in range(5)}
    return pl.pallas_call(
        functools.partial(local_kernel, h),
        grid=(1,),
        in_specs=in_specs,
        out_specs=[col_spec] * 2 + [row_spec] * 2 + [gate_spec],
        out_shape=shapes,
        input_output_aliases=aliases,
        compiler_params=pltpu.CompilerParams(dimension_semantics=("arbitrary",)),
        cost_estimate=pl.CostEstimate(
            flops=flops,
            transcendentals=0,
            bytes_accessed=block_len * (4 * width * 2 + 4 * width * 4 + 2 * nlev * 4),
        ),
    )(*args)


def state_kernel(q_ref, k_ref, v_ref, do_ref, g_ref, st_ref, gs_ref):
    nlev = g_ref.shape[0]
    gate = gate_rows(g_ref, pl.program_id(0))
    nbits = gs_ref.shape[0]
    first = nlev - nbits
    st_ref[...] = dot_tn(k_ref[...], v_ref[...]).astype(jnp.bfloat16).astype(st_ref.dtype)
    do_t = jnp.transpose(do_ref[...].astype(jnp.float32))
    q = q_ref[...]
    for b in range(nbits):
        scaled_t = (gate[first + b : first + b + 1, :] * do_t).astype(jnp.bfloat16)
        gs_ref[b] = dot_nn(scaled_t, q).astype(jnp.bfloat16).astype(gs_ref.dtype)


def state_part(query_rows, key_rows, value_rows, out_grad, gate_t, nbits):
    heads, block_len, width = query_rows.shape
    nlev = gate_t.shape[0]
    row_spec = pl.BlockSpec((None, block_len, width), lambda h: (h, 0, 0))
    gate_spec = pl.BlockSpec((nlev, heads, block_len), lambda h: (0, 0, 0))
    bf = jnp.bfloat16
    return pl.pallas_call(
        state_kernel,
        grid=(heads,),
        in_specs=[row_spec] * 4 + [gate_spec],
        out_specs=[
            pl.BlockSpec((None, width, width), lambda h: (h, 0, 0)),
            pl.BlockSpec((nbits, None, width, width), lambda h: (0, h, 0, 0)),
        ],
        out_shape=[
            jax.ShapeDtypeStruct((heads, width, width), jnp.float32),
            jax.ShapeDtypeStruct((nbits, heads, width, width), jnp.float32),
        ],
        compiler_params=pltpu.CompilerParams(dimension_semantics=("arbitrary",)),
        cost_estimate=pl.CostEstimate(
            flops=heads * block_len * width * width * 2 * (nbits + 1),
            transcendentals=0,
            bytes_accessed=heads * block_len * (4 * width * 2 + nlev * 4),
        ),
    )(query_rows, key_rows, value_rows, out_grad, gate_t)


def final_kernel(q_ref, k_ref, v_ref, do_ref, o_ref, dq_ref, dk_ref, dv_ref, ggl_ref, g_ref,
                 ls_ref, kst_ref, attn_ref, gq_ref, gk_ref, gv_ref, gg_ref):
    block_len = q_ref.shape[0]
    nlev = g_ref.shape[0]
    nbits = ls_ref.shape[0]
    first = nlev - nbits
    key_state_t = kst_ref[...]
    h = pl.program_id(0)
    gate = gate_rows(g_ref, h)
    width = ls_ref.shape[1]
    state_t = jnp.concatenate(
        [jnp.transpose(ls_ref[b].astype(jnp.float32)).astype(jnp.bfloat16) for b in range(nbits)], axis=0
    )
    state = jnp.concatenate([ls_ref[b] for b in range(nbits)], axis=0)
    gg = [ggl_ref[lev : lev + 1, :] for lev in range(nlev)]
    cross_rows = [[] for _ in range(nbits)]
    for i in range(block_len // TILE):
        ts = pl.ds(i * TILE, TILE)
        qi = q_ref[ts, :]
        doi = do_ref[ts, :]
        do_t = jnp.transpose(doi.astype(jnp.float32))
        attn_t = o_ref[:, ts]
        grad_q_t = dq_ref[:, ts]
        out_all = dot_nt(state_t, qi)
        back_all = dot_nt(state, doi)
        for b in range(nbits):
            weight = gate[first + b : first + b + 1, i * TILE : (i + 1) * TILE]
            level_out_t = out_all[b * width : (b + 1) * width]
            level_back_t = back_all[b * width : (b + 1) * width]
            attn_t = attn_t + weight * level_out_t
            grad_q_t = grad_q_t + weight * level_back_t
            dotted = jnp.sum(level_out_t * do_t, axis=0, keepdims=True)
            cross_rows[b].append(weight * dotted)
        attn_ref[ts, :] = jnp.transpose(attn_t).astype(attn_ref.dtype)
        gq_ref[ts, :] = jnp.transpose(grad_q_t).astype(gq_ref.dtype)
        gk_ref[ts, :] = (dk_ref[ts, :] + dot_nn(v_ref[ts, :], key_state_t)).astype(gk_ref.dtype)
        gv_ref[ts, :] = (dv_ref[ts, :] + dot_nt(k_ref[ts, :], key_state_t)).astype(gv_ref.dtype)
    for b in range(nbits):
        gg[first + b] = jnp.concatenate(cross_rows[b], axis=1)
    for lev in range(nlev):
        gg_ref[lev, pl.ds(h, 1), :] = gg[lev]


def final_part(query_rows, key_rows, value_rows, out_grad, partials, gate_t, level_state, key_state_t):
    heads, block_len, width = query_rows.shape
    nlev = gate_t.shape[0]
    nbits = level_state.shape[0]
    full_gate = pl.BlockSpec((nlev, heads, block_len), lambda h: (0, 0, 0))
    row_spec = pl.BlockSpec((None, block_len, width), lambda h: (h, 0, 0))
    col_spec = pl.BlockSpec((None, width, block_len), lambda h: (h, 0, 0))
    gate_spec = pl.BlockSpec((None, nlev, block_len), lambda h: (h, 0, 0))
    ls_spec = pl.BlockSpec((nbits, None, width, width), lambda h: (0, h, 0, 0))
    ks_spec = pl.BlockSpec((None, width, width), lambda h: (h, 0, 0))
    bf = jnp.bfloat16
    return pl.pallas_call(
        final_kernel,
        grid=(heads,),
        in_specs=[row_spec] * 4 + [col_spec] * 2 + [row_spec] * 2
        + [gate_spec, full_gate, ls_spec, ks_spec],
        out_specs=[row_spec] * 4 + [pl.BlockSpec((nlev, heads, block_len), lambda h: (0, 0, 0))],
        out_shape=[jax.ShapeDtypeStruct((heads, block_len, width), bf)] * 4
        + [jax.ShapeDtypeStruct((nlev, heads, block_len), jnp.float32)],
        compiler_params=pltpu.CompilerParams(dimension_semantics=("arbitrary",)),
        cost_estimate=pl.CostEstimate(
            flops=heads * block_len * width * width * 2 * (2 * nbits + 2),
            transcendentals=0,
            bytes_accessed=heads * block_len * (8 * width * 2 + 4 * width * 4 + 4 * nlev * 4),
        ),
    )(query_rows, key_rows, value_rows, out_grad, *partials[:4], partials[4], gate_t,
      level_state, key_state_t)


def same_doc(block_levels, earlier, later):
    picked = lax.dynamic_slice(block_levels, (later, earlier), (1, 1))
    return picked.reshape(1, 1, 1) >= 0


def step_masks(block_levels, me, k):
    bit = ((me >> k) & 1) == 1
    lo = (me >> (k + 1)) << (k + 1)
    end_low = lo + (1 << k) - 1
    end_high = lo + (2 << k) - 1
    joined = same_doc(block_levels, end_low, end_high)
    mine = same_doc(block_levels, end_low, me)
    return bit, joined, mine


def pairs_of(k, ctx_len, sender_bit=None):
    return [
        (j, j ^ (1 << k))
        for j in range(ctx_len)
        if sender_bit is None or ((j >> k) & 1) == sender_bit
    ]


def per_device(query_rows, key_rows, value_rows, out_grad, level_gate, block_levels, ctx_len):
    level_total = level_gate.shape[0]
    block_len = query_rows.shape[1]
    log_block = block_len.bit_length() - 1
    nbits = level_total - log_block - 1
    me = lax.axis_index("ctx")
    weights = jnp.exp(level_gate)

    gate_t = weights
    own_state, grad_state = state_part(query_rows, key_rows, value_rows, out_grad, gate_t, nbits)
    grad_wide = grad_state
    heads = query_rows.shape[0]
    fwd_x = own_state
    bwd_acc = None
    levels = []
    partials = None
    for r in range(nbits):
        kf = r
        kb = nbits - 1 - r
        if kf == 0 or kf == nbits - 1:
            fwd_got = lax.ppermute(
                fwd_x.astype(jnp.bfloat16), "ctx",
                pairs_of(kf, ctx_len),
            ).astype(jnp.float32)
        else:
            fwd_got = lax.ppermute(fwd_x, "ctx", pairs_of(kf, ctx_len))
        bit, joined, mine = step_masks(block_levels, me, kb)
        term = jnp.where(bit & mine, grad_wide[kb], 0.0)
        if bwd_acc is None:
            send, own = term, None
            bwd_pairs = pairs_of(kb, ctx_len)
        else:
            kept = jnp.where(joined, bwd_acc, 0.0)
            send = jnp.where(bit, term + kept, bwd_acc)
            own = jnp.where(bit, bwd_acc, kept)
            bwd_pairs = pairs_of(kb, ctx_len)
        if own is None:
            bwd_got = lax.ppermute(send.astype(jnp.bfloat16), "ctx", bwd_pairs).astype(jnp.float32)
        else:
            bwd_got = lax.ppermute(send, "ctx", bwd_pairs)
        if r < heads:
            partials = local_part(query_rows, key_rows, value_rows, out_grad, gate_t, r, partials)
            fwd_got, bwd_got, partials = lax.optimization_barrier((fwd_got, bwd_got, partials))
        bwd_acc = bwd_got if own is None else own + bwd_got
        bit, joined, mine = step_masks(block_levels, me, kf)
        levels.append(jnp.where(bit & mine, fwd_got, 0.0).astype(jnp.bfloat16))
        if kf < nbits - 1:
            fwd_x = jnp.where(
                bit, fwd_x + jnp.where(joined, fwd_got, 0.0), fwd_got + jnp.where(joined, fwd_x, 0.0)
            )
    for h in range(nbits, heads):
        partials = local_part(query_rows, key_rows, value_rows, out_grad, gate_t, h, partials)
    level_state = jnp.stack(levels)
    key_state_t = bwd_acc.astype(jnp.bfloat16)
    attn, grad_q, grad_k, grad_v, grad_gate = final_part(
        query_rows, key_rows, value_rows, out_grad, partials, gate_t, level_state, key_state_t
    )
    return (attn, grad_q, grad_k, grad_v, grad_gate)


def solution(mesh):
    ctx_len = mesh.shape["ctx"]
    in_specs = (
        P("head", "ctx", None),
        P("head", "ctx", None),
        P("head", "ctx", None),
        P("head", "ctx", None),
        P(None, "head", "ctx"),
        P(),
    )
    out_specs = (
        P("head", "ctx", None),
        P("head", "ctx", None),
        P("head", "ctx", None),
        P("head", "ctx", None),
        P(None, "head", "ctx"),
    )

    def body(*args):
        return per_device(*args, ctx_len=ctx_len)

    return jax.shard_map(
        body, mesh=mesh, in_specs=in_specs, out_specs=out_specs, check_vma=False
    )
```

```python
import jax
import jax.numpy as jnp
from jax import lax
from jax.experimental import pallas as pl
from jax.experimental.pallas import tpu as pltpu
from jax.sharding import PartitionSpec as P


TILE = 256
SUB = 128
ROWS = 512


def bit_length_small(numbers, count):
    total = jnp.zeros(numbers.shape, jnp.int32)
    for shift_by in range(count):
        total = total + (numbers >= (1 << shift_by)).astype(jnp.int32)
    return total


def dot_nt(a, b):
    return lax.dot_general(a, b, (((1,), (1,)), ((), ())), preferred_element_type=jnp.float32)


def dot_tn(a, b):
    return lax.dot_general(a, b, (((0,), (0,)), ((), ())), preferred_element_type=jnp.float32)


def dot_nn(a, b):
    return lax.dot_general(a, b, (((1,), (0,)), ((), ())), preferred_element_type=jnp.float32)


def local_kernel(q_ref, k_ref, v_ref, do_ref, g_ref, *refs):
    o_ref, dq_ref, dk_ref, dv_ref, gg_ref = refs[-5:]
    block_len = q_ref.shape[0]
    tiles = block_len // TILE
    log_tile = TILE.bit_length() - 1
    log_sub = SUB.bit_length() - 1
    keys = lax.broadcasted_iota(jnp.int32, (SUB, SUB), 0)
    queries = lax.broadcasted_iota(jnp.int32, (SUB, SUB), 1)
    diag_level = jnp.where(
        keys <= queries, bit_length_small(jnp.bitwise_xor(keys, queries), log_sub), -1
    )
    for ref in (o_ref, dq_ref, dk_ref, dv_ref, gg_ref):
        ref[...] = jnp.zeros(ref.shape, jnp.float32)

    def pair(t0, s0, size, level):
        ts = pl.ds(t0, size)
        ss = pl.ds(s0, size)
        qi = q_ref[ts, :]
        doi = do_ref[ts, :]
        kj = k_ref[ss, :]
        vj = v_ref[ss, :]
        gi = g_ref[:, ts]
        scores = dot_nt(kj, qi)
        back = dot_nt(vj, doi)
        prod = scores * back
        if level is not None:
            weight = gi[level : level + 1, :]
            gg_ref[level : level + 1, ts] += jnp.sum(prod, axis=0, keepdims=True)
        else:
            weight = jnp.zeros((size, size), jnp.float32)
            for lev in range(log_sub + 1):
                hit = diag_level == lev
                weight = jnp.where(hit, gi[lev : lev + 1, :], weight)
                gg_ref[lev : lev + 1, ts] += jnp.sum(
                    jnp.where(hit, prod, 0.0), axis=0, keepdims=True
                )
        probs = (scores * weight).astype(jnp.bfloat16)
        dprobs = (back * weight).astype(jnp.bfloat16)
        o_ref[:, ts] += dot_tn(vj, probs)
        dq_ref[:, ts] += dot_tn(kj, dprobs)
        dk_ref[ss, :] += dot_nn(dprobs, qi)
        dv_ref[ss, :] += dot_nn(probs, doi)

    for i in range(tiles):
        for j in range(i):
            pair(i * TILE, j * TILE, TILE, log_tile + (i ^ j).bit_length())
        for a in range(TILE // SUB):
            for b in range(a):
                pair(i * TILE + a * SUB, i * TILE + b * SUB, SUB, log_sub + (a ^ b).bit_length())
            pair(i * TILE + a * SUB, i * TILE + a * SUB, SUB, None)
    gg_ref[...] = gg_ref[...] * g_ref[...]


def local_part(query_rows, key_rows, value_rows, out_grad, gate_t, h, outs):
    heads, block_len, width = query_rows.shape
    nlev = gate_t.shape[1]
    f32 = jnp.float32
    pairs = (block_len // TILE) * (block_len // TILE + 1) // 2
    flops = pairs * 6 * 2 * TILE * TILE * width
    shapes = [jax.ShapeDtypeStruct((heads, width, block_len), f32)] * 2 + [
        jax.ShapeDtypeStruct((heads, block_len, width), f32)
    ] * 2 + [jax.ShapeDtypeStruct((heads, nlev, block_len), f32)]
    row_spec = pl.BlockSpec((None, block_len, width), lambda i: (h, 0, 0))
    col_spec = pl.BlockSpec((None, width, block_len), lambda i: (h, 0, 0))
    gate_spec = pl.BlockSpec((None, nlev, block_len), lambda i: (h, 0, 0))
    args = (query_rows, key_rows, value_rows, out_grad, gate_t)
    in_specs = [row_spec] * 4 + [gate_spec]
    aliases = {}
    if outs is not None:
        args = args + tuple(outs)
        in_specs = in_specs + [pl.BlockSpec(memory_space=pl.ANY)] * 5
        aliases = {5 + n: n for n in range(5)}
    return pl.pallas_call(
        local_kernel,
        grid=(1,),
        in_specs=in_specs,
        out_specs=[col_spec] * 2 + [row_spec] * 2 + [gate_spec],
        out_shape=shapes,
        input_output_aliases=aliases,
        compiler_params=pltpu.CompilerParams(dimension_semantics=("arbitrary",)),
        cost_estimate=pl.CostEstimate(
            flops=flops,
            transcendentals=0,
            bytes_accessed=block_len * (4 * width * 2 + 4 * width * 4 + 2 * nlev * 4),
        ),
    )(*args)


def state_kernel(q_ref, k_ref, v_ref, do_ref, g_ref, st_ref, gs_ref):
    nlev = g_ref.shape[0]
    nbits = gs_ref.shape[0]
    first = nlev - nbits
    st_ref[...] = dot_tn(k_ref[...], v_ref[...]).astype(jnp.bfloat16).astype(st_ref.dtype)
    do_t = jnp.transpose(do_ref[...].astype(jnp.float32))
    q = q_ref[...]
    for b in range(nbits):
        scaled_t = (g_ref[first + b : first + b + 1, :] * do_t).astype(jnp.bfloat16)
        gs_ref[b] = dot_nn(scaled_t, q).astype(jnp.bfloat16).astype(gs_ref.dtype)


def state_part(query_rows, key_rows, value_rows, out_grad, gate_t, nbits):
    heads, block_len, width = query_rows.shape
    nlev = gate_t.shape[1]
    row_spec = pl.BlockSpec((None, block_len, width), lambda h: (h, 0, 0))
    gate_spec = pl.BlockSpec((None, nlev, block_len), lambda h: (h, 0, 0))
    bf = jnp.bfloat16
    return pl.pallas_call(
        state_kernel,
        grid=(heads,),
        in_specs=[row_spec] * 4 + [gate_spec],
        out_specs=[
            pl.BlockSpec((None, width, width), lambda h: (h, 0, 0)),
            pl.BlockSpec((nbits, None, width, width), lambda h: (0, h, 0, 0)),
        ],
        out_shape=[
            jax.ShapeDtypeStruct((heads, width, width), jnp.float32),
            jax.ShapeDtypeStruct((nbits, heads, width, width), jnp.float32),
        ],
        compiler_params=pltpu.CompilerParams(dimension_semantics=("arbitrary",)),
        cost_estimate=pl.CostEstimate(
            flops=heads * block_len * width * width * 2 * (nbits + 1),
            transcendentals=0,
            bytes_accessed=heads * block_len * (4 * width * 2 + nlev * 4),
        ),
    )(query_rows, key_rows, value_rows, out_grad, gate_t)


def final_kernel(q_ref, k_ref, v_ref, do_ref, o_ref, dq_ref, dk_ref, dv_ref, ggl_ref, g_ref,
                 ls_ref, kst_ref, attn_ref, gq_ref, gk_ref, gv_ref, gg_ref):
    block_len = q_ref.shape[0]
    nlev = g_ref.shape[0]
    nbits = ls_ref.shape[0]
    first = nlev - nbits
    key_state_t = kst_ref[...]
    h = pl.program_id(0)
    width = ls_ref.shape[1]
    state_t = jnp.concatenate(
        [jnp.transpose(ls_ref[b].astype(jnp.float32)).astype(jnp.bfloat16) for b in range(nbits)], axis=0
    )
    state = jnp.concatenate([ls_ref[b] for b in range(nbits)], axis=0)
    gg = [ggl_ref[lev : lev + 1, :] for lev in range(nlev)]
    cross_rows = [[] for _ in range(nbits)]
    for i in range(block_len // ROWS):
        ts = pl.ds(i * ROWS, ROWS)
        qi = q_ref[ts, :]
        doi = do_ref[ts, :]
        do_t = jnp.transpose(doi.astype(jnp.float32))
        attn_t = o_ref[:, ts]
        grad_q_t = dq_ref[:, ts]
        out_all = dot_nt(state_t, qi)
        back_all = dot_nt(state, doi)
        for b in range(nbits):
            weight = g_ref[first + b : first + b + 1, ts]
            level_out_t = out_all[b * width : (b + 1) * width]
            level_back_t = back_all[b * width : (b + 1) * width]
            attn_t = attn_t + weight * level_out_t
            grad_q_t = grad_q_t + weight * level_back_t
            dotted = jnp.sum(level_out_t * do_t, axis=0, keepdims=True)
            cross_rows[b].append(weight * dotted)
        attn_ref[ts, :] = jnp.transpose(attn_t).astype(attn_ref.dtype)
        gq_ref[ts, :] = jnp.transpose(grad_q_t).astype(gq_ref.dtype)
        gk_ref[ts, :] = (dk_ref[ts, :] + dot_nn(v_ref[ts, :], key_state_t)).astype(gk_ref.dtype)
        gv_ref[ts, :] = (dv_ref[ts, :] + dot_nt(k_ref[ts, :], key_state_t)).astype(gv_ref.dtype)
    for b in range(nbits):
        gg[first + b] = jnp.concatenate(cross_rows[b], axis=1)
    for lev in range(nlev):
        gg_ref[lev, pl.ds(h, 1), :] = gg[lev]


def final_part(query_rows, key_rows, value_rows, out_grad, partials, gate_t, level_state, key_state_t):
    heads, block_len, width = query_rows.shape
    nlev = gate_t.shape[1]
    nbits = level_state.shape[0]
    row_spec = pl.BlockSpec((None, block_len, width), lambda h: (h, 0, 0))
    col_spec = pl.BlockSpec((None, width, block_len), lambda h: (h, 0, 0))
    gate_spec = pl.BlockSpec((None, nlev, block_len), lambda h: (h, 0, 0))
    ls_spec = pl.BlockSpec((nbits, None, width, width), lambda h: (0, h, 0, 0))
    ks_spec = pl.BlockSpec((None, width, width), lambda h: (h, 0, 0))
    bf = jnp.bfloat16
    return pl.pallas_call(
        final_kernel,
        grid=(heads,),
        in_specs=[row_spec] * 4 + [col_spec] * 2 + [row_spec] * 2
        + [gate_spec, gate_spec, ls_spec, ks_spec],
        out_specs=[row_spec] * 4 + [pl.BlockSpec((nlev, heads, block_len), lambda h: (0, 0, 0))],
        out_shape=[jax.ShapeDtypeStruct((heads, block_len, width), bf)] * 4
        + [jax.ShapeDtypeStruct((nlev, heads, block_len), jnp.float32)],
        compiler_params=pltpu.CompilerParams(dimension_semantics=("arbitrary",)),
        cost_estimate=pl.CostEstimate(
            flops=heads * block_len * width * width * 2 * (2 * nbits + 2),
            transcendentals=0,
            bytes_accessed=heads * block_len * (8 * width * 2 + 4 * width * 4 + 4 * nlev * 4),
        ),
    )(query_rows, key_rows, value_rows, out_grad, *partials[:4], partials[4], gate_t,
      level_state, key_state_t)


def same_doc(block_levels, earlier, later):
    picked = lax.dynamic_slice(block_levels, (later, earlier), (1, 1))
    return picked.reshape(1, 1, 1) >= 0


def step_masks(block_levels, me, k):
    bit = ((me >> k) & 1) == 1
    lo = (me >> (k + 1)) << (k + 1)
    end_low = lo + (1 << k) - 1
    end_high = lo + (2 << k) - 1
    joined = same_doc(block_levels, end_low, end_high)
    mine = same_doc(block_levels, end_low, me)
    return bit, joined, mine


def pairs_of(k, ctx_len, sender_bit=None):
    return [
        (j, j ^ (1 << k))
        for j in range(ctx_len)
        if sender_bit is None or ((j >> k) & 1) == sender_bit
    ]


def per_device(query_rows, key_rows, value_rows, out_grad, level_gate, block_levels, ctx_len):
    level_total = level_gate.shape[0]
    block_len = query_rows.shape[1]
    log_block = block_len.bit_length() - 1
    nbits = level_total - log_block - 1
    me = lax.axis_index("ctx")
    weights = jnp.exp(level_gate)

    gate_t = weights.transpose(1, 0, 2)
    own_state, grad_state = state_part(query_rows, key_rows, value_rows, out_grad, gate_t, nbits)
    grad_wide = grad_state
    heads = query_rows.shape[0]
    fwd_x = own_state
    bwd_acc = None
    levels = []
    partials = None
    for r in range(nbits):
        kf = r
        kb = nbits - 1 - r
        if kf == 0 or kf == nbits - 1:
            fwd_got = lax.ppermute(
                fwd_x.astype(jnp.bfloat16), "ctx",
                pairs_of(kf, ctx_len),
            ).astype(jnp.float32)
        else:
            fwd_got = lax.ppermute(fwd_x, "ctx", pairs_of(kf, ctx_len))
        bit, joined, mine = step_masks(block_levels, me, kb)
        term = jnp.where(bit & mine, grad_wide[kb], 0.0)
        if bwd_acc is None:
            send, own = term, None
            bwd_pairs = pairs_of(kb, ctx_len)
        else:
            kept = jnp.where(joined, bwd_acc, 0.0)
            send = jnp.where(bit, term + kept, bwd_acc)
            own = jnp.where(bit, bwd_acc, kept)
            bwd_pairs = pairs_of(kb, ctx_len)
        if own is None:
            bwd_got = lax.ppermute(send.astype(jnp.bfloat16), "ctx", bwd_pairs).astype(jnp.float32)
        else:
            bwd_got = lax.ppermute(send, "ctx", bwd_pairs)
        if r < heads:
            partials = local_part(query_rows, key_rows, value_rows, out_grad, gate_t, r, partials)
            fwd_got, bwd_got, partials = lax.optimization_barrier((fwd_got, bwd_got, partials))
        bwd_acc = bwd_got if own is None else own + bwd_got
        bit, joined, mine = step_masks(block_levels, me, kf)
        levels.append(jnp.where(bit & mine, fwd_got, 0.0).astype(jnp.bfloat16))
        if kf < nbits - 1:
            fwd_x = jnp.where(
                bit, fwd_x + jnp.where(joined, fwd_got, 0.0), fwd_got + jnp.where(joined, fwd_x, 0.0)
            )
    for h in range(nbits, heads):
        partials = local_part(query_rows, key_rows, value_rows, out_grad, gate_t, h, partials)
    level_state = jnp.stack(levels)
    key_state_t = bwd_acc.astype(jnp.bfloat16)
    attn, grad_q, grad_k, grad_v, grad_gate = final_part(
        query_rows, key_rows, value_rows, out_grad, partials, gate_t, level_state, key_state_t
    )
    return (attn, grad_q, grad_k, grad_v, grad_gate)


def solution(mesh):
    ctx_len = mesh.shape["ctx"]
    in_specs = (
        P("head", "ctx", None),
        P("head", "ctx", None),
        P("head", "ctx", None),
        P("head", "ctx", None),
        P(None, "head", "ctx"),
        P(),
    )
    out_specs = (
        P("head", "ctx", None),
        P("head", "ctx", None),
        P("head", "ctx", None),
        P("head", "ctx", None),
        P(None, "head", "ctx"),
    )

    def body(*args):
        return per_device(*args, ctx_len=ctx_len)

    return jax.shard_map(
        body, mesh=mesh, in_specs=in_specs, out_specs=out_specs, check_vma=False
    )
```
